32 devices in a mesh: dp: 4 (over y, core), seq: 8 (over z, x).
Axes of the slice: x: 2, y: 2, z: 4, core: 2. Of those that a mesh axis runs over, the one named last changes fastest.
Arguments:
- query: bfloat16 [4, 1024, 2048], P('dp', 'seq'), may hold values from -4.5 to 4.5
- keys: bfloat16 [4, 1024, 2048], P('dp', 'seq'), may hold values from -4.5 to 4.5
- values: bfloat16 [4, 1024, 2048], P('dp', 'seq'), may hold values from -18 to 18
- out_weight: bfloat16 [2048, 2048], P('dp'), may hold values from -0.125 to 0.125
- grad_out: bfloat16 [4, 1024, 2048], P('dp', 'seq'), may hold values from -6 to 6
- far_blocks: int32 [4, 16, 16, 5], P('dp'), may hold values from 0 to 15, as said below
- far_live: int32 [4, 16, 16], P('dp'), may hold values from 1 to 5, as said below
Outputs:
- mixed: bfloat16 [4, 1024, 2048], P('dp', 'seq')
- grad_query: bfloat16 [4, 1024, 2048], P('dp', 'seq')
- grad_keys: bfloat16 [4, 1024, 2048], P('dp', 'seq')
- grad_values: bfloat16 [4, 1024, 2048], P('dp', 'seq')
- weight_grad: float32 [2048, 2048], P(('dp', 'seq'))
The draws below stay inside these ranges and needn't reach their ends.
Inputs may be any that keep to these rules, and one draw needn't show every extreme that they name: `far_blocks`: for every document, head and query block b the 5 listed blocks are different and none of them is b - 1, b or b + 1. `far_live`: in every document some head uses all 5 listed distant blocks for some query block.
All inputs are finite; a program needn't handle non-finite values.
Results may differ from the reference program's by a relative error of at most 0.017.
Values may be sent and summed in bfloat16 or wider, within the bound.
No kernel may reach another device: no remote copies, remote signals or barrier semaphores. Data moves between devices by JAX's collectives and lax.ppermute only.
A program may use at most 128 MiB of HBM per device.

```python
import jax
import jax.numpy as jnp
from jax import lax

HEADS = 16
HEAD_DIM = 128
OUT_DIM = 2048
BLOCK = 64
FAR_BLOCKS = 5
DOCS = 4
SEQ_LEN = 1024
FEATURES = 2048


def draw_query(key, part):
    shape = (DOCS, SEQ_LEN, HEADS * HEAD_DIM)
    base = jnp.clip(1.5 * jax.random.normal(jax.random.fold_in(key, 1), shape, jnp.float32), -4.5, 4.5)
    return base.astype(jnp.bfloat16)


def draw_keys(key, part):
    shape = (DOCS, SEQ_LEN, HEADS * HEAD_DIM)
    base = jnp.clip(jax.random.normal(jax.random.fold_in(key, 2), shape, jnp.float32), -4.5, 4.5)
    return base.astype(jnp.bfloat16)


def draw_far_blocks(key, part):
    number = SEQ_LEN // BLOCK
    spread = jax.random.randint(jax.random.fold_in(key, 21), (DOCS, HEADS, number, number - 3), 0, 1 << 15)
    ranked = spread * (number - 3) + jnp.arange(number - 3, dtype=jnp.int32)
    unused, offsets = lax.top_k(ranked, FAR_BLOCKS)
    starts = jnp.arange(number, dtype=jnp.int32)[None, None, :, None]
    return ((starts + 2 + offsets.astype(jnp.int32)) % number).astype(jnp.int32)


def draw_far_live(key, part):
    number = SEQ_LEN // BLOCK
    most = jax.random.randint(jax.random.fold_in(key, 31), (DOCS, HEADS), 1, FAR_BLOCKS + 1)
    fullest = jax.random.randint(jax.random.fold_in(key, 32), (DOCS,), 0, HEADS)
    most = jnp.where(jnp.arange(HEADS, dtype=jnp.int32)[None, :] == fullest[:, None], FAR_BLOCKS, most)
    live = 1 + jax.random.randint(jax.random.fold_in(key, 33), (DOCS, HEADS, number), 0, FAR_BLOCKS) % most[:, :, None]
    full_at = jax.random.randint(jax.random.fold_in(key, 34), (DOCS, HEADS), 0, number)
    live = jnp.where(jnp.arange(number, dtype=jnp.int32)[None, None, :] == full_at[:, :, None], most[:, :, None], live)
    return live.astype(jnp.int32)


def shard_levels(stream_key, shape, cuts, smallest, top_value):
    level = 1.0
    for position, blocks in cuts:
        draws = jax.random.uniform(jax.random.fold_in(jax.random.fold_in(stream_key, 6), position), (blocks,), jnp.float32, smallest / len(cuts), top_value / len(cuts))
        level = level * jnp.repeat(jnp.exp(draws), shape[position] // blocks).reshape((-1,) + (1,) * (len(shape) - 1 - position))
    return level


def normal_values(stream_key, extent, width, bound, cuts=(), kind=jnp.bfloat16):
    drawn = width * jax.random.normal(stream_key, extent, jnp.float32)
    if cuts:
        drawn = drawn * shard_levels(stream_key, extent, cuts, -0.22, 0.18)
    return jnp.clip(drawn, -bound, bound).astype(kind)


def setup_inputs(seed: int = 0) -> dict:
    splits = jax.random.split(jax.random.key(seed), 8)
    query = draw_query(jax.random.fold_in(splits[7], 71), 0)
    keys = draw_keys(jax.random.fold_in(splits[7], 71), 0)
    values = normal_values(splits[2], (DOCS, SEQ_LEN, FEATURES), 3.0, 18.0, ((0, 4), (1, 8)))
    out_weight = normal_values(splits[3], (FEATURES, OUT_DIM), FEATURES ** -0.5, 0.125, ((0, 4),))
    grad_out = normal_values(splits[4], (DOCS, SEQ_LEN, OUT_DIM), 1.0, 6.0, ((0, 4), (1, 8)))
    far_blocks = draw_far_blocks(jax.random.fold_in(splits[7], 71), 0)
    far_live = draw_far_live(jax.random.fold_in(splits[7], 71), 0)
    return {"query": query, "keys": keys, "values": values, "out_weight": out_weight, "grad_out": grad_out, "far_blocks": far_blocks, "far_live": far_live}


NEG = -1e30


def key_slots(blocks, live):
    number = blocks.shape[0]
    starts = jnp.arange(number, dtype=jnp.int32)[:, None]
    window = starts - 1 + jnp.arange(3, dtype=jnp.int32)[None, :]
    slot_ids = jnp.concatenate([window, blocks.astype(jnp.int32)], axis=1)
    far_pos = jnp.arange(blocks.shape[1], dtype=jnp.int32)[None, :]
    usable = jnp.concatenate([(window >= 0) & (window < number), far_pos < live[:, None]], axis=1)
    return jnp.clip(slot_ids, 0, number - 1), usable


def gather_slots(table, slot_ids):
    chosen = table[slot_ids]
    return chosen.reshape(chosen.shape[0], chosen.shape[1] * chosen.shape[2], chosen.shape[3])


def one_head(inputs):
    q_head, k_head, v_head, g_head, blocks, live = inputs
    number = blocks.shape[0]
    head_dim = q_head.shape[-1]
    scale = head_dim ** -0.5
    slot_ids, usable = key_slots(blocks, live)
    q_blocks = q_head.reshape(number, -1, head_dim).astype(jnp.float32)
    block_rows = q_blocks.shape[1]
    k_table = k_head.reshape(number, block_rows, head_dim)
    v_table = v_head.reshape(number, block_rows, head_dim)
    k_rows = gather_slots(k_table, slot_ids).astype(jnp.float32)
    v_rows = gather_slots(v_table, slot_ids).astype(jnp.float32)
    visible = jnp.repeat(usable, block_rows, axis=1)[:, None, :]
    scores = jnp.where(visible, jnp.einsum("nqd,nkd->nqk", q_blocks, k_rows) * scale, NEG)
    row_max = jnp.max(scores, axis=-1, keepdims=True)
    log_total = row_max + jnp.log(jnp.sum(jnp.exp(scores - row_max), axis=-1, keepdims=True))
    softmax_w = jnp.exp(scores - log_total)
    probs = lax.optimization_barrier(softmax_w.astype(jnp.bfloat16)).astype(jnp.float32)
    attention = jnp.einsum("nqk,nkd->nqd", probs, v_rows).astype(jnp.bfloat16)
    g_blocks = g_head.reshape(number, block_rows, head_dim).astype(jnp.float32)
    row_dots = jnp.sum(g_blocks * attention.astype(jnp.float32), axis=-1, keepdims=True)
    grad_probs = jnp.einsum("nqd,nkd->nqk", g_blocks, v_rows)
    grad_scores = lax.optimization_barrier((softmax_w * (grad_probs - row_dots)).astype(jnp.bfloat16)).astype(jnp.float32)
    grad_q = scale * jnp.einsum("nqk,nkd->nqd", grad_scores, k_rows)
    slots_n = slot_ids.shape[1]
    flat_ids = slot_ids.reshape(-1)
    key_terms = scale * jnp.einsum("nqk,nqd->nkd", grad_scores, q_blocks)
    value_terms = jnp.einsum("nqk,nqd->nkd", probs, g_blocks)
    grad_k = jax.ops.segment_sum(key_terms.reshape(number * slots_n, block_rows, head_dim), flat_ids, num_segments=number)
    grad_v = jax.ops.segment_sum(value_terms.reshape(number * slots_n, block_rows, head_dim), flat_ids, num_segments=number)
    return (attention.reshape(-1, head_dim),
            grad_q.astype(jnp.bfloat16).reshape(-1, head_dim),
            grad_k.astype(jnp.bfloat16).reshape(-1, head_dim),
            grad_v.astype(jnp.bfloat16).reshape(-1, head_dim))


def reference(query, keys, values, out_weight, grad_out, far_blocks, far_live):
    doc_count, length, features = query.shape
    head_count = far_blocks.shape[1]
    head_dim = features // head_count
    out_width = grad_out.shape[-1]
    grad_attn = jnp.dot(grad_out.reshape(-1, out_width), out_weight.T, preferred_element_type=jnp.float32)
    grad_attn = grad_attn.astype(jnp.bfloat16).reshape(doc_count, length, features)

    def by_head(array):
        return array.reshape(length, head_count, head_dim).transpose(1, 0, 2)

    def one_doc(inputs):
        q_doc, k_doc, v_doc, g_doc, blocks, live = inputs
        results = lax.map(one_head, (by_head(q_doc), by_head(k_doc), by_head(v_doc), by_head(g_doc), blocks, live))
        return tuple(r.transpose(1, 0, 2).reshape(length, features) for r in results)

    attention, grad_query, grad_keys, grad_values = lax.map(one_doc, (query, keys, values, grad_attn, far_blocks, far_live))
    flat_attn = attention.reshape(-1, features)
    mixed = jnp.dot(flat_attn, out_weight, preferred_element_type=jnp.float32).astype(jnp.bfloat16)
    mixed = mixed.reshape(doc_count, length, out_width)
    weight_grad = jnp.dot(flat_attn.T, grad_out.reshape(-1, out_width), preferred_element_type=jnp.float32)
    weight_grad = weight_grad * ((doc_count * length) ** -0.5)
    return mixed, grad_query, grad_keys, grad_values, weight_grad
```

```python
import jax
import jax.numpy as jnp
from jax import lax
from jax.sharding import PartitionSpec as P

NEG = -1e30


def block_mask(blocks, live):
    number = blocks.shape[1]
    rows = jnp.arange(number, dtype=jnp.int32)[:, None]
    cols = jnp.arange(number, dtype=jnp.int32)[None, :]
    window = jnp.abs(rows - cols) <= 1
    far_pos = jnp.arange(blocks.shape[2], dtype=jnp.int32)
    far_used = far_pos[None, None, :] < live[:, :, None]
    hits = (blocks[:, :, :, None] == cols[None, None, :, :]) & far_used[:, :, :, None]
    return window[None] | jnp.any(hits, axis=2)


def expand_mask(mask, block_rows):
    h, nb, _ = mask.shape
    full = jnp.broadcast_to(mask[:, :, None, :, None], (h, nb, block_rows, nb, block_rows))
    return full.reshape(h, nb * block_rows, nb * block_rows)


def heads_attention(q, k, v, g, mask, block_rows):
    head_dim = q.shape[-1]
    scale = head_dim ** (-0.5)
    visible = expand_mask(mask, block_rows)
    raw = jnp.einsum("hqd,hkd->hqk", q, k, preferred_element_type=jnp.float32) * scale
    scores = jnp.where(visible, raw, NEG)
    row_max = jnp.max(scores, axis=-1, keepdims=True)
    log_total = row_max + jnp.log(jnp.sum(jnp.exp(scores - row_max), axis=-1, keepdims=True))
    softmax_w = jnp.exp(scores - log_total)
    probs = softmax_w.astype(jnp.bfloat16)
    attention = jnp.einsum("hqk,hkd->hqd", probs, v, preferred_element_type=jnp.float32).astype(
        jnp.bfloat16
    )
    row_dots = jnp.sum(
        g.astype(jnp.float32) * attention.astype(jnp.float32), axis=-1, keepdims=True
    )
    grad_probs = jnp.einsum("hqd,hkd->hqk", g, v, preferred_element_type=jnp.float32)
    dscore = (softmax_w * (grad_probs - row_dots)).astype(jnp.bfloat16)
    grad_q = scale * jnp.einsum("hqk,hkd->hqd", dscore, k, preferred_element_type=jnp.float32)
    grad_k = scale * jnp.einsum("hqk,hqd->hkd", dscore, q, preferred_element_type=jnp.float32)
    grad_v = jnp.einsum("hqk,hqd->hkd", probs, g, preferred_element_type=jnp.float32)
    return (
        attention,
        grad_q.astype(jnp.bfloat16),
        grad_k.astype(jnp.bfloat16),
        grad_v.astype(jnp.bfloat16),
    )


def per_device(query, keys, values, out_weight, grad_out, far_blocks, far_live):
    n_dp = lax.axis_size("dp")
    n_seq = lax.axis_size("seq")
    d_idx = lax.axis_index("dp")
    s_idx = lax.axis_index("seq")
    head_count = far_blocks.shape[1]
    per_dev = head_count // n_seq
    features = query.shape[2]
    head_dim = features // head_count
    width = per_dev * head_dim
    number = far_blocks.shape[2]

    stacked = jnp.stack([query[0], keys[0], values[0]])
    heads_qkv = lax.all_to_all(stacked, "seq", split_axis=2, concat_axis=1, tiled=True)
    length = heads_qkv.shape[1]
    block_rows = length // number

    weight = lax.all_gather(out_weight, "dp", axis=0, tiled=True)
    grad_doc = lax.all_gather(grad_out[0], "seq", axis=0, tiled=True)
    lower = s_idx * width
    weight_rows = lax.dynamic_slice_in_dim(weight, lower, width, 0)
    grad_heads = lax.dot_general(
        grad_doc, weight_rows, (((1,), (1,)), ((), ())), preferred_element_type=jnp.float32
    ).astype(jnp.bfloat16)

    def by_head(array):
        return array.reshape(length, per_dev, head_dim).transpose(1, 0, 2)

    head_start = s_idx * per_dev
    blocks_dev = lax.dynamic_slice_in_dim(far_blocks[0], head_start, per_dev, 0)
    live_dev = lax.dynamic_slice_in_dim(far_live[0], head_start, per_dev, 0)
    mask = block_mask(blocks_dev, live_dev)

    results = heads_attention(
        by_head(heads_qkv[0]),
        by_head(heads_qkv[1]),
        by_head(heads_qkv[2]),
        by_head(grad_heads),
        mask,
        block_rows,
    )
    flat = jnp.stack([r.transpose(1, 0, 2).reshape(length, width) for r in results])
    attn_heads = flat[0]
    back = lax.all_to_all(flat, "seq", split_axis=1, concat_axis=2, tiled=True)
    attention = back[0]
    mixed = jnp.dot(attention, weight, preferred_element_type=jnp.float32).astype(jnp.bfloat16)[
        None
    ]

    norm_factor = (n_dp * query.shape[0] * length) ** (-0.5)
    partial = lax.dot_general(
        attn_heads, grad_doc, (((0,), (0,)), ((), ())), preferred_element_type=jnp.float32
    )
    reduced = lax.psum_scatter(partial * norm_factor, "dp", scatter_dimension=0, tiled=True)
    perm = []
    for d in range(n_dp):
        for s in range(n_seq):
            block = s * n_dp + d
            perm.append((d * n_seq + s, block))
    weight_grad = lax.ppermute(reduced, ("dp", "seq"), perm=perm)
    return (mixed, back[1][None], back[2][None], back[3][None], weight_grad)


def solution(mesh):
    in_specs = (
        P("dp", "seq", None),
        P("dp", "seq", None),
        P("dp", "seq", None),
        P("dp", None),
        P("dp", "seq", None),
        P("dp", None, None, None),
        P("dp", None, None),
    )
    out_specs = (
        P("dp", "seq", None),
        P("dp", "seq", None),
        P("dp", "seq", None),
        P("dp", "seq", None),
        P(("dp", "seq"), None),
    )
    return jax.shard_map(
        per_device, mesh=mesh, in_specs=in_specs, out_specs=out_specs, check_vma=False
    )
```

```python
import functools

import jax
import jax.numpy as jnp
from jax import lax
from jax.sharding import PartitionSpec as P

NEG = -1e30


def block_mask(blocks, live):
    number = blocks.shape[1]
    rows = jnp.arange(number, dtype=jnp.int32)[:, None]
    cols = jnp.arange(number, dtype=jnp.int32)[None, :]
    window = jnp.abs(rows - cols) <= 1
    far_pos = jnp.arange(blocks.shape[2], dtype=jnp.int32)
    far_used = far_pos[None, None, :] < live[:, :, None]
    hits = (blocks[:, :, :, None] == cols[None, None, :, :]) & far_used[:, :, :, None]
    return window[None] | jnp.any(hits, axis=2)


def expand_mask(mask, block_rows):
    h, nb, _ = mask.shape
    full = jnp.broadcast_to(mask[:, :, None, :, None], (h, nb, block_rows, nb, block_rows))
    return full.reshape(h, nb * block_rows, nb * block_rows)


def heads_attention(q, k, v, g, mask, block_rows):
    head_dim = q.shape[-1]
    scale = head_dim ** (-0.5)
    visible = expand_mask(mask, block_rows)
    raw = jnp.einsum("hqd,hkd->hqk", q, k, preferred_element_type=jnp.float32) * scale
    scores = jnp.where(visible, raw, NEG)
    row_max = jnp.max(scores, axis=-1, keepdims=True)
    log_total = row_max + jnp.log(jnp.sum(jnp.exp(scores - row_max), axis=-1, keepdims=True))
    softmax_w = jnp.exp(scores - log_total)
    probs = softmax_w.astype(jnp.bfloat16)
    attention = jnp.einsum("hqk,hkd->hqd", probs, v, preferred_element_type=jnp.float32).astype(
        jnp.bfloat16
    )
    row_dots = jnp.sum(
        g.astype(jnp.float32) * attention.astype(jnp.float32), axis=-1, keepdims=True
    )
    grad_probs = jnp.einsum("hqd,hkd->hqk", g, v, preferred_element_type=jnp.float32)
    dscore = (softmax_w * (grad_probs - row_dots)).astype(jnp.bfloat16)
    grad_q = scale * jnp.einsum("hqk,hkd->hqd", dscore, k, preferred_element_type=jnp.float32)
    grad_k = scale * jnp.einsum("hqk,hqd->hkd", dscore, q, preferred_element_type=jnp.float32)
    grad_v = jnp.einsum("hqk,hqd->hkd", probs, g, preferred_element_type=jnp.float32)
    return (
        attention,
        grad_q.astype(jnp.bfloat16),
        grad_k.astype(jnp.bfloat16),
        grad_v.astype(jnp.bfloat16),
    )


def ring_gather(block, ring, axis):
    n = len(ring)
    position = [0] * n
    for p, member in enumerate(ring):
        position[member] = p
    forward = [(ring[p], ring[(p + 1) % n]) for p in range(n)]
    backward = [(ring[p], ring[(p - 1) % n]) for p in range(n)]
    ring_arr = jnp.array(ring, jnp.int32)
    me = lax.axis_index(axis)
    p = jnp.array(position, jnp.int32)[me]
    out = jnp.zeros((n,) + block.shape, block.dtype)
    out = lax.dynamic_update_index_in_dim(out, block, me, 0)
    ahead, behind = block, block
    n_fwd = n // 2
    n_bwd = n - 1 - n_fwd
    for k in range(1, n_fwd + 1):
        ahead = lax.ppermute(ahead, axis, forward)
        out = lax.dynamic_update_index_in_dim(out, ahead, ring_arr[(p - k) % n], 0)
        if k <= n_bwd:
            behind = lax.ppermute(behind, axis, backward)
            out = lax.dynamic_update_index_in_dim(out, behind, ring_arr[(p + k) % n], 0)
    return out.reshape((n * block.shape[0],) + block.shape[1:])


def per_device(ring, query, keys, values, out_weight, grad_out, far_blocks, far_live):
    n_dp = lax.axis_size("dp")
    n_seq = lax.axis_size("seq")
    d_idx = lax.axis_index("dp")
    s_idx = lax.axis_index("seq")
    head_count = far_blocks.shape[1]
    per_dev = head_count // n_seq
    features = query.shape[2]
    head_dim = features // head_count
    width = per_dev * head_dim
    number = far_blocks.shape[2]

    stacked = jnp.stack([query[0], keys[0], values[0]])
    heads_qkv = lax.all_to_all(stacked, "seq", split_axis=2, concat_axis=1, tiled=True)
    length = heads_qkv.shape[1]
    block_rows = length // number

    weight = lax.all_gather(out_weight, "dp", axis=0, tiled=True)
    grad_doc = ring_gather(grad_out[0], ring, "seq")
    lower = s_idx * width
    weight_rows = lax.dynamic_slice_in_dim(weight, lower, width, 0)
    grad_heads = lax.dot_general(
        grad_doc, weight_rows, (((1,), (1,)), ((), ())), preferred_element_type=jnp.float32
    ).astype(jnp.bfloat16)

    def by_head(array):
        return array.reshape(length, per_dev, head_dim).transpose(1, 0, 2)

    head_start = s_idx * per_dev
    blocks_dev = lax.dynamic_slice_in_dim(far_blocks[0], head_start, per_dev, 0)
    live_dev = lax.dynamic_slice_in_dim(far_live[0], head_start, per_dev, 0)
    mask = block_mask(blocks_dev, live_dev)

    results = heads_attention(
        by_head(heads_qkv[0]),
        by_head(heads_qkv[1]),
        by_head(heads_qkv[2]),
        by_head(grad_heads),
        mask,
        block_rows,
    )
    flat = jnp.stack([r.transpose(1, 0, 2).reshape(length, width) for r in results])
    attn_heads = flat[0]
    back = lax.all_to_all(flat, "seq", split_axis=1, concat_axis=2, tiled=True)
    attention = back[0]
    mixed = jnp.dot(attention, weight, preferred_element_type=jnp.float32).astype(jnp.bfloat16)[
        None
    ]

    norm_factor = (n_dp * query.shape[0] * length) ** (-0.5)
    partial = lax.dot_general(
        attn_heads, grad_doc, (((0,), (0,)), ((), ())), preferred_element_type=jnp.float32
    )
    reduced = lax.psum_scatter(partial * norm_factor, "dp", scatter_dimension=0, tiled=True)
    perm = []
    for d in range(n_dp):
        for s in range(n_seq):
            block = s * n_dp + d
            perm.append((d * n_seq + s, block))
    weight_grad = lax.ppermute(reduced, ("dp", "seq"), perm=perm)
    return (mixed, back[1][None], back[2][None], back[3][None], weight_grad)


def grid_cycle(rows, cols):
    cycle = [(r, 0) for r in range(rows)]
    for i, r in enumerate(range(rows - 1, -1, -1)):
        span = range(1, cols) if i % 2 == 0 else range(cols - 1, 0, -1)
        cycle.extend((r, c) for c in span)
    return cycle


def seq_ring(mesh):
    n_seq = mesh.shape["seq"]
    try:
        column = mesh.devices.reshape(-1, n_seq)[0]
        coords = [(d.coords[2], d.coords[0]) for d in column]
        zs = sorted({c[0] for c in coords})
        xs = sorted({c[1] for c in coords})
        where = {c: s for s, c in enumerate(coords)}
        if len(where) == n_seq and len(zs) * len(xs) == n_seq:
            if len(zs) % 2 == 0:
                cells = [(zs[r], xs[c]) for r, c in grid_cycle(len(zs), len(xs))]
            else:
                cells = [(zs[c], xs[r]) for r, c in grid_cycle(len(xs), len(zs))]
            order = [where[c] for c in cells]
            if sorted(order) == list(range(n_seq)):
                return tuple(order)
    except (AttributeError, IndexError, TypeError, KeyError):
        pass
    return tuple(range(n_seq))


def solution(mesh):
    ring = seq_ring(mesh)
    in_specs = (
        P("dp", "seq", None),
        P("dp", "seq", None),
        P("dp", "seq", None),
        P("dp", None),
        P("dp", "seq", None),
        P("dp", None, None, None),
        P("dp", None, None),
    )
    out_specs = (
        P("dp", "seq", None),
        P("dp", "seq", None),
        P("dp", "seq", None),
        P("dp", "seq", None),
        P(("dp", "seq"), None),
    )
    return jax.shard_map(
        functools.partial(per_device, ring), mesh=mesh, in_specs=in_specs, out_specs=out_specs, check_vma=False
    )
```

```python
import functools

import jax
import jax.numpy as jnp
from jax import lax
from jax.sharding import PartitionSpec as P

NEG = -1e30


def block_mask(blocks, live):
    number = blocks.shape[1]
    rows = jnp.arange(number, dtype=jnp.int32)[:, None]
    cols = jnp.arange(number, dtype=jnp.int32)[None, :]
    window = jnp.abs(rows - cols) <= 1
    far_pos = jnp.arange(blocks.shape[2], dtype=jnp.int32)
    far_used = far_pos[None, None, :] < live[:, :, None]
    hits = (blocks[:, :, :, None] == cols[None, None, :, :]) & far_used[:, :, :, None]
    return window[None] | jnp.any(hits, axis=2)


def one_head(q, k, v, g, mask, number):
    length, head_dim = q.shape
    rows = length // number
    scale = head_dim ** (-0.5)
    qb = q.reshape(number, rows, head_dim)
    gb = g.reshape(number, rows, head_dim)
    visible = jnp.repeat(mask, rows, axis=1)[:, None, :]
    raw = jnp.einsum("bqd,kd->bqk", qb, k, preferred_element_type=jnp.float32) * scale
    scores = jnp.where(visible, raw, NEG)
    row_max = jnp.max(scores, axis=-1, keepdims=True)
    log_total = row_max + jnp.log(jnp.sum(jnp.exp(scores - row_max), axis=-1, keepdims=True))
    softmax_w = jnp.exp(scores - log_total)
    probs = softmax_w.astype(jnp.bfloat16)
    attention = jnp.einsum("bqk,kd->bqd", probs, v, preferred_element_type=jnp.float32).astype(
        jnp.bfloat16
    )
    row_dots = jnp.sum(
        gb.astype(jnp.float32) * attention.astype(jnp.float32), axis=-1, keepdims=True
    )
    grad_probs = jnp.einsum("bqd,kd->bqk", gb, v, preferred_element_type=jnp.float32)
    dscore = (softmax_w * (grad_probs - row_dots)).astype(jnp.bfloat16)
    grad_q = scale * jnp.einsum("bqk,kd->bqd", dscore, k, preferred_element_type=jnp.float32)
    grad_k = scale * jnp.einsum("bqk,bqd->kd", dscore, qb, preferred_element_type=jnp.float32)
    grad_v = jnp.einsum("bqk,bqd->kd", probs, gb, preferred_element_type=jnp.float32)
    return (
        attention.reshape(length, head_dim),
        grad_q.reshape(length, head_dim).astype(jnp.bfloat16),
        grad_k.astype(jnp.bfloat16),
        grad_v.astype(jnp.bfloat16),
    )


def ring_gather(block, ring, axis):
    n = len(ring)
    position = [0] * n
    for p, member in enumerate(ring):
        position[member] = p
    forward = [(ring[p], ring[(p + 1) % n]) for p in range(n)]
    backward = [(ring[p], ring[(p - 1) % n]) for p in range(n)]
    ring_arr = jnp.array(ring, jnp.int32)
    me = lax.axis_index(axis)
    p = jnp.array(position, jnp.int32)[me]
    out = jnp.zeros((n,) + block.shape, block.dtype)
    out = lax.dynamic_update_index_in_dim(out, block, me, 0)
    ahead, behind = block, block
    n_fwd = n // 2
    n_bwd = n - 1 - n_fwd
    for k in range(1, n_fwd + 1):
        ahead = lax.ppermute(ahead, axis, forward)
        out = lax.dynamic_update_index_in_dim(out, ahead, ring_arr[(p - k) % n], 0)
        if k <= n_bwd:
            behind = lax.ppermute(behind, axis, backward)
            out = lax.dynamic_update_index_in_dim(out, behind, ring_arr[(p + k) % n], 0)
    return out.reshape((n * block.shape[0],) + block.shape[1:])


def per_device(ring, query, keys, values, out_weight, grad_out, far_blocks, far_live):
    n_dp = lax.axis_size("dp")
    n_seq = lax.axis_size("seq")
    d_idx = lax.axis_index("dp")
    s_idx = lax.axis_index("seq")
    head_count = far_blocks.shape[1]
    per_dev = head_count // n_seq
    features = query.shape[2]
    head_dim = features // head_count
    width = per_dev * head_dim
    number = far_blocks.shape[2]

    stacked = jnp.stack([query[0], keys[0], values[0]])
    heads_qkv = lax.all_to_all(stacked, "seq", split_axis=2, concat_axis=1, tiled=True)
    length = heads_qkv.shape[1]
    block_rows = length // number

    weight = lax.all_gather(out_weight, "dp", axis=0, tiled=True)
    grad_doc = ring_gather(grad_out[0], ring, "seq")
    lower = s_idx * width
    weight_rows = lax.dynamic_slice_in_dim(weight, lower, width, 0)
    grad_heads = lax.dot_general(
        grad_doc, weight_rows, (((1,), (1,)), ((), ())), preferred_element_type=jnp.float32
    ).astype(jnp.bfloat16)

    head_start = s_idx * per_dev
    blocks_dev = lax.dynamic_slice_in_dim(far_blocks[0], head_start, per_dev, 0)
    live_dev = lax.dynamic_slice_in_dim(far_live[0], head_start, per_dev, 0)
    mask = block_mask(blocks_dev, live_dev)

    results = []
    for head in range(per_dev):
        cols = slice(head * head_dim, (head + 1) * head_dim)
        results.append(
            one_head(
                heads_qkv[0][:, cols],
                heads_qkv[1][:, cols],
                heads_qkv[2][:, cols],
                grad_heads[:, cols],
                mask[head],
                number,
            )
        )
    attn_heads = jnp.concatenate([r[0] for r in results], axis=1)
    attention = lax.all_to_all(attn_heads, "seq", split_axis=0, concat_axis=1, tiled=True)
    mixed = jnp.dot(attention, weight, preferred_element_type=jnp.float32).astype(jnp.bfloat16)[
        None
    ]
    grads = jnp.stack(
        [jnp.concatenate([r[i] for r in results], axis=1) for i in (1, 2, 3)]
    )
    back = lax.all_to_all(grads, "seq", split_axis=1, concat_axis=2, tiled=True)

    norm_factor = (n_dp * query.shape[0] * length) ** (-0.5)
    partial = lax.dot_general(
        attn_heads, grad_doc, (((0,), (0,)), ((), ())), preferred_element_type=jnp.float32
    )
    reduced = lax.psum_scatter(partial * norm_factor, "dp", scatter_dimension=0, tiled=True)
    perm = []
    for d in range(n_dp):
        for s in range(n_seq):
            block = s * n_dp + d
            perm.append((d * n_seq + s, block))
    weight_grad = lax.ppermute(reduced, ("dp", "seq"), perm=perm)
    return (mixed, back[0][None], back[1][None], back[2][None], weight_grad)


def grid_cycle(rows, cols):
    cycle = [(r, 0) for r in range(rows)]
    for i, r in enumerate(range(rows - 1, -1, -1)):
        span = range(1, cols) if i % 2 == 0 else range(cols - 1, 0, -1)
        cycle.extend((r, c) for c in span)
    return cycle


def seq_ring(mesh):
    n_seq = mesh.shape["seq"]
    try:
        column = mesh.devices.reshape(-1, n_seq)[0]
        coords = [(d.coords[2], d.coords[0]) for d in column]
        zs = sorted({c[0] for c in coords})
        xs = sorted({c[1] for c in coords})
        where = {c: s for s, c in enumerate(coords)}
        if len(where) == n_seq and len(zs) * len(xs) == n_seq:
            if len(zs) % 2 == 0:
                cells = [(zs[r], xs[c]) for r, c in grid_cycle(len(zs), len(xs))]
            else:
                cells = [(zs[c], xs[r]) for r, c in grid_cycle(len(xs), len(zs))]
            order = [where[c] for c in cells]
            if sorted(order) == list(range(n_seq)):
                return tuple(order)
    except (AttributeError, IndexError, TypeError, KeyError):
        pass
    return tuple(range(n_seq))


def solution(mesh):
    ring = seq_ring(mesh)
    in_specs = (
        P("dp", "seq", None),
        P("dp", "seq", None),
        P("dp", "seq", None),
        P("dp", None),
        P("dp", "seq", None),
        P("dp", None, None, None),
        P("dp", None, None),
    )
    out_specs = (
        P("dp", "seq", None),
        P("dp", "seq", None),
        P("dp", "seq", None),
        P("dp", "seq", None),
        P(("dp", "seq"), None),
    )
    return jax.shard_map(
        functools.partial(per_device, ring), mesh=mesh, in_specs=in_specs, out_specs=out_specs, check_vma=False
    )
```

```python
import functools

import jax
import jax.numpy as jnp
from jax import lax
from jax.sharding import PartitionSpec as P

NEG = -1e30


def block_mask(blocks, live):
    number = blocks.shape[1]
    rows = jnp.arange(number, dtype=jnp.int32)[:, None]
    cols = jnp.arange(number, dtype=jnp.int32)[None, :]
    window = jnp.abs(rows - cols) <= 1
    far_pos = jnp.arange(blocks.shape[2], dtype=jnp.int32)
    far_used = far_pos[None, None, :] < live[:, :, None]
    hits = (blocks[:, :, :, None] == cols[None, None, :, :]) & far_used[:, :, :, None]
    return window[None] | jnp.any(hits, axis=2)


def one_head(q, k, v, g, mask, number):
    length, head_dim = q.shape
    rows = length // number
    scale = head_dim ** (-0.5)
    qb = q.reshape(number, rows, head_dim)
    gb = g.reshape(number, rows, head_dim)
    visible = jnp.repeat(mask, rows, axis=1)[:, None, :]
    raw = jnp.einsum("bqd,kd->bqk", qb, k, preferred_element_type=jnp.float32) * scale
    scores = jnp.where(visible, raw, NEG)
    row_max = jnp.max(scores, axis=-1, keepdims=True)
    log_total = row_max + jnp.log(jnp.sum(jnp.exp(scores - row_max), axis=-1, keepdims=True))
    softmax_w = jnp.exp(scores - log_total)
    probs = softmax_w.astype(jnp.bfloat16)
    attention = jnp.einsum("bqk,kd->bqd", probs, v, preferred_element_type=jnp.float32).astype(
        jnp.bfloat16
    )
    row_dots = jnp.sum(
        gb.astype(jnp.float32) * attention.astype(jnp.float32), axis=-1, keepdims=True
    )
    grad_probs = jnp.einsum("bqd,kd->bqk", gb, v, preferred_element_type=jnp.float32)
    dscore = (softmax_w * (grad_probs - row_dots)).astype(jnp.bfloat16)
    grad_q = scale * jnp.einsum("bqk,kd->bqd", dscore, k, preferred_element_type=jnp.float32)
    grad_k = scale * jnp.einsum("bqk,bqd->kd", dscore, qb, preferred_element_type=jnp.float32)
    grad_v = jnp.einsum("bqk,bqd->kd", probs, gb, preferred_element_type=jnp.float32)
    return (
        attention.reshape(length, head_dim),
        grad_q.reshape(length, head_dim).astype(jnp.bfloat16),
        grad_k.astype(jnp.bfloat16),
        grad_v.astype(jnp.bfloat16),
    )


def ring_gather(block, ring, axis):
    n = len(ring)
    position = [0] * n
    for p, member in enumerate(ring):
        position[member] = p
    forward = [(ring[p], ring[(p + 1) % n]) for p in range(n)]
    backward = [(ring[p], ring[(p - 1) % n]) for p in range(n)]
    ring_arr = jnp.array(ring, jnp.int32)
    me = lax.axis_index(axis)
    p = jnp.array(position, jnp.int32)[me]
    out = jnp.zeros((n,) + block.shape, block.dtype)
    out = lax.dynamic_update_index_in_dim(out, block, me, 0)
    ahead, behind = block, block
    n_fwd = n // 2
    n_bwd = n - 1 - n_fwd
    for k in range(1, n_fwd + 1):
        ahead = lax.ppermute(ahead, axis, forward)
        out = lax.dynamic_update_index_in_dim(out, ahead, ring_arr[(p - k) % n], 0)
        if k <= n_bwd:
            behind = lax.ppermute(behind, axis, backward)
            out = lax.dynamic_update_index_in_dim(out, behind, ring_arr[(p + k) % n], 0)
    return out.reshape((n * block.shape[0],) + block.shape[1:])


def per_device(ring, query, keys, values, out_weight, grad_out, far_blocks, far_live):
    n_dp = lax.axis_size("dp")
    n_seq = lax.axis_size("seq")
    d_idx = lax.axis_index("dp")
    s_idx = lax.axis_index("seq")
    head_count = far_blocks.shape[1]
    per_dev = head_count // n_seq
    features = query.shape[2]
    head_dim = features // head_count
    width = per_dev * head_dim
    number = far_blocks.shape[2]

    stacked = jnp.stack([query[0], keys[0], values[0]])
    heads_qkv = lax.all_to_all(stacked, "seq", split_axis=2, concat_axis=1, tiled=True)
    length = heads_qkv.shape[1]
    block_rows = length // number

    weight = lax.all_gather(out_weight, "dp", axis=0, tiled=True)
    grad_tokens = lax.dot_general(
        grad_out[0], weight, (((1,), (1,)), ((), ())), preferred_element_type=jnp.float32
    ).astype(jnp.bfloat16)
    grad_heads = lax.all_to_all(grad_tokens, "seq", split_axis=1, concat_axis=0, tiled=True)
    grad_src, grad_heads = lax.optimization_barrier((grad_out[0], grad_heads))
    grad_doc = ring_gather(grad_src, ring, "seq")

    head_start = s_idx * per_dev
    blocks_dev = lax.dynamic_slice_in_dim(far_blocks[0], head_start, per_dev, 0)
    live_dev = lax.dynamic_slice_in_dim(far_live[0], head_start, per_dev, 0)
    mask = block_mask(blocks_dev, live_dev)

    results = []
    for head in range(per_dev):
        cols = slice(head * head_dim, (head + 1) * head_dim)
        results.append(
            one_head(
                heads_qkv[0][:, cols],
                heads_qkv[1][:, cols],
                heads_qkv[2][:, cols],
                grad_heads[:, cols],
                mask[head],
                number,
            )
        )
    attn_heads = jnp.concatenate([r[0] for r in results], axis=1)
    attention = lax.all_to_all(attn_heads, "seq", split_axis=0, concat_axis=1, tiled=True)
    mixed = jnp.dot(attention, weight, preferred_element_type=jnp.float32).astype(jnp.bfloat16)[
        None
    ]
    grads = jnp.stack(
        [jnp.concatenate([r[i] for r in results], axis=1) for i in (1, 2, 3)]
    )
    back = lax.all_to_all(grads, "seq", split_axis=1, concat_axis=2, tiled=True)

    norm_factor = (n_dp * query.shape[0] * length) ** (-0.5)
    partial = lax.dot_general(
        attn_heads, grad_doc, (((0,), (0,)), ((), ())), preferred_element_type=jnp.float32
    )
    reduced = lax.psum_scatter(partial * norm_factor, "dp", scatter_dimension=0, tiled=True)
    perm = []
    for d in range(n_dp):
        for s in range(n_seq):
            block = s * n_dp + d
            perm.append((d * n_seq + s, block))
    weight_grad = lax.ppermute(reduced, ("dp", "seq"), perm=perm)
    return (mixed, back[0][None], back[1][None], back[2][None], weight_grad)


def grid_cycle(rows, cols):
    cycle = [(r, 0) for r in range(rows)]
    for i, r in enumerate(range(rows - 1, -1, -1)):
        span = range(1, cols) if i % 2 == 0 else range(cols - 1, 0, -1)
        cycle.extend((r, c) for c in span)
    return cycle


def seq_ring(mesh):
    n_seq = mesh.shape["seq"]
    try:
        column = mesh.devices.reshape(-1, n_seq)[0]
        coords = [(d.coords[2], d.coords[0]) for d in column]
        zs = sorted({c[0] for c in coords})
        xs = sorted({c[1] for c in coords})
        where = {c: s for s, c in enumerate(coords)}
        if len(where) == n_seq and len(zs) * len(xs) == n_seq:
            if len(zs) % 2 == 0:
                cells = [(zs[r], xs[c]) for r, c in grid_cycle(len(zs), len(xs))]
            else:
                cells = [(zs[c], xs[r]) for r, c in grid_cycle(len(xs), len(zs))]
            order = [where[c] for c in cells]
            if sorted(order) == list(range(n_seq)):
                return tuple(order)
    except (AttributeError, IndexError, TypeError, KeyError):
        pass
    return tuple(range(n_seq))


def solution(mesh):
    ring = seq_ring(mesh)
    in_specs = (
        P("dp", "seq", None),
        P("dp", "seq", None),
        P("dp", "seq", None),
        P("dp", None),
        P("dp", "seq", None),
        P("dp", None, None, None),
        P("dp", None, None),
    )
    out_specs = (
        P("dp", "seq", None),
        P("dp", "seq", None),
        P("dp", "seq", None),
        P("dp", "seq", None),
        P(("dp", "seq"), None),
    )
    return jax.shard_map(
        functools.partial(per_device, ring), mesh=mesh, in_specs=in_specs, out_specs=out_specs, check_vma=False
    )
```

```python
import functools

import jax
import jax.numpy as jnp
from jax import lax
from jax.sharding import PartitionSpec as P

NEG = -1e30


def block_mask(blocks, live):
    number = blocks.shape[1]
    rows = jnp.arange(number, dtype=jnp.int32)[:, None]
    cols = jnp.arange(number, dtype=jnp.int32)[None, :]
    window = jnp.abs(rows - cols) <= 1
    far_pos = jnp.arange(blocks.shape[2], dtype=jnp.int32)
    far_used = far_pos[None, None, :] < live[:, :, None]
    hits = (blocks[:, :, :, None] == cols[None, None, :, :]) & far_used[:, :, :, None]
    return window[None] | jnp.any(hits, axis=2)


def one_head(q, k, v, g, mask, number):
    length, head_dim = q.shape
    rows = length // number
    scale = head_dim ** (-0.5)
    qb = q.reshape(number, rows, head_dim)
    gb = g.reshape(number, rows, head_dim)
    visible = jnp.repeat(mask, rows, axis=1)[:, None, :]
    raw = jnp.einsum("bqd,kd->bqk", qb, k, preferred_element_type=jnp.float32) * scale
    scores = jnp.where(visible, raw, NEG)
    row_max = jnp.max(scores, axis=-1, keepdims=True)
    log_total = row_max + jnp.log(jnp.sum(jnp.exp(scores - row_max), axis=-1, keepdims=True))
    softmax_w = jnp.exp(scores - log_total)
    probs = softmax_w.astype(jnp.bfloat16)
    attention = jnp.einsum("bqk,kd->bqd", probs, v, preferred_element_type=jnp.float32).astype(
        jnp.bfloat16
    )
    row_dots = jnp.sum(
        gb.astype(jnp.float32) * attention.astype(jnp.float32), axis=-1, keepdims=True
    )
    grad_probs = jnp.einsum("bqd,kd->bqk", gb, v, preferred_element_type=jnp.float32)
    dscore = (softmax_w * (grad_probs - row_dots)).astype(jnp.bfloat16)
    grad_q = scale * jnp.einsum("bqk,kd->bqd", dscore, k, preferred_element_type=jnp.float32)
    grad_k = scale * jnp.einsum("bqk,bqd->kd", dscore, qb, preferred_element_type=jnp.float32)
    grad_v = jnp.einsum("bqk,bqd->kd", probs, gb, preferred_element_type=jnp.float32)
    return (
        attention.reshape(length, head_dim),
        grad_q.reshape(length, head_dim).astype(jnp.bfloat16),
        grad_k.astype(jnp.bfloat16),
        grad_v.astype(jnp.bfloat16),
    )


def ring_gather(block, ring, axis):
    n = len(ring)
    position = [0] * n
    for p, member in enumerate(ring):
        position[member] = p
    forward = [(ring[p], ring[(p + 1) % n]) for p in range(n)]
    backward = [(ring[p], ring[(p - 1) % n]) for p in range(n)]
    ring_arr = jnp.array(ring, jnp.int32)
    me = lax.axis_index(axis)
    p = jnp.array(position, jnp.int32)[me]
    out = jnp.zeros((n,) + block.shape, block.dtype)
    out = lax.dynamic_update_index_in_dim(out, block, me, 0)
    ahead, behind = block, block
    n_fwd = n // 2
    n_bwd = n - 1 - n_fwd
    for k in range(1, n_fwd + 1):
        ahead = lax.ppermute(ahead, axis, forward)
        out = lax.dynamic_update_index_in_dim(out, ahead, ring_arr[(p - k) % n], 0)
        if k <= n_bwd:
            behind = lax.ppermute(behind, axis, backward)
            out = lax.dynamic_update_index_in_dim(out, behind, ring_arr[(p + k) % n], 0)
    return out.reshape((n * block.shape[0],) + block.shape[1:])


def permute_all_to_all(x, ring, axis, split_axis, concat_axis):
    n = len(ring)
    position = [0] * n
    for p, member in enumerate(ring):
        position[member] = p
    ring_arr = jnp.array(ring, jnp.int32)
    me = lax.axis_index(axis)
    p = jnp.array(position, jnp.int32)[me]
    piece = x.shape[split_axis] // n
    shape = list(x.shape)
    shape[split_axis] = piece
    shape[concat_axis] = shape[concat_axis] * n
    out = jnp.zeros(shape, x.dtype)
    span = x.shape[concat_axis]
    own = lax.dynamic_slice_in_dim(x, me * piece, piece, split_axis)
    out = lax.dynamic_update_slice_in_dim(out, own, me * span, concat_axis)
    for k in range(1, n):
        perm = [(ring[q], ring[(q + k) % n]) for q in range(n)]
        dest = ring_arr[(p + k) % n]
        sent = lax.dynamic_slice_in_dim(x, dest * piece, piece, split_axis)
        got = lax.ppermute(sent, axis, perm)
        src = ring_arr[(p - k) % n]
        out = lax.dynamic_update_slice_in_dim(out, got, src * span, concat_axis)
    return out


def per_device(ring, query, keys, values, out_weight, grad_out, far_blocks, far_live):
    n_dp = lax.axis_size("dp")
    n_seq = lax.axis_size("seq")
    d_idx = lax.axis_index("dp")
    s_idx = lax.axis_index("seq")
    head_count = far_blocks.shape[1]
    per_dev = head_count // n_seq
    features = query.shape[2]
    head_dim = features // head_count
    width = per_dev * head_dim
    number = far_blocks.shape[2]

    stacked = jnp.stack([query[0], keys[0], values[0]])
    heads_qkv = permute_all_to_all(stacked, ring, "seq", 2, 1)
    length = heads_qkv.shape[1]
    block_rows = length // number

    weight = lax.all_gather(out_weight, "dp", axis=0, tiled=True)
    grad_doc = ring_gather(grad_out[0], ring, "seq")
    lower = s_idx * width
    weight_rows = lax.dynamic_slice_in_dim(weight, lower, width, 0)
    grad_heads = lax.dot_general(
        grad_doc, weight_rows, (((1,), (1,)), ((), ())), preferred_element_type=jnp.float32
    ).astype(jnp.bfloat16)

    head_start = s_idx * per_dev
    blocks_dev = lax.dynamic_slice_in_dim(far_blocks[0], head_start, per_dev, 0)
    live_dev = lax.dynamic_slice_in_dim(far_live[0], head_start, per_dev, 0)
    mask = block_mask(blocks_dev, live_dev)

    results = []
    for head in range(per_dev):
        cols = slice(head * head_dim, (head + 1) * head_dim)
        results.append(
            one_head(
                heads_qkv[0][:, cols],
                heads_qkv[1][:, cols],
                heads_qkv[2][:, cols],
                grad_heads[:, cols],
                mask[head],
                number,
            )
        )
    attn_heads = jnp.concatenate([r[0] for r in results], axis=1)
    attention = lax.all_to_all(attn_heads, "seq", split_axis=0, concat_axis=1, tiled=True)
    mixed = jnp.dot(attention, weight, preferred_element_type=jnp.float32).astype(jnp.bfloat16)[
        None
    ]
    grads = jnp.stack(
        [jnp.concatenate([r[i] for r in results], axis=1) for i in (1, 2, 3)]
    )
    back = lax.all_to_all(grads, "seq", split_axis=1, concat_axis=2, tiled=True)

    norm_factor = (n_dp * query.shape[0] * length) ** (-0.5)
    partial = lax.dot_general(
        attn_heads, grad_doc, (((0,), (0,)), ((), ())), preferred_element_type=jnp.float32
    )
    reduced = lax.psum_scatter(partial * norm_factor, "dp", scatter_dimension=0, tiled=True)
    perm = []
    for d in range(n_dp):
        for s in range(n_seq):
            block = s * n_dp + d
            perm.append((d * n_seq + s, block))
    weight_grad = lax.ppermute(reduced, ("dp", "seq"), perm=perm)
    return (mixed, back[0][None], back[1][None], back[2][None], weight_grad)


def grid_cycle(rows, cols):
    cycle = [(r, 0) for r in range(rows)]
    for i, r in enumerate(range(rows - 1, -1, -1)):
        span = range(1, cols) if i % 2 == 0 else range(cols - 1, 0, -1)
        cycle.extend((r, c) for c in span)
    return cycle


def seq_ring(mesh):
    n_seq = mesh.shape["seq"]
    try:
        column = mesh.devices.reshape(-1, n_seq)[0]
        coords = [(d.coords[2], d.coords[0]) for d in column]
        zs = sorted({c[0] for c in coords})
        xs = sorted({c[1] for c in coords})
        where = {c: s for s, c in enumerate(coords)}
        if len(where) == n_seq and len(zs) * len(xs) == n_seq:
            if len(zs) % 2 == 0:
                cells = [(zs[r], xs[c]) for r, c in grid_cycle(len(zs), len(xs))]
            else:
                cells = [(zs[c], xs[r]) for r, c in grid_cycle(len(xs), len(zs))]
            order = [where[c] for c in cells]
            if sorted(order) == list(range(n_seq)):
                return tuple(order)
    except (AttributeError, IndexError, TypeError, KeyError):
        pass
    return tuple(range(n_seq))


def solution(mesh):
    ring = seq_ring(mesh)
    in_specs = (
        P("dp", "seq", None),
        P("dp", "seq", None),
        P("dp", "seq", None),
        P("dp", None),
        P("dp", "seq", None),
        P("dp", None, None, None),
        P("dp", None, None),
    )
    out_specs = (
        P("dp", "seq", None),
        P("dp", "seq", None),
        P("dp", "seq", None),
        P("dp", "seq", None),
        P(("dp", "seq"), None),
    )
    return jax.shard_map(
        functools.partial(per_device, ring), mesh=mesh, in_specs=in_specs, out_specs=out_specs, check_vma=False
    )
```

```python
import functools

import jax
import jax.numpy as jnp
from jax import lax
from jax.sharding import PartitionSpec as P

NEG = -1e30


def block_mask(blocks, live):
    number = blocks.shape[1]
    rows = jnp.arange(number, dtype=jnp.int32)[:, None]
    cols = jnp.arange(number, dtype=jnp.int32)[None, :]
    window = jnp.abs(rows - cols) <= 1
    far_pos = jnp.arange(blocks.shape[2], dtype=jnp.int32)
    far_used = far_pos[None, None, :] < live[:, :, None]
    hits = (blocks[:, :, :, None] == cols[None, None, :, :]) & far_used[:, :, :, None]
    return window[None] | jnp.any(hits, axis=2)


def one_head(q, k, v, g, mask, number):
    length, head_dim = q.shape
    rows = length // number
    scale = head_dim ** (-0.5)
    qb = q.reshape(number, rows, head_dim)
    gb = g.reshape(number, rows, head_dim)
    visible = jnp.repeat(mask, rows, axis=1)[:, None, :]
    raw = jnp.einsum("bqd,kd->bqk", qb, k, preferred_element_type=jnp.float32) * scale
    scores = jnp.where(visible, raw, NEG)
    row_max = jnp.max(scores, axis=-1, keepdims=True)
    log_total = row_max + jnp.log(jnp.sum(jnp.exp(scores - row_max), axis=-1, keepdims=True))
    softmax_w = jnp.exp(scores - log_total)
    probs = softmax_w.astype(jnp.bfloat16)
    attention = jnp.einsum("bqk,kd->bqd", probs, v, preferred_element_type=jnp.float32).astype(
        jnp.bfloat16
    )
    row_dots = jnp.sum(
        gb.astype(jnp.float32) * attention.astype(jnp.float32), axis=-1, keepdims=True
    )
    grad_probs = jnp.einsum("bqd,kd->bqk", gb, v, preferred_element_type=jnp.float32)
    dscore = (softmax_w * (grad_probs - row_dots)).astype(jnp.bfloat16)
    grad_q = scale * jnp.einsum("bqk,kd->bqd", dscore, k, preferred_element_type=jnp.float32)
    grad_k = scale * jnp.einsum("bqk,bqd->kd", dscore, qb, preferred_element_type=jnp.float32)
    grad_v = jnp.einsum("bqk,bqd->kd", probs, gb, preferred_element_type=jnp.float32)
    return (
        attention.reshape(length, head_dim),
        grad_q.reshape(length, head_dim).astype(jnp.bfloat16),
        grad_k.astype(jnp.bfloat16),
        grad_v.astype(jnp.bfloat16),
    )


def ring_gather(block, ring, axis):
    n = len(ring)
    position = [0] * n
    for p, member in enumerate(ring):
        position[member] = p
    forward = [(ring[p], ring[(p + 1) % n]) for p in range(n)]
    backward = [(ring[p], ring[(p - 1) % n]) for p in range(n)]
    ring_arr = jnp.array(ring, jnp.int32)
    me = lax.axis_index(axis)
    p = jnp.array(position, jnp.int32)[me]
    out = jnp.zeros((n,) + block.shape, block.dtype)
    out = lax.dynamic_update_index_in_dim(out, block, me, 0)
    ahead, behind = block, block
    n_fwd = n // 2
    n_bwd = n - 1 - n_fwd
    for k in range(1, n_fwd + 1):
        ahead = lax.ppermute(ahead, axis, forward)
        out = lax.dynamic_update_index_in_dim(out, ahead, ring_arr[(p - k) % n], 0)
        if k <= n_bwd:
            behind = lax.ppermute(behind, axis, backward)
            out = lax.dynamic_update_index_in_dim(out, behind, ring_arr[(p + k) % n], 0)
    return out.reshape((n * block.shape[0],) + block.shape[1:])


def per_device(ring, query, keys, values, out_weight, grad_out, far_blocks, far_live):
    n_dp = lax.axis_size("dp")
    n_seq = lax.axis_size("seq")
    d_idx = lax.axis_index("dp")
    s_idx = lax.axis_index("seq")
    head_count = far_blocks.shape[1]
    per_dev = head_count // n_seq
    features = query.shape[2]
    head_dim = features // head_count
    width = per_dev * head_dim
    number = far_blocks.shape[2]

    stacked = jnp.stack([query[0], keys[0], values[0]])
    heads_qkv = lax.all_to_all(stacked, "seq", split_axis=2, concat_axis=1, tiled=True)
    length = heads_qkv.shape[1]
    block_rows = length // number

    weight = lax.all_gather(out_weight, "dp", axis=0, tiled=True)
    grad_doc = ring_gather(grad_out[0], ring, "seq")
    lower = s_idx * width
    weight_rows = lax.dynamic_slice_in_dim(weight, lower, width, 0)
    grad_heads = lax.dot_general(
        grad_doc, weight_rows, (((1,), (1,)), ((), ())), preferred_element_type=jnp.float32
    ).astype(jnp.bfloat16)

    head_start = s_idx * per_dev
    blocks_dev = lax.dynamic_slice_in_dim(far_blocks[0], head_start, per_dev, 0)
    live_dev = lax.dynamic_slice_in_dim(far_live[0], head_start, per_dev, 0)
    mask = block_mask(blocks_dev, live_dev)

    results = []
    for head in range(per_dev):
        cols = slice(head * head_dim, (head + 1) * head_dim)
        results.append(
            one_head(
                heads_qkv[0][:, cols],
                heads_qkv[1][:, cols],
                heads_qkv[2][:, cols],
                grad_heads[:, cols],
                mask[head],
                number,
            )
        )
    attn_heads = jnp.concatenate([r[0] for r in results], axis=1)
    attention = lax.all_to_all(attn_heads, "seq", split_axis=0, concat_axis=1, tiled=True)
    mixed = jnp.dot(attention, weight, preferred_element_type=jnp.float32).astype(jnp.bfloat16)[
        None
    ]
    back = [
        lax.all_to_all(
            jnp.concatenate([r[i] for r in results], axis=1),
            "seq",
            split_axis=0,
            concat_axis=1,
            tiled=True,
        )[None]
        for i in (1, 2, 3)
    ]

    norm_factor = (n_dp * query.shape[0] * length) ** (-0.5)
    partial = lax.dot_general(
        attn_heads, grad_doc, (((0,), (0,)), ((), ())), preferred_element_type=jnp.float32
    )
    reduced = lax.psum_scatter(partial * norm_factor, "dp", scatter_dimension=0, tiled=True)
    perm = []
    for d in range(n_dp):
        for s in range(n_seq):
            block = s * n_dp + d
            perm.append((d * n_seq + s, block))
    weight_grad = lax.ppermute(reduced, ("dp", "seq"), perm=perm)
    return (mixed, back[0], back[1], back[2], weight_grad)


def grid_cycle(rows, cols):
    cycle = [(r, 0) for r in range(rows)]
    for i, r in enumerate(range(rows - 1, -1, -1)):
        span = range(1, cols) if i % 2 == 0 else range(cols - 1, 0, -1)
        cycle.extend((r, c) for c in span)
    return cycle


def seq_ring(mesh):
    n_seq = mesh.shape["seq"]
    try:
        column = mesh.devices.reshape(-1, n_seq)[0]
        coords = [(d.coords[2], d.coords[0]) for d in column]
        zs = sorted({c[0] for c in coords})
        xs = sorted({c[1] for c in coords})
        where = {c: s for s, c in enumerate(coords)}
        if len(where) == n_seq and len(zs) * len(xs) == n_seq:
            if len(zs) % 2 == 0:
                cells = [(zs[r], xs[c]) for r, c in grid_cycle(len(zs), len(xs))]
            else:
                cells = [(zs[c], xs[r]) for r, c in grid_cycle(len(xs), len(zs))]
            order = [where[c] for c in cells]
            if sorted(order) == list(range(n_seq)):
                return tuple(order)
    except (AttributeError, IndexError, TypeError, KeyError):
        pass
    return tuple(range(n_seq))


def solution(mesh):
    ring = seq_ring(mesh)
    in_specs = (
        P("dp", "seq", None),
        P("dp", "seq", None),
        P("dp", "seq", None),
        P("dp", None),
        P("dp", "seq", None),
        P("dp", None, None, None),
        P("dp", None, None),
    )
    out_specs = (
        P("dp", "seq", None),
        P("dp", "seq", None),
        P("dp", "seq", None),
        P("dp", "seq", None),
        P(("dp", "seq"), None),
    )
    return jax.shard_map(
        functools.partial(per_device, ring), mesh=mesh, in_specs=in_specs, out_specs=out_specs, check_vma=False
    )
```

```python
import functools

import jax
import jax.numpy as jnp
from jax import lax
from jax.sharding import PartitionSpec as P

NEG = -1e30


def block_mask(blocks, live):
    number = blocks.shape[1]
    rows = jnp.arange(number, dtype=jnp.int32)[:, None]
    cols = jnp.arange(number, dtype=jnp.int32)[None, :]
    window = jnp.abs(rows - cols) <= 1
    far_pos = jnp.arange(blocks.shape[2], dtype=jnp.int32)
    far_used = far_pos[None, None, :] < live[:, :, None]
    hits = (blocks[:, :, :, None] == cols[None, None, :, :]) & far_used[:, :, :, None]
    return window[None] | jnp.any(hits, axis=2)


def one_head(q, k, v, g, mask, number):
    length, head_dim = q.shape
    rows = length // number
    scale = head_dim ** (-0.5)
    qb = q.reshape(number, rows, head_dim)
    gb = g.reshape(number, rows, head_dim)
    visible = jnp.repeat(mask, rows, axis=1)[:, None, :]
    raw = jnp.einsum("bqd,kd->bqk", qb, k, preferred_element_type=jnp.float32) * scale
    scores = jnp.where(visible, raw, NEG)
    row_max = jnp.max(scores, axis=-1, keepdims=True)
    log_total = row_max + jnp.log(jnp.sum(jnp.exp(scores - row_max), axis=-1, keepdims=True))
    softmax_w = jnp.exp(scores - log_total)
    probs = softmax_w.astype(jnp.bfloat16)
    attention = jnp.einsum("bqk,kd->bqd", probs, v, preferred_element_type=jnp.float32).astype(
        jnp.bfloat16
    )
    row_dots = jnp.sum(
        gb.astype(jnp.float32) * attention.astype(jnp.float32), axis=-1, keepdims=True
    )
    grad_probs = jnp.einsum("bqd,kd->bqk", gb, v, preferred_element_type=jnp.float32)
    dscore = (softmax_w * (grad_probs - row_dots)).astype(jnp.bfloat16)
    grad_q = scale * jnp.einsum("bqk,kd->bqd", dscore, k, preferred_element_type=jnp.float32)
    grad_k = scale * jnp.einsum("bqk,bqd->kd", dscore, qb, preferred_element_type=jnp.float32)
    grad_v = jnp.einsum("bqk,bqd->kd", probs, gb, preferred_element_type=jnp.float32)
    return (
        attention.reshape(length, head_dim),
        grad_q.reshape(length, head_dim).astype(jnp.bfloat16),
        grad_k.astype(jnp.bfloat16),
        grad_v.astype(jnp.bfloat16),
    )


def ring_gather(block, ring, axis):
    n = len(ring)
    position = [0] * n
    for p, member in enumerate(ring):
        position[member] = p
    forward = [(ring[p], ring[(p + 1) % n]) for p in range(n)]
    backward = [(ring[p], ring[(p - 1) % n]) for p in range(n)]
    ring_arr = jnp.array(ring, jnp.int32)
    me = lax.axis_index(axis)
    p = jnp.array(position, jnp.int32)[me]
    out = jnp.zeros((n,) + block.shape, block.dtype)
    out = lax.dynamic_update_index_in_dim(out, block, me, 0)
    ahead, behind = block, block
    n_fwd = n // 2
    n_bwd = n - 1 - n_fwd
    for k in range(1, n_fwd + 1):
        ahead = lax.ppermute(ahead, axis, forward)
        out = lax.dynamic_update_index_in_dim(out, ahead, ring_arr[(p - k) % n], 0)
        if k <= n_bwd:
            behind = lax.ppermute(behind, axis, backward)
            out = lax.dynamic_update_index_in_dim(out, behind, ring_arr[(p + k) % n], 0)
    return out.reshape((n * block.shape[0],) + block.shape[1:])


def per_device(ring, query, keys, values, out_weight, grad_out, far_blocks, far_live):
    n_dp = lax.axis_size("dp")
    n_seq = lax.axis_size("seq")
    d_idx = lax.axis_index("dp")
    s_idx = lax.axis_index("seq")
    head_count = far_blocks.shape[1]
    per_dev = head_count // n_seq
    features = query.shape[2]
    head_dim = features // head_count
    width = per_dev * head_dim
    number = far_blocks.shape[2]

    stacked = jnp.stack([query[0], keys[0], values[0]])
    heads_qkv = lax.all_to_all(stacked, "seq", split_axis=2, concat_axis=1, tiled=True)
    length = heads_qkv.shape[1]
    block_rows = length // number

    weight = lax.all_gather(out_weight, "dp", axis=0, tiled=True)
    grad_doc = ring_gather(grad_out[0], ring, "seq")
    lower = s_idx * width
    weight_rows = lax.dynamic_slice_in_dim(weight, lower, width, 0)
    grad_heads = lax.dot_general(
        grad_doc, weight_rows, (((1,), (1,)), ((), ())), preferred_element_type=jnp.float32
    ).astype(jnp.bfloat16)

    head_start = s_idx * per_dev
    blocks_dev = lax.dynamic_slice_in_dim(far_blocks[0], head_start, per_dev, 0)
    live_dev = lax.dynamic_slice_in_dim(far_live[0], head_start, per_dev, 0)
    mask = block_mask(blocks_dev, live_dev)

    results = []
    for head in range(per_dev):
        cols = slice(head * head_dim, (head + 1) * head_dim)
        results.append(
            one_head(
                heads_qkv[0][:, cols],
                heads_qkv[1][:, cols],
                heads_qkv[2][:, cols],
                grad_heads[:, cols],
                mask[head],
                number,
            )
        )
    attn_heads = jnp.concatenate([r[0] for r in results], axis=1)
    attention = lax.all_to_all(attn_heads, "seq", split_axis=0, concat_axis=1, tiled=True)
    grads = [jnp.concatenate([r[i] for r in results], axis=1) for i in (1, 2, 3)]
    attention, grads = lax.optimization_barrier((attention, grads))
    mixed = jnp.dot(attention, weight, preferred_element_type=jnp.float32).astype(jnp.bfloat16)[
        None
    ]
    back = [
        lax.all_to_all(g, "seq", split_axis=0, concat_axis=1, tiled=True)[None] for g in grads
    ]

    norm_factor = (n_dp * query.shape[0] * length) ** (-0.5)
    partial = lax.dot_general(
        attn_heads, grad_doc, (((0,), (0,)), ((), ())), preferred_element_type=jnp.float32
    )
    reduced = lax.psum_scatter(partial * norm_factor, "dp", scatter_dimension=0, tiled=True)
    perm = []
    for d in range(n_dp):
        for s in range(n_seq):
            block = s * n_dp + d
            perm.append((d * n_seq + s, block))
    weight_grad = lax.ppermute(reduced, ("dp", "seq"), perm=perm)
    return (mixed, back[0], back[1], back[2], weight_grad)


def grid_cycle(rows, cols):
    cycle = [(r, 0) for r in range(rows)]
    for i, r in enumerate(range(rows - 1, -1, -1)):
        span = range(1, cols) if i % 2 == 0 else range(cols - 1, 0, -1)
        cycle.extend((r, c) for c in span)
    return cycle


def seq_ring(mesh):
    n_seq = mesh.shape["seq"]
    try:
        column = mesh.devices.reshape(-1, n_seq)[0]
        coords = [(d.coords[2], d.coords[0]) for d in column]
        zs = sorted({c[0] for c in coords})
        xs = sorted({c[1] for c in coords})
        where = {c: s for s, c in enumerate(coords)}
        if len(where) == n_seq and len(zs) * len(xs) == n_seq:
            if len(zs) % 2 == 0:
                cells = [(zs[r], xs[c]) for r, c in grid_cycle(len(zs), len(xs))]
            else:
                cells = [(zs[c], xs[r]) for r, c in grid_cycle(len(xs), len(zs))]
            order = [where[c] for c in cells]
            if sorted(order) == list(range(n_seq)):
                return tuple(order)
    except (AttributeError, IndexError, TypeError, KeyError):
        pass
    return tuple(range(n_seq))


def solution(mesh):
    ring = seq_ring(mesh)
    in_specs = (
        P("dp", "seq", None),
        P("dp", "seq", None),
        P("dp", "seq", None),
        P("dp", None),
        P("dp", "seq", None),
        P("dp", None, None, None),
        P("dp", None, None),
    )
    out_specs = (
        P("dp", "seq", None),
        P("dp", "seq", None),
        P("dp", "seq", None),
        P("dp", "seq", None),
        P(("dp", "seq"), None),
    )
    return jax.shard_map(
        functools.partial(per_device, ring), mesh=mesh, in_specs=in_specs, out_specs=out_specs, check_vma=False
    )
```

```python
import functools

import jax
import jax.numpy as jnp
from jax import lax
from jax.sharding import PartitionSpec as P

NEG = -1e30


def block_mask(blocks, live):
    number = blocks.shape[1]
    rows = jnp.arange(number, dtype=jnp.int32)[:, None]
    cols = jnp.arange(number, dtype=jnp.int32)[None, :]
    window = jnp.abs(rows - cols) <= 1
    far_pos = jnp.arange(blocks.shape[2], dtype=jnp.int32)
    far_used = far_pos[None, None, :] < live[:, :, None]
    hits = (blocks[:, :, :, None] == cols[None, None, :, :]) & far_used[:, :, :, None]
    return window[None] | jnp.any(hits, axis=2)


def one_head(q, k, v, g, mask, number):
    length, head_dim = q.shape
    rows = length // number
    scale = head_dim ** (-0.5)
    qb = q.reshape(number, rows, head_dim)
    gb = g.reshape(number, rows, head_dim)
    visible = jnp.repeat(mask, rows, axis=1)[:, None, :]
    raw = jnp.einsum("bqd,kd->bqk", qb, k, preferred_element_type=jnp.float32) * scale
    scores = jnp.where(visible, raw, NEG)
    row_max = jnp.max(scores, axis=-1, keepdims=True)
    log_total = row_max + jnp.log(jnp.sum(jnp.exp(scores - row_max), axis=-1, keepdims=True))
    softmax_w = jnp.exp(scores - log_total)
    probs = softmax_w.astype(jnp.bfloat16)
    attention = jnp.einsum("bqk,kd->bqd", probs, v, preferred_element_type=jnp.float32).astype(
        jnp.bfloat16
    )
    row_dots = jnp.sum(
        gb.astype(jnp.float32) * attention.astype(jnp.float32), axis=-1, keepdims=True
    )
    grad_probs = jnp.einsum("bqd,kd->bqk", gb, v, preferred_element_type=jnp.float32)
    dscore = (softmax_w * (grad_probs - row_dots)).astype(jnp.bfloat16)
    grad_q = scale * jnp.einsum("bqk,kd->bqd", dscore, k, preferred_element_type=jnp.float32)
    grad_k = scale * jnp.einsum("bqk,bqd->kd", dscore, qb, preferred_element_type=jnp.float32)
    grad_v = jnp.einsum("bqk,bqd->kd", probs, gb, preferred_element_type=jnp.float32)
    return (
        attention.reshape(length, head_dim),
        grad_q.reshape(length, head_dim).astype(jnp.bfloat16),
        grad_k.astype(jnp.bfloat16),
        grad_v.astype(jnp.bfloat16),
    )


def ring_gather(block, ring, axis):
    n = len(ring)
    position = [0] * n
    for p, member in enumerate(ring):
        position[member] = p
    forward = [(ring[p], ring[(p + 1) % n]) for p in range(n)]
    backward = [(ring[p], ring[(p - 1) % n]) for p in range(n)]
    ring_arr = jnp.array(ring, jnp.int32)
    me = lax.axis_index(axis)
    p = jnp.array(position, jnp.int32)[me]
    out = jnp.zeros((n,) + block.shape, block.dtype)
    out = lax.dynamic_update_index_in_dim(out, block, me, 0)
    ahead, behind = block, block
    n_fwd = n // 2
    n_bwd = n - 1 - n_fwd
    for k in range(1, n_fwd + 1):
        ahead = lax.ppermute(ahead, axis, forward)
        out = lax.dynamic_update_index_in_dim(out, ahead, ring_arr[(p - k) % n], 0)
        if k <= n_bwd:
            behind = lax.ppermute(behind, axis, backward)
            out = lax.dynamic_update_index_in_dim(out, behind, ring_arr[(p + k) % n], 0)
    return out.reshape((n * block.shape[0],) + block.shape[1:])


def per_device(ring, query, keys, values, out_weight, grad_out, far_blocks, far_live):
    n_dp = lax.axis_size("dp")
    n_seq = lax.axis_size("seq")
    d_idx = lax.axis_index("dp")
    s_idx = lax.axis_index("seq")
    head_count = far_blocks.shape[1]
    per_dev = head_count // n_seq
    features = query.shape[2]
    head_dim = features // head_count
    width = per_dev * head_dim
    number = far_blocks.shape[2]

    stacked = jnp.stack([query[0], keys[0], values[0]])
    heads_qkv = lax.all_to_all(stacked, "seq", split_axis=2, concat_axis=1, tiled=True)
    length = heads_qkv.shape[1]
    block_rows = length // number

    weight = lax.all_gather(out_weight, "dp", axis=0, tiled=True)
    grad_doc = ring_gather(grad_out[0], ring, "seq")
    lower = s_idx * width
    weight_rows = lax.dynamic_slice_in_dim(weight, lower, width, 0)
    grad_heads = lax.dot_general(
        grad_doc, weight_rows, (((1,), (1,)), ((), ())), preferred_element_type=jnp.float32
    ).astype(jnp.bfloat16)

    head_start = s_idx * per_dev
    blocks_dev = lax.dynamic_slice_in_dim(far_blocks[0], head_start, per_dev, 0)
    live_dev = lax.dynamic_slice_in_dim(far_live[0], head_start, per_dev, 0)
    mask = block_mask(blocks_dev, live_dev)

    results = []
    for head in range(per_dev):
        cols = slice(head * head_dim, (head + 1) * head_dim)
        results.append(
            one_head(
                heads_qkv[0][:, cols],
                heads_qkv[1][:, cols],
                heads_qkv[2][:, cols],
                grad_heads[:, cols],
                mask[head],
                number,
            )
        )
    attn_heads = jnp.concatenate([r[0] for r in results], axis=1)
    arrived = [
        lax.all_to_all(jnp.stack(r), "seq", split_axis=1, concat_axis=2, tiled=True)
        for r in results
    ]
    tokens = arrived[0].shape[1]
    weight_parts = weight.reshape(n_seq, per_dev, head_dim, weight.shape[1])
    mixed_sum = None
    for head in range(per_dev):
        part = jnp.dot(
            arrived[head][0],
            weight_parts[:, head].reshape(n_seq * head_dim, weight.shape[1]),
            preferred_element_type=jnp.float32,
        )
        mixed_sum = part if mixed_sum is None else mixed_sum + part
    mixed = mixed_sum.astype(jnp.bfloat16)[None]
    joined = jnp.stack(
        [a.reshape(4, tokens, n_seq, head_dim) for a in arrived], axis=3
    ).reshape(4, tokens, features)
    back = [joined[i][None] for i in (1, 2, 3)]

    norm_factor = (n_dp * query.shape[0] * length) ** (-0.5)
    partial = lax.dot_general(
        attn_heads, grad_doc, (((0,), (0,)), ((), ())), preferred_element_type=jnp.float32
    )
    reduced = lax.psum_scatter(partial * norm_factor, "dp", scatter_dimension=0, tiled=True)
    perm = []
    for d in range(n_dp):
        for s in range(n_seq):
            block = s * n_dp + d
            perm.append((d * n_seq + s, block))
    weight_grad = lax.ppermute(reduced, ("dp", "seq"), perm=perm)
    return (mixed, back[0], back[1], back[2], weight_grad)


def grid_cycle(rows, cols):
    cycle = [(r, 0) for r in range(rows)]
    for i, r in enumerate(range(rows - 1, -1, -1)):
        span = range(1, cols) if i % 2 == 0 else range(cols - 1, 0, -1)
        cycle.extend((r, c) for c in span)
    return cycle


def seq_ring(mesh):
    n_seq = mesh.shape["seq"]
    try:
        column = mesh.devices.reshape(-1, n_seq)[0]
        coords = [(d.coords[2], d.coords[0]) for d in column]
        zs = sorted({c[0] for c in coords})
        xs = sorted({c[1] for c in coords})
        where = {c: s for s, c in enumerate(coords)}
        if len(where) == n_seq and len(zs) * len(xs) == n_seq:
            if len(zs) % 2 == 0:
                cells = [(zs[r], xs[c]) for r, c in grid_cycle(len(zs), len(xs))]
            else:
                cells = [(zs[c], xs[r]) for r, c in grid_cycle(len(xs), len(zs))]
            order = [where[c] for c in cells]
            if sorted(order) == list(range(n_seq)):
                return tuple(order)
    except (AttributeError, IndexError, TypeError, KeyError):
        pass
    return tuple(range(n_seq))


def solution(mesh):
    ring = seq_ring(mesh)
    in_specs = (
        P("dp", "seq", None),
        P("dp", "seq", None),
        P("dp", "seq", None),
        P("dp", None),
        P("dp", "seq", None),
        P("dp", None, None, None),
        P("dp", None, None),
    )
    out_specs = (
        P("dp", "seq", None),
        P("dp", "seq", None),
        P("dp", "seq", None),
        P("dp", "seq", None),
        P(("dp", "seq"), None),
    )
    return jax.shard_map(
        functools.partial(per_device, ring), mesh=mesh, in_specs=in_specs, out_specs=out_specs, check_vma=False
    )
```

```python
import functools

import jax
import jax.numpy as jnp
from jax import lax
from jax.sharding import PartitionSpec as P

NEG = -1e30


def block_mask(blocks, live):
    number = blocks.shape[1]
    rows = jnp.arange(number, dtype=jnp.int32)[:, None]
    cols = jnp.arange(number, dtype=jnp.int32)[None, :]
    window = jnp.abs(rows - cols) <= 1
    far_pos = jnp.arange(blocks.shape[2], dtype=jnp.int32)
    far_used = far_pos[None, None, :] < live[:, :, None]
    hits = (blocks[:, :, :, None] == cols[None, None, :, :]) & far_used[:, :, :, None]
    return window[None] | jnp.any(hits, axis=2)


def one_head(q, k, v, g, mask, number):
    length, head_dim = q.shape
    rows = length // number
    scale = head_dim ** (-0.5)
    qb = q.reshape(number, rows, head_dim)
    gb = g.reshape(number, rows, head_dim)
    visible = jnp.repeat(mask, rows, axis=1)[:, None, :]
    raw = jnp.einsum("bqd,kd->bqk", qb, k, preferred_element_type=jnp.float32) * scale
    scores = jnp.where(visible, raw, NEG)
    row_max = jnp.max(scores, axis=-1, keepdims=True)
    log_total = row_max + jnp.log(jnp.sum(jnp.exp(scores - row_max), axis=-1, keepdims=True))
    softmax_w = jnp.exp(scores - log_total)
    probs = softmax_w.astype(jnp.bfloat16)
    attention = jnp.einsum("bqk,kd->bqd", probs, v, preferred_element_type=jnp.float32).astype(
        jnp.bfloat16
    )
    row_dots = jnp.sum(
        gb.astype(jnp.float32) * attention.astype(jnp.float32), axis=-1, keepdims=True
    )
    grad_probs = jnp.einsum("bqd,kd->bqk", gb, v, preferred_element_type=jnp.float32)
    dscore = (softmax_w * (grad_probs - row_dots)).astype(jnp.bfloat16)
    grad_q = scale * jnp.einsum("bqk,kd->bqd", dscore, k, preferred_element_type=jnp.float32)
    grad_k = scale * jnp.einsum("bqk,bqd->kd", dscore, qb, preferred_element_type=jnp.float32)
    grad_v = jnp.einsum("bqk,bqd->kd", probs, gb, preferred_element_type=jnp.float32)
    return (
        attention.reshape(length, head_dim),
        grad_q.reshape(length, head_dim).astype(jnp.bfloat16),
        grad_k.astype(jnp.bfloat16),
        grad_v.astype(jnp.bfloat16),
    )


def ring_gather(block, ring, axis):
    n = len(ring)
    position = [0] * n
    for p, member in enumerate(ring):
        position[member] = p
    forward = [(ring[p], ring[(p + 1) % n]) for p in range(n)]
    backward = [(ring[p], ring[(p - 1) % n]) for p in range(n)]
    ring_arr = jnp.array(ring, jnp.int32)
    me = lax.axis_index(axis)
    p = jnp.array(position, jnp.int32)[me]
    out = jnp.zeros((n,) + block.shape, block.dtype)
    out = lax.dynamic_update_index_in_dim(out, block, me, 0)
    ahead, behind = block, block
    n_fwd = n // 2
    n_bwd = n - 1 - n_fwd
    for k in range(1, n_fwd + 1):
        ahead = lax.ppermute(ahead, axis, forward)
        out = lax.dynamic_update_index_in_dim(out, ahead, ring_arr[(p - k) % n], 0)
        if k <= n_bwd:
            behind = lax.ppermute(behind, axis, backward)
            out = lax.dynamic_update_index_in_dim(out, behind, ring_arr[(p + k) % n], 0)
    return out.reshape((n * block.shape[0],) + block.shape[1:])


def head_plan(n_dp, n_seq, head_count, head_dim, features):
    per_dev = head_count // n_seq
    rows = features // (n_dp * n_seq)
    group = head_dim // rows if rows and head_dim % rows == 0 else 0
    if group and n_seq % group == 0 and n_dp == group * per_dev:
        stride = n_seq // group
        plan = [
            [stride * ((s % group) * per_dev + j) + s // group for j in range(per_dev)]
            for s in range(n_seq)
        ]
        return plan, group, rows
    return [[s * per_dev + j for j in range(per_dev)] for s in range(n_seq)], 0, rows


def per_device(ring, query, keys, values, out_weight, grad_out, far_blocks, far_live):
    n_dp = lax.axis_size("dp")
    n_seq = lax.axis_size("seq")
    s_idx = lax.axis_index("seq")
    head_count = far_blocks.shape[1]
    per_dev = head_count // n_seq
    features = query.shape[2]
    head_dim = features // head_count
    number = far_blocks.shape[2]
    plan, group, rows = head_plan(n_dp, n_seq, head_count, head_dim, features)
    order = [h for heads in plan for h in heads]
    plan_arr = jnp.array(plan, jnp.int32)
    my_heads = plan_arr[s_idx]

    stacked = jnp.stack([query[0], keys[0], values[0]])
    tokens = stacked.shape[1]
    by_head = stacked.reshape(3, tokens, head_count, head_dim)
    stacked = jnp.stack([by_head[:, :, h] for h in order], axis=2).reshape(3, tokens, features)
    heads_qkv = lax.all_to_all(stacked, "seq", split_axis=2, concat_axis=1, tiled=True)
    length = heads_qkv.shape[1]

    weight = lax.all_gather(out_weight, "dp", axis=0, tiled=True)
    weight_heads = weight.reshape(head_count, head_dim, weight.shape[1])
    grad_doc = ring_gather(grad_out[0], ring, "seq")
    weight_rows = jnp.concatenate(
        [lax.dynamic_index_in_dim(weight_heads, my_heads[j], 0, False) for j in range(per_dev)]
    )
    grad_heads = lax.dot_general(
        grad_doc, weight_rows, (((1,), (1,)), ((), ())), preferred_element_type=jnp.float32
    ).astype(jnp.bfloat16)

    blocks_dev = jnp.stack(
        [lax.dynamic_index_in_dim(far_blocks[0], my_heads[j], 0, False) for j in range(per_dev)]
    )
    live_dev = jnp.stack(
        [lax.dynamic_index_in_dim(far_live[0], my_heads[j], 0, False) for j in range(per_dev)]
    )
    mask = block_mask(blocks_dev, live_dev)

    results = []
    for head in range(per_dev):
        cols = slice(head * head_dim, (head + 1) * head_dim)
        results.append(
            one_head(
                heads_qkv[0][:, cols],
                heads_qkv[1][:, cols],
                heads_qkv[2][:, cols],
                grad_heads[:, cols],
                mask[head],
                number,
            )
        )
    attn_heads = jnp.stack([r[0] for r in results], axis=1)
    arrived = [
        lax.all_to_all(jnp.stack(r), "seq", split_axis=1, concat_axis=2, tiled=True)
        for r in results
    ]
    pieces = [a.reshape(4, tokens, n_seq, head_dim) for a in arrived]
    where = {}
    for s, heads in enumerate(plan):
        for j, h in enumerate(heads):
            where[h] = (s, j)
    joined = jnp.concatenate(
        [pieces[where[h][1]][:, :, where[h][0]] for h in range(head_count)], axis=2
    )
    mixed = jnp.dot(joined[0], weight, preferred_element_type=jnp.float32).astype(jnp.bfloat16)[
        None
    ]
    back = [joined[i][None] for i in (1, 2, 3)]

    norm_factor = (n_dp * query.shape[0] * length) ** (-0.5)
    if group:
        me = s_idx % group
        sub = attn_heads.reshape(length, per_dev, group, rows)
        slots = jnp.zeros((length, group, per_dev, rows), attn_heads.dtype)
        slots = lax.dynamic_update_index_in_dim(
            slots, lax.dynamic_index_in_dim(sub, me, 2, False), me, 1
        )
        for shift in range(1, group):
            perm = [
                (base + i, base + (i + shift) % group)
                for base in range(0, n_seq, group)
                for i in range(group)
            ]
            target = (me + shift) % group
            sent = lax.dynamic_index_in_dim(sub, target, 2, False)
            got = lax.ppermute(sent, "seq", perm)
            source = (me - shift) % group
            slots = lax.dynamic_update_index_in_dim(slots, got, source, 1)
        mine = slots.reshape(length, n_dp * rows)
        partial = lax.dot_general(
            mine, grad_doc, (((0,), (0,)), ((), ())), preferred_element_type=jnp.float32
        )
        weight_grad = lax.psum_scatter(
            partial * norm_factor, "dp", scatter_dimension=0, tiled=True
        )
    else:
        partial = lax.dot_general(
            attn_heads.reshape(length, per_dev * head_dim),
            grad_doc,
            (((0,), (0,)), ((), ())),
            preferred_element_type=jnp.float32,
        )
        reduced = lax.psum_scatter(partial * norm_factor, "dp", scatter_dimension=0, tiled=True)
        perm = []
        for d in range(n_dp):
            for s in range(n_seq):
                perm.append((d * n_seq + s, s * n_dp + d))
        weight_grad = lax.ppermute(reduced, ("dp", "seq"), perm=perm)
    return (mixed, back[0], back[1], back[2], weight_grad)


def grid_cycle(rows, cols):
    cycle = [(r, 0) for r in range(rows)]
    for i, r in enumerate(range(rows - 1, -1, -1)):
        span = range(1, cols) if i % 2 == 0 else range(cols - 1, 0, -1)
        cycle.extend((r, c) for c in span)
    return cycle


def seq_ring(mesh):
    n_seq = mesh.shape["seq"]
    try:
        column = mesh.devices.reshape(-1, n_seq)[0]
        coords = [(d.coords[2], d.coords[0]) for d in column]
        zs = sorted({c[0] for c in coords})
        xs = sorted({c[1] for c in coords})
        where = {c: s for s, c in enumerate(coords)}
        if len(where) == n_seq and len(zs) * len(xs) == n_seq:
            if len(zs) % 2 == 0:
                cells = [(zs[r], xs[c]) for r, c in grid_cycle(len(zs), len(xs))]
            else:
                cells = [(zs[c], xs[r]) for r, c in grid_cycle(len(xs), len(zs))]
            order = [where[c] for c in cells]
            if sorted(order) == list(range(n_seq)):
                return tuple(order)
    except (AttributeError, IndexError, TypeError, KeyError):
        pass
    return tuple(range(n_seq))


def solution(mesh):
    ring = seq_ring(mesh)
    in_specs = (
        P("dp", "seq", None),
        P("dp", "seq", None),
        P("dp", "seq", None),
        P("dp", None),
        P("dp", "seq", None),
        P("dp", None, None, None),
        P("dp", None, None),
    )
    out_specs = (
        P("dp", "seq", None),
        P("dp", "seq", None),
        P("dp", "seq", None),
        P("dp", "seq", None),
        P(("dp", "seq"), None),
    )
    return jax.shard_map(
        functools.partial(per_device, ring), mesh=mesh, in_specs=in_specs, out_specs=out_specs, check_vma=False
    )
```

```python
import functools

import jax
import jax.numpy as jnp
from jax import lax
from jax.sharding import PartitionSpec as P

NEG = -1e30


def block_mask(blocks, live):
    number = blocks.shape[1]
    rows = jnp.arange(number, dtype=jnp.int32)[:, None]
    cols = jnp.arange(number, dtype=jnp.int32)[None, :]
    window = jnp.abs(rows - cols) <= 1
    far_pos = jnp.arange(blocks.shape[2], dtype=jnp.int32)
    far_used = far_pos[None, None, :] < live[:, :, None]
    hits = (blocks[:, :, :, None] == cols[None, None, :, :]) & far_used[:, :, :, None]
    return window[None] | jnp.any(hits, axis=2)


def head_forward(q, k, v, mask, number):
    length, head_dim = q.shape
    rows = length // number
    scale = head_dim ** (-0.5)
    qb = q.reshape(number, rows, head_dim)
    visible = jnp.repeat(mask, rows, axis=1)[:, None, :]
    raw = jnp.einsum("bqd,kd->bqk", qb, k, preferred_element_type=jnp.float32) * scale
    scores = jnp.where(visible, raw, NEG)
    row_max = jnp.max(scores, axis=-1, keepdims=True)
    log_total = row_max + jnp.log(jnp.sum(jnp.exp(scores - row_max), axis=-1, keepdims=True))
    softmax_w = jnp.exp(scores - log_total)
    probs = softmax_w.astype(jnp.bfloat16)
    attention = jnp.einsum("bqk,kd->bqd", probs, v, preferred_element_type=jnp.float32).astype(
        jnp.bfloat16
    )
    return softmax_w, attention


def head_backward(q, k, v, g, softmax_w, attention, number):
    length, head_dim = q.shape
    rows = length // number
    scale = head_dim ** (-0.5)
    qb = q.reshape(number, rows, head_dim)
    gb = g.reshape(number, rows, head_dim)
    probs = softmax_w.astype(jnp.bfloat16)
    row_dots = jnp.sum(
        gb.astype(jnp.float32) * attention.astype(jnp.float32), axis=-1, keepdims=True
    )
    grad_probs = jnp.einsum("bqd,kd->bqk", gb, v, preferred_element_type=jnp.float32)
    dscore = (softmax_w * (grad_probs - row_dots)).astype(jnp.bfloat16)
    grad_q = scale * jnp.einsum("bqk,kd->bqd", dscore, k, preferred_element_type=jnp.float32)
    grad_k = scale * jnp.einsum("bqk,bqd->kd", dscore, qb, preferred_element_type=jnp.float32)
    grad_v = jnp.einsum("bqk,bqd->kd", probs, gb, preferred_element_type=jnp.float32)
    return (
        attention.reshape(length, head_dim),
        grad_q.reshape(length, head_dim).astype(jnp.bfloat16),
        grad_k.astype(jnp.bfloat16),
        grad_v.astype(jnp.bfloat16),
    )


def ring_gather(block, ring, axis):
    n = len(ring)
    position = [0] * n
    for p, member in enumerate(ring):
        position[member] = p
    forward = [(ring[p], ring[(p + 1) % n]) for p in range(n)]
    backward = [(ring[p], ring[(p - 1) % n]) for p in range(n)]
    ring_arr = jnp.array(ring, jnp.int32)
    me = lax.axis_index(axis)
    p = jnp.array(position, jnp.int32)[me]
    out = jnp.zeros((n,) + block.shape, block.dtype)
    out = lax.dynamic_update_index_in_dim(out, block, me, 0)
    ahead, behind = block, block
    n_fwd = n // 2
    n_bwd = n - 1 - n_fwd
    for k in range(1, n_fwd + 1):
        ahead = lax.ppermute(ahead, axis, forward)
        out = lax.dynamic_update_index_in_dim(out, ahead, ring_arr[(p - k) % n], 0)
        if k <= n_bwd:
            behind = lax.ppermute(behind, axis, backward)
            out = lax.dynamic_update_index_in_dim(out, behind, ring_arr[(p + k) % n], 0)
    return out.reshape((n * block.shape[0],) + block.shape[1:])


def head_plan(n_dp, n_seq, head_count, head_dim, features):
    per_dev = head_count // n_seq
    rows = features // (n_dp * n_seq)
    group = head_dim // rows if rows and head_dim % rows == 0 else 0
    if group and n_seq % group == 0 and n_dp == group * per_dev:
        stride = n_seq // group
        plan = [
            [stride * ((s % group) * per_dev + j) + s // group for j in range(per_dev)]
            for s in range(n_seq)
        ]
        return plan, group, rows
    return [[s * per_dev + j for j in range(per_dev)] for s in range(n_seq)], 0, rows


def per_device(ring, query, keys, values, out_weight, grad_out, far_blocks, far_live):
    n_dp = lax.axis_size("dp")
    n_seq = lax.axis_size("seq")
    s_idx = lax.axis_index("seq")
    head_count = far_blocks.shape[1]
    per_dev = head_count // n_seq
    features = query.shape[2]
    head_dim = features // head_count
    number = far_blocks.shape[2]
    plan, group, rows = head_plan(n_dp, n_seq, head_count, head_dim, features)
    order = [h for heads in plan for h in heads]
    plan_arr = jnp.array(plan, jnp.int32)
    my_heads = plan_arr[s_idx]

    stacked = jnp.stack([query[0], keys[0], values[0]])
    tokens = stacked.shape[1]
    by_head = stacked.reshape(3, tokens, head_count, head_dim)
    stacked = jnp.stack([by_head[:, :, h] for h in order], axis=2).reshape(3, tokens, features)
    heads_qkv = lax.all_to_all(stacked, "seq", split_axis=2, concat_axis=1, tiled=True)
    length = heads_qkv.shape[1]

    weight = lax.all_gather(out_weight, "dp", axis=0, tiled=True)
    weight_heads = weight.reshape(head_count, head_dim, weight.shape[1])
    grad_doc = ring_gather(grad_out[0], ring, "seq")
    weight_rows = jnp.concatenate(
        [lax.dynamic_index_in_dim(weight_heads, my_heads[j], 0, False) for j in range(per_dev)]
    )
    grad_heads = lax.dot_general(
        grad_doc, weight_rows, (((1,), (1,)), ((), ())), preferred_element_type=jnp.float32
    ).astype(jnp.bfloat16)

    blocks_dev = jnp.stack(
        [lax.dynamic_index_in_dim(far_blocks[0], my_heads[j], 0, False) for j in range(per_dev)]
    )
    live_dev = jnp.stack(
        [lax.dynamic_index_in_dim(far_live[0], my_heads[j], 0, False) for j in range(per_dev)]
    )
    mask = block_mask(blocks_dev, live_dev)

    def head_cols(array, head):
        return array[:, head * head_dim : (head + 1) * head_dim]

    forward = [
        head_forward(
            head_cols(heads_qkv[0], j), head_cols(heads_qkv[1], j), head_cols(heads_qkv[2], j),
            mask[j], number,
        )
        for j in range(per_dev)
    ]
    attn_heads = jnp.stack([f[1].reshape(length, head_dim) for f in forward], axis=1)

    norm_factor = (n_dp * query.shape[0] * length) ** (-0.5)
    if group:
        me = s_idx % group
        sub = attn_heads.reshape(length, per_dev, group, rows)
        slots = jnp.zeros((length, group, per_dev, rows), attn_heads.dtype)
        slots = lax.dynamic_update_index_in_dim(
            slots, lax.dynamic_index_in_dim(sub, me, 2, False), me, 1
        )
        for shift in range(1, group):
            perm = [
                (base + i, base + (i + shift) % group)
                for base in range(0, n_seq, group)
                for i in range(group)
            ]
            target = (me + shift) % group
            sent = lax.dynamic_index_in_dim(sub, target, 2, False)
            got = lax.ppermute(sent, "seq", perm)
            source = (me - shift) % group
            slots = lax.dynamic_update_index_in_dim(slots, got, source, 1)
        mine = slots.reshape(length, n_dp * rows)
        partial = lax.dot_general(
            mine, grad_doc, (((0,), (0,)), ((), ())), preferred_element_type=jnp.float32
        )

        def weight_grad_of(partial):
            return lax.psum_scatter(partial * norm_factor, "dp", scatter_dimension=0, tiled=True)
    else:
        partial = lax.dot_general(
            attn_heads.reshape(length, per_dev * head_dim),
            grad_doc,
            (((0,), (0,)), ((), ())),
            preferred_element_type=jnp.float32,
        )

        def weight_grad_of(partial):
            reduced = lax.psum_scatter(
                partial * norm_factor, "dp", scatter_dimension=0, tiled=True
            )
            perm = []
            for d in range(n_dp):
                for s in range(n_seq):
                    perm.append((d * n_seq + s, s * n_dp + d))
            return lax.ppermute(reduced, ("dp", "seq"), perm=perm)
    partial, grad_heads = lax.optimization_barrier((partial, grad_heads))
    weight_grad = weight_grad_of(partial)

    results = [
        head_backward(
            head_cols(heads_qkv[0], j), head_cols(heads_qkv[1], j), head_cols(heads_qkv[2], j),
            head_cols(grad_heads, j), forward[j][0], forward[j][1], number,
        )
        for j in range(per_dev)
    ]
    arrived = [
        lax.all_to_all(jnp.stack(r), "seq", split_axis=1, concat_axis=2, tiled=True)
        for r in results
    ]
    pieces = [a.reshape(4, tokens, n_seq, head_dim) for a in arrived]
    where = {}
    for s, heads in enumerate(plan):
        for j, h in enumerate(heads):
            where[h] = (s, j)
    joined = jnp.concatenate(
        [pieces[where[h][1]][:, :, where[h][0]] for h in range(head_count)], axis=2
    )
    mixed = jnp.dot(joined[0], weight, preferred_element_type=jnp.float32).astype(jnp.bfloat16)[
        None
    ]
    back = [joined[i][None] for i in (1, 2, 3)]
    return (mixed, back[0], back[1], back[2], weight_grad)


def grid_cycle(rows, cols):
    cycle = [(r, 0) for r in range(rows)]
    for i, r in enumerate(range(rows - 1, -1, -1)):
        span = range(1, cols) if i % 2 == 0 else range(cols - 1, 0, -1)
        cycle.extend((r, c) for c in span)
    return cycle


def seq_ring(mesh):
    n_seq = mesh.shape["seq"]
    try:
        column = mesh.devices.reshape(-1, n_seq)[0]
        coords = [(d.coords[2], d.coords[0]) for d in column]
        zs = sorted({c[0] for c in coords})
        xs = sorted({c[1] for c in coords})
        where = {c: s for s, c in enumerate(coords)}
        if len(where) == n_seq and len(zs) * len(xs) == n_seq:
            if len(zs) % 2 == 0:
                cells = [(zs[r], xs[c]) for r, c in grid_cycle(len(zs), len(xs))]
            else:
                cells = [(zs[c], xs[r]) for r, c in grid_cycle(len(xs), len(zs))]
            order = [where[c] for c in cells]
            if sorted(order) == list(range(n_seq)):
                return tuple(order)
    except (AttributeError, IndexError, TypeError, KeyError):
        pass
    return tuple(range(n_seq))


def solution(mesh):
    ring = seq_ring(mesh)
    in_specs = (
        P("dp", "seq", None),
        P("dp", "seq", None),
        P("dp", "seq", None),
        P("dp", None),
        P("dp", "seq", None),
        P("dp", None, None, None),
        P("dp", None, None),
    )
    out_specs = (
        P("dp", "seq", None),
        P("dp", "seq", None),
        P("dp", "seq", None),
        P("dp", "seq", None),
        P(("dp", "seq"), None),
    )
    return jax.shard_map(
        functools.partial(per_device, ring), mesh=mesh, in_specs=in_specs, out_specs=out_specs, check_vma=False
    )
```

```python
import functools

import jax
import jax.numpy as jnp
from jax import lax
from jax.sharding import PartitionSpec as P

NEG = -1e30


def block_mask(blocks, live):
    number = blocks.shape[1]
    rows = jnp.arange(number, dtype=jnp.int32)[:, None]
    cols = jnp.arange(number, dtype=jnp.int32)[None, :]
    window = jnp.abs(rows - cols) <= 1
    far_pos = jnp.arange(blocks.shape[2], dtype=jnp.int32)
    far_used = far_pos[None, None, :] < live[:, :, None]
    hits = (blocks[:, :, :, None] == cols[None, None, :, :]) & far_used[:, :, :, None]
    return window[None] | jnp.any(hits, axis=2)


def head_forward(q, k, v, mask, number):
    length, head_dim = q.shape
    rows = length // number
    scale = head_dim ** (-0.5)
    qb = q.reshape(number, rows, head_dim)
    visible = jnp.repeat(mask, rows, axis=1)[:, None, :]
    raw = jnp.einsum("bqd,kd->bqk", qb, k, preferred_element_type=jnp.float32) * scale
    scores = jnp.where(visible, raw, NEG)
    row_max = jnp.max(scores, axis=-1, keepdims=True)
    log_total = row_max + jnp.log(jnp.sum(jnp.exp(scores - row_max), axis=-1, keepdims=True))
    softmax_w = jnp.exp(scores - log_total)
    probs = softmax_w.astype(jnp.bfloat16)
    attention = jnp.einsum("bqk,kd->bqd", probs, v, preferred_element_type=jnp.float32).astype(
        jnp.bfloat16
    )
    return softmax_w, attention


def head_backward(q, k, v, g, softmax_w, attention, number):
    length, head_dim = q.shape
    rows = length // number
    scale = head_dim ** (-0.5)
    qb = q.reshape(number, rows, head_dim)
    gb = g.reshape(number, rows, head_dim)
    probs = softmax_w.astype(jnp.bfloat16)
    row_dots = jnp.sum(
        gb.astype(jnp.float32) * attention.astype(jnp.float32), axis=-1, keepdims=True
    )
    grad_probs = jnp.einsum("bqd,kd->bqk", gb, v, preferred_element_type=jnp.float32)
    dscore = (softmax_w * (grad_probs - row_dots)).astype(jnp.bfloat16)
    grad_q = scale * jnp.einsum("bqk,kd->bqd", dscore, k, preferred_element_type=jnp.float32)
    grad_k = scale * jnp.einsum("bqk,bqd->kd", dscore, qb, preferred_element_type=jnp.float32)
    grad_v = jnp.einsum("bqk,bqd->kd", probs, gb, preferred_element_type=jnp.float32)
    return (
        attention.reshape(length, head_dim),
        grad_q.reshape(length, head_dim).astype(jnp.bfloat16),
        grad_k.astype(jnp.bfloat16),
        grad_v.astype(jnp.bfloat16),
    )


def ring_gather(block, ring, axis):
    n = len(ring)
    position = [0] * n
    for p, member in enumerate(ring):
        position[member] = p
    forward = [(ring[p], ring[(p + 1) % n]) for p in range(n)]
    backward = [(ring[p], ring[(p - 1) % n]) for p in range(n)]
    ring_arr = jnp.array(ring, jnp.int32)
    me = lax.axis_index(axis)
    p = jnp.array(position, jnp.int32)[me]
    out = jnp.zeros((n,) + block.shape, block.dtype)
    out = lax.dynamic_update_index_in_dim(out, block, me, 0)
    ahead, behind = block, block
    n_fwd = n // 2
    n_bwd = n - 1 - n_fwd
    for k in range(1, n_fwd + 1):
        ahead = lax.ppermute(ahead, axis, forward)
        out = lax.dynamic_update_index_in_dim(out, ahead, ring_arr[(p - k) % n], 0)
        if k <= n_bwd:
            behind = lax.ppermute(behind, axis, backward)
            out = lax.dynamic_update_index_in_dim(out, behind, ring_arr[(p + k) % n], 0)
    return out.reshape((n * block.shape[0],) + block.shape[1:])


def head_plan(n_dp, n_seq, head_count, head_dim, features):
    per_dev = head_count // n_seq
    rows = features // (n_dp * n_seq)
    group = head_dim // rows if rows and head_dim % rows == 0 else 0
    if group and n_seq % group == 0 and n_dp == group * per_dev:
        stride = n_seq // group
        plan = [
            [stride * ((s % group) * per_dev + j) + s // group for j in range(per_dev)]
            for s in range(n_seq)
        ]
        return plan, group, rows
    return [[s * per_dev + j for j in range(per_dev)] for s in range(n_seq)], 0, rows


def per_device(ring, query, keys, values, out_weight, grad_out, far_blocks, far_live):
    n_dp = lax.axis_size("dp")
    n_seq = lax.axis_size("seq")
    s_idx = lax.axis_index("seq")
    head_count = far_blocks.shape[1]
    per_dev = head_count // n_seq
    features = query.shape[2]
    head_dim = features // head_count
    number = far_blocks.shape[2]
    plan, group, rows = head_plan(n_dp, n_seq, head_count, head_dim, features)
    order = [h for heads in plan for h in heads]
    plan_arr = jnp.array(plan, jnp.int32)
    my_heads = plan_arr[s_idx]

    stacked = jnp.stack([query[0], keys[0], values[0]])
    tokens = stacked.shape[1]
    by_head = stacked.reshape(3, tokens, head_count, head_dim)
    stacked = jnp.stack([by_head[:, :, h] for h in order], axis=2).reshape(3, tokens, features)
    heads_qkv = lax.all_to_all(stacked, "seq", split_axis=2, concat_axis=1, tiled=True)
    length = heads_qkv.shape[1]

    weight = lax.all_gather(out_weight, "dp", axis=0, tiled=True)
    weight_heads = weight.reshape(head_count, head_dim, weight.shape[1])
    grad_doc = ring_gather(grad_out[0], ring, "seq")
    weight_rows = jnp.concatenate(
        [lax.dynamic_index_in_dim(weight_heads, my_heads[j], 0, False) for j in range(per_dev)]
    )
    grad_heads = lax.dot_general(
        grad_doc, weight_rows, (((1,), (1,)), ((), ())), preferred_element_type=jnp.float32
    ).astype(jnp.bfloat16)

    blocks_dev = jnp.stack(
        [lax.dynamic_index_in_dim(far_blocks[0], my_heads[j], 0, False) for j in range(per_dev)]
    )
    live_dev = jnp.stack(
        [lax.dynamic_index_in_dim(far_live[0], my_heads[j], 0, False) for j in range(per_dev)]
    )
    mask = block_mask(blocks_dev, live_dev)

    def head_cols(array, head):
        return array[:, head * head_dim : (head + 1) * head_dim]

    forward = [
        head_forward(
            head_cols(heads_qkv[0], j), head_cols(heads_qkv[1], j), head_cols(heads_qkv[2], j),
            mask[j], number,
        )
        for j in range(per_dev)
    ]
    attn_heads = jnp.stack([f[1].reshape(length, head_dim) for f in forward], axis=1)

    norm_factor = (n_dp * query.shape[0] * length) ** (-0.5)
    if group:
        me = s_idx % group
        sub = attn_heads.reshape(length, per_dev, group, rows)
        slots = jnp.zeros((length, group, per_dev, rows), attn_heads.dtype)
        slots = lax.dynamic_update_index_in_dim(
            slots, lax.dynamic_index_in_dim(sub, me, 2, False), me, 1
        )
        for shift in range(1, group):
            perm = [
                (base + i, base + (i + shift) % group)
                for base in range(0, n_seq, group)
                for i in range(group)
            ]
            target = (me + shift) % group
            sent = lax.dynamic_index_in_dim(sub, target, 2, False)
            got = lax.ppermute(sent, "seq", perm)
            source = (me - shift) % group
            slots = lax.dynamic_update_index_in_dim(slots, got, source, 1)
        mine = slots.reshape(length, n_dp * rows)
        partial = lax.dot_general(
            mine, grad_doc, (((0,), (0,)), ((), ())), preferred_element_type=jnp.float32
        )

        def weight_grad_of(partial):
            return lax.psum_scatter(partial, "dp", scatter_dimension=0, tiled=True)
    else:
        partial = lax.dot_general(
            attn_heads.reshape(length, per_dev * head_dim),
            grad_doc,
            (((0,), (0,)), ((), ())),
            preferred_element_type=jnp.float32,
        )

        def weight_grad_of(partial):
            reduced = lax.psum_scatter(partial, "dp", scatter_dimension=0, tiled=True)
            perm = []
            for d in range(n_dp):
                for s in range(n_seq):
                    perm.append((d * n_seq + s, s * n_dp + d))
            return lax.ppermute(reduced, ("dp", "seq"), perm=perm)
    partial, grad_heads = lax.optimization_barrier((partial * norm_factor, grad_heads))
    weight_grad = weight_grad_of(partial)

    results = [
        head_backward(
            head_cols(heads_qkv[0], j), head_cols(heads_qkv[1], j), head_cols(heads_qkv[2], j),
            head_cols(grad_heads, j), forward[j][0], forward[j][1], number,
        )
        for j in range(per_dev)
    ]
    arrived = [
        lax.all_to_all(jnp.stack(r), "seq", split_axis=1, concat_axis=2, tiled=True)
        for r in results
    ]
    pieces = [a.reshape(4, tokens, n_seq, head_dim) for a in arrived]
    where = {}
    for s, heads in enumerate(plan):
        for j, h in enumerate(heads):
            where[h] = (s, j)
    joined = jnp.concatenate(
        [pieces[where[h][1]][:, :, where[h][0]] for h in range(head_count)], axis=2
    )
    weight_heads = weight.reshape(head_count, head_dim, weight.shape[1])
    mixed_sum = None
    for j in range(per_dev):
        rows_j = jnp.concatenate([weight_heads[plan[s][j]] for s in range(n_seq)])
        part = jnp.dot(arrived[j][0], rows_j, preferred_element_type=jnp.float32)
        mixed_sum = part if mixed_sum is None else mixed_sum + part
    mixed = mixed_sum.astype(jnp.bfloat16)[None]
    back = [joined[i][None] for i in (1, 2, 3)]
    return (mixed, back[0], back[1], back[2], weight_grad)


def grid_cycle(rows, cols):
    cycle = [(r, 0) for r in range(rows)]
    for i, r in enumerate(range(rows - 1, -1, -1)):
        span = range(1, cols) if i % 2 == 0 else range(cols - 1, 0, -1)
        cycle.extend((r, c) for c in span)
    return cycle


def seq_ring(mesh):
    n_seq = mesh.shape["seq"]
    try:
        column = mesh.devices.reshape(-1, n_seq)[0]
        coords = [(d.coords[2], d.coords[0]) for d in column]
        zs = sorted({c[0] for c in coords})
        xs = sorted({c[1] for c in coords})
        where = {c: s for s, c in enumerate(coords)}
        if len(where) == n_seq and len(zs) * len(xs) == n_seq:
            if len(zs) % 2 == 0:
                cells = [(zs[r], xs[c]) for r, c in grid_cycle(len(zs), len(xs))]
            else:
                cells = [(zs[c], xs[r]) for r, c in grid_cycle(len(xs), len(zs))]
            order = [where[c] for c in cells]
            if sorted(order) == list(range(n_seq)):
                return tuple(order)
    except (AttributeError, IndexError, TypeError, KeyError):
        pass
    return tuple(range(n_seq))


def solution(mesh):
    ring = seq_ring(mesh)
    in_specs = (
        P("dp", "seq", None),
        P("dp", "seq", None),
        P("dp", "seq", None),
        P("dp", None),
        P("dp", "seq", None),
        P("dp", None, None, None),
        P("dp", None, None),
    )
    out_specs = (
        P("dp", "seq", None),
        P("dp", "seq", None),
        P("dp", "seq", None),
        P("dp", "seq", None),
        P(("dp", "seq"), None),
    )
    return jax.shard_map(
        functools.partial(per_device, ring), mesh=mesh, in_specs=in_specs, out_specs=out_specs, check_vma=False
    )
```

```python
import functools

import jax
import jax.numpy as jnp
from jax import lax
from jax.sharding import PartitionSpec as P

NEG = -1e30


def block_mask(blocks, live):
    number = blocks.shape[1]
    rows = jnp.arange(number, dtype=jnp.int32)[:, None]
    cols = jnp.arange(number, dtype=jnp.int32)[None, :]
    window = jnp.abs(rows - cols) <= 1
    far_pos = jnp.arange(blocks.shape[2], dtype=jnp.int32)
    far_used = far_pos[None, None, :] < live[:, :, None]
    hits = (blocks[:, :, :, None] == cols[None, None, :, :]) & far_used[:, :, :, None]
    return window[None] | jnp.any(hits, axis=2)


def head_forward(q, k, v, mask, number):
    length, head_dim = q.shape
    rows = length // number
    scale = head_dim ** (-0.5)
    qb = q.reshape(number, rows, head_dim)
    visible = jnp.repeat(mask, rows, axis=1)[:, None, :]
    raw = jnp.einsum("bqd,kd->bqk", qb, k, preferred_element_type=jnp.float32) * scale
    scores = jnp.where(visible, raw, NEG)
    row_max = jnp.max(scores, axis=-1, keepdims=True)
    log_total = row_max + jnp.log(jnp.sum(jnp.exp(scores - row_max), axis=-1, keepdims=True))
    softmax_w = jnp.exp(scores - log_total)
    probs = softmax_w.astype(jnp.bfloat16)
    attention = jnp.einsum("bqk,kd->bqd", probs, v, preferred_element_type=jnp.float32).astype(
        jnp.bfloat16
    )
    return softmax_w, attention


def head_backward(q, k, v, g, softmax_w, attention, number):
    length, head_dim = q.shape
    rows = length // number
    scale = head_dim ** (-0.5)
    qb = q.reshape(number, rows, head_dim)
    gb = g.reshape(number, rows, head_dim)
    probs = softmax_w.astype(jnp.bfloat16)
    row_dots = jnp.sum(
        gb.astype(jnp.float32) * attention.astype(jnp.float32), axis=-1, keepdims=True
    )
    grad_probs = jnp.einsum("bqd,kd->bqk", gb, v, preferred_element_type=jnp.float32)
    dscore = (softmax_w * (grad_probs - row_dots)).astype(jnp.bfloat16)
    grad_q = scale * jnp.einsum("bqk,kd->bqd", dscore, k, preferred_element_type=jnp.float32)
    grad_k = scale * jnp.einsum("bqk,bqd->kd", dscore, qb, preferred_element_type=jnp.float32)
    grad_v = jnp.einsum("bqk,bqd->kd", probs, gb, preferred_element_type=jnp.float32)
    return (
        attention.reshape(length, head_dim),
        grad_q.reshape(length, head_dim).astype(jnp.bfloat16),
        grad_k.astype(jnp.bfloat16),
        grad_v.astype(jnp.bfloat16),
    )


def ring_gather(block, ring, axis):
    n = len(ring)
    position = [0] * n
    for p, member in enumerate(ring):
        position[member] = p
    forward = [(ring[p], ring[(p + 1) % n]) for p in range(n)]
    backward = [(ring[p], ring[(p - 1) % n]) for p in range(n)]
    ring_arr = jnp.array(ring, jnp.int32)
    me = lax.axis_index(axis)
    p = jnp.array(position, jnp.int32)[me]
    out = jnp.zeros((n,) + block.shape, block.dtype)
    out = lax.dynamic_update_index_in_dim(out, block, me, 0)
    ahead, behind = block, block
    n_fwd = n // 2
    n_bwd = n - 1 - n_fwd
    for k in range(1, n_fwd + 1):
        ahead = lax.ppermute(ahead, axis, forward)
        out = lax.dynamic_update_index_in_dim(out, ahead, ring_arr[(p - k) % n], 0)
        if k <= n_bwd:
            behind = lax.ppermute(behind, axis, backward)
            out = lax.dynamic_update_index_in_dim(out, behind, ring_arr[(p + k) % n], 0)
    return out.reshape((n * block.shape[0],) + block.shape[1:])


def head_plan(n_dp, n_seq, head_count, head_dim, features):
    per_dev = head_count // n_seq
    rows = features // (n_dp * n_seq)
    group = head_dim // rows if rows and head_dim % rows == 0 else 0
    if group and n_seq % group == 0 and n_dp == group * per_dev:
        stride = n_seq // group
        plan = [
            [stride * ((s % group) * per_dev + j) + s // group for j in range(per_dev)]
            for s in range(n_seq)
        ]
        return plan, group, rows
    return [[s * per_dev + j for j in range(per_dev)] for s in range(n_seq)], 0, rows


def per_device(ring, query, keys, values, out_weight, grad_out, far_blocks, far_live):
    n_dp = lax.axis_size("dp")
    n_seq = lax.axis_size("seq")
    s_idx = lax.axis_index("seq")
    head_count = far_blocks.shape[1]
    per_dev = head_count // n_seq
    features = query.shape[2]
    head_dim = features // head_count
    number = far_blocks.shape[2]
    plan, group, rows = head_plan(n_dp, n_seq, head_count, head_dim, features)
    order = [h for heads in plan for h in heads]
    plan_arr = jnp.array(plan, jnp.int32)
    my_heads = plan_arr[s_idx]

    stacked = jnp.stack([query[0], keys[0], values[0]])
    tokens = stacked.shape[1]
    by_head = stacked.reshape(3, tokens, head_count, head_dim)
    stacked = jnp.stack([by_head[:, :, h] for h in order], axis=2).reshape(3, tokens, features)
    heads_qkv = lax.all_to_all(stacked, "seq", split_axis=2, concat_axis=1, tiled=True)
    length = heads_qkv.shape[1]

    weight = lax.all_gather(out_weight, "dp", axis=0, tiled=True)
    weight_heads = weight.reshape(head_count, head_dim, weight.shape[1])
    grad_doc = ring_gather(grad_out[0], ring, "seq")
    weight_rows = jnp.concatenate(
        [lax.dynamic_index_in_dim(weight_heads, my_heads[j], 0, False) for j in range(per_dev)]
    )
    grad_heads = lax.dot_general(
        grad_doc, weight_rows, (((1,), (1,)), ((), ())), preferred_element_type=jnp.float32
    ).astype(jnp.bfloat16)

    blocks_dev = jnp.stack(
        [lax.dynamic_index_in_dim(far_blocks[0], my_heads[j], 0, False) for j in range(per_dev)]
    )
    live_dev = jnp.stack(
        [lax.dynamic_index_in_dim(far_live[0], my_heads[j], 0, False) for j in range(per_dev)]
    )
    mask = block_mask(blocks_dev, live_dev)

    def head_cols(array, head):
        return array[:, head * head_dim : (head + 1) * head_dim]

    forward = [
        head_forward(
            head_cols(heads_qkv[0], j), head_cols(heads_qkv[1], j), head_cols(heads_qkv[2], j),
            mask[j], number,
        )
        for j in range(per_dev)
    ]
    attn_heads = jnp.stack([f[1].reshape(length, head_dim) for f in forward], axis=1)

    norm_factor = (n_dp * query.shape[0] * length) ** (-0.5)
    if group:
        me = s_idx % group
        sub = attn_heads.reshape(length, per_dev, group, rows)
        slots = jnp.zeros((length, group, per_dev, rows), attn_heads.dtype)
        slots = lax.dynamic_update_index_in_dim(
            slots, lax.dynamic_index_in_dim(sub, me, 2, False), me, 1
        )
        for shift in range(1, group):
            perm = [
                (base + i, base + (i + shift) % group)
                for base in range(0, n_seq, group)
                for i in range(group)
            ]
            target = (me + shift) % group
            sent = lax.dynamic_index_in_dim(sub, target, 2, False)
            got = lax.ppermute(sent, "seq", perm)
            source = (me - shift) % group
            slots = lax.dynamic_update_index_in_dim(slots, got, source, 1)
        mine = slots.reshape(length, n_dp * rows)
        partial = lax.dot_general(
            mine, grad_doc, (((0,), (0,)), ((), ())), preferred_element_type=jnp.float32
        )

        def weight_grad_of(partial):
            summed = lax.psum_scatter(
                partial.astype(jnp.bfloat16), "dp", scatter_dimension=0, tiled=True
            )
            return summed.astype(jnp.float32)
    else:
        partial = lax.dot_general(
            attn_heads.reshape(length, per_dev * head_dim),
            grad_doc,
            (((0,), (0,)), ((), ())),
            preferred_element_type=jnp.float32,
        )

        def weight_grad_of(partial):
            reduced = lax.psum_scatter(partial, "dp", scatter_dimension=0, tiled=True)
            perm = []
            for d in range(n_dp):
                for s in range(n_seq):
                    perm.append((d * n_seq + s, s * n_dp + d))
            return lax.ppermute(reduced, ("dp", "seq"), perm=perm)
    partial, grad_heads = lax.optimization_barrier((partial * norm_factor, grad_heads))
    weight_grad = weight_grad_of(partial)

    results = [
        head_backward(
            head_cols(heads_qkv[0], j), head_cols(heads_qkv[1], j), head_cols(heads_qkv[2], j),
            head_cols(grad_heads, j), forward[j][0], forward[j][1], number,
        )
        for j in range(per_dev)
    ]
    arrived = [
        lax.all_to_all(jnp.stack(r), "seq", split_axis=1, concat_axis=2, tiled=True)
        for r in results
    ]
    pieces = [a.reshape(4, tokens, n_seq, head_dim) for a in arrived]
    where = {}
    for s, heads in enumerate(plan):
        for j, h in enumerate(heads):
            where[h] = (s, j)
    joined = jnp.concatenate(
        [pieces[where[h][1]][:, :, where[h][0]] for h in range(head_count)], axis=2
    )
    mixed = jnp.dot(joined[0], weight, preferred_element_type=jnp.float32).astype(jnp.bfloat16)[
        None
    ]
    back = [joined[i][None] for i in (1, 2, 3)]
    return (mixed, back[0], back[1], back[2], weight_grad)


def grid_cycle(rows, cols):
    cycle = [(r, 0) for r in range(rows)]
    for i, r in enumerate(range(rows - 1, -1, -1)):
        span = range(1, cols) if i % 2 == 0 else range(cols - 1, 0, -1)
        cycle.extend((r, c) for c in span)
    return cycle


def seq_ring(mesh):
    n_seq = mesh.shape["seq"]
    try:
        column = mesh.devices.reshape(-1, n_seq)[0]
        coords = [(d.coords[2], d.coords[0]) for d in column]
        zs = sorted({c[0] for c in coords})
        xs = sorted({c[1] for c in coords})
        where = {c: s for s, c in enumerate(coords)}
        if len(where) == n_seq and len(zs) * len(xs) == n_seq:
            if len(zs) % 2 == 0:
                cells = [(zs[r], xs[c]) for r, c in grid_cycle(len(zs), len(xs))]
            else:
                cells = [(zs[c], xs[r]) for r, c in grid_cycle(len(xs), len(zs))]
            order = [where[c] for c in cells]
            if sorted(order) == list(range(n_seq)):
                return tuple(order)
    except (AttributeError, IndexError, TypeError, KeyError):
        pass
    return tuple(range(n_seq))


def solution(mesh):
    ring = seq_ring(mesh)
    in_specs = (
        P("dp", "seq", None),
        P("dp", "seq", None),
        P("dp", "seq", None),
        P("dp", None),
        P("dp", "seq", None),
        P("dp", None, None, None),
        P("dp", None, None),
    )
    out_specs = (
        P("dp", "seq", None),
        P("dp", "seq", None),
        P("dp", "seq", None),
        P("dp", "seq", None),
        P(("dp", "seq"), None),
    )
    return jax.shard_map(
        functools.partial(per_device, ring), mesh=mesh, in_specs=in_specs, out_specs=out_specs, check_vma=False
    )
```

```python
import functools

import jax
import jax.numpy as jnp
from jax import lax
from jax.sharding import PartitionSpec as P

NEG = -1e30


def block_mask(blocks, live):
    number = blocks.shape[1]
    rows = jnp.arange(number, dtype=jnp.int32)[:, None]
    cols = jnp.arange(number, dtype=jnp.int32)[None, :]
    window = jnp.abs(rows - cols) <= 1
    far_pos = jnp.arange(blocks.shape[2], dtype=jnp.int32)
    far_used = far_pos[None, None, :] < live[:, :, None]
    hits = (blocks[:, :, :, None] == cols[None, None, :, :]) & far_used[:, :, :, None]
    return window[None] | jnp.any(hits, axis=2)


def head_forward(q, k, v, mask, number):
    length, head_dim = q.shape
    rows = length // number
    scale = head_dim ** (-0.5)
    qb = q.reshape(number, rows, head_dim)
    visible = jnp.repeat(mask, rows, axis=1)[:, None, :]
    raw = jnp.einsum("bqd,kd->bqk", qb, k, preferred_element_type=jnp.float32) * scale
    scores = jnp.where(visible, raw, NEG)
    row_max = jnp.max(scores, axis=-1, keepdims=True)
    log_total = row_max + jnp.log(jnp.sum(jnp.exp(scores - row_max), axis=-1, keepdims=True))
    softmax_w = jnp.exp(scores - log_total)
    probs = softmax_w.astype(jnp.bfloat16)
    attention = jnp.einsum("bqk,kd->bqd", probs, v, preferred_element_type=jnp.float32).astype(
        jnp.bfloat16
    )
    return softmax_w, attention


def head_backward(q, k, v, g, softmax_w, attention, number):
    length, head_dim = q.shape
    rows = length // number
    scale = head_dim ** (-0.5)
    qb = q.reshape(number, rows, head_dim)
    gb = g.reshape(number, rows, head_dim)
    probs = softmax_w.astype(jnp.bfloat16)
    row_dots = jnp.sum(
        gb.astype(jnp.float32) * attention.astype(jnp.float32), axis=-1, keepdims=True
    )
    grad_probs = jnp.einsum("bqd,kd->bqk", gb, v, preferred_element_type=jnp.float32)
    dscore = (softmax_w * (grad_probs - row_dots)).astype(jnp.bfloat16)
    grad_q = scale * jnp.einsum("bqk,kd->bqd", dscore, k, preferred_element_type=jnp.float32)
    grad_k = scale * jnp.einsum("bqk,bqd->kd", dscore, qb, preferred_element_type=jnp.float32)
    grad_v = jnp.einsum("bqk,bqd->kd", probs, gb, preferred_element_type=jnp.float32)
    return (
        attention.reshape(length, head_dim),
        grad_q.reshape(length, head_dim).astype(jnp.bfloat16),
        grad_k.astype(jnp.bfloat16),
        grad_v.astype(jnp.bfloat16),
    )


def ring_gather(block, ring, axis):
    n = len(ring)
    position = [0] * n
    for p, member in enumerate(ring):
        position[member] = p
    forward = [(ring[p], ring[(p + 1) % n]) for p in range(n)]
    backward = [(ring[p], ring[(p - 1) % n]) for p in range(n)]
    ring_arr = jnp.array(ring, jnp.int32)
    me = lax.axis_index(axis)
    p = jnp.array(position, jnp.int32)[me]
    out = jnp.zeros((n,) + block.shape, block.dtype)
    out = lax.dynamic_update_index_in_dim(out, block, me, 0)
    ahead, behind = block, block
    n_fwd = n // 2
    n_bwd = n - 1 - n_fwd
    for k in range(1, n_fwd + 1):
        ahead = lax.ppermute(ahead, axis, forward)
        out = lax.dynamic_update_index_in_dim(out, ahead, ring_arr[(p - k) % n], 0)
        if k <= n_bwd:
            behind = lax.ppermute(behind, axis, backward)
            out = lax.dynamic_update_index_in_dim(out, behind, ring_arr[(p + k) % n], 0)
    return out.reshape((n * block.shape[0],) + block.shape[1:])


def head_plan(n_dp, n_seq, head_count, head_dim, features):
    per_dev = head_count // n_seq
    rows = features // (n_dp * n_seq)
    group = head_dim // rows if rows and head_dim % rows == 0 else 0
    if group and n_seq % group == 0 and n_dp == group * per_dev:
        stride = n_seq // group
        plan = [
            [stride * ((s % group) * per_dev + j) + s // group for j in range(per_dev)]
            for s in range(n_seq)
        ]
        return plan, group, rows
    return [[s * per_dev + j for j in range(per_dev)] for s in range(n_seq)], 0, rows


def per_device(ring, query, keys, values, out_weight, grad_out, far_blocks, far_live):
    n_dp = lax.axis_size("dp")
    n_seq = lax.axis_size("seq")
    s_idx = lax.axis_index("seq")
    head_count = far_blocks.shape[1]
    per_dev = head_count // n_seq
    features = query.shape[2]
    head_dim = features // head_count
    number = far_blocks.shape[2]
    plan, group, rows = head_plan(n_dp, n_seq, head_count, head_dim, features)
    order = [h for heads in plan for h in heads]
    plan_arr = jnp.array(plan, jnp.int32)
    my_heads = plan_arr[s_idx]

    stacked = jnp.stack([query[0], keys[0], values[0]])
    tokens = stacked.shape[1]
    by_head = stacked.reshape(3, tokens, head_count, head_dim)
    stacked = jnp.stack([by_head[:, :, h] for h in order], axis=2).reshape(3, tokens, features)
    heads_qkv = lax.all_to_all(stacked, "seq", split_axis=2, concat_axis=1, tiled=True)
    length = heads_qkv.shape[1]

    weight = lax.all_gather(out_weight, "dp", axis=0, tiled=True)
    weight_heads = weight.reshape(head_count, head_dim, weight.shape[1])
    grad_doc = ring_gather(grad_out[0], ring, "seq")
    weight_rows = jnp.concatenate(
        [lax.dynamic_index_in_dim(weight_heads, my_heads[j], 0, False) for j in range(per_dev)]
    )
    grad_heads = lax.dot_general(
        grad_doc, weight_rows, (((1,), (1,)), ((), ())), preferred_element_type=jnp.float32
    ).astype(jnp.bfloat16)

    blocks_dev = jnp.stack(
        [lax.dynamic_index_in_dim(far_blocks[0], my_heads[j], 0, False) for j in range(per_dev)]
    )
    live_dev = jnp.stack(
        [lax.dynamic_index_in_dim(far_live[0], my_heads[j], 0, False) for j in range(per_dev)]
    )
    mask = block_mask(blocks_dev, live_dev)

    def head_cols(array, head):
        return array[:, head * head_dim : (head + 1) * head_dim]

    forward = [
        head_forward(
            head_cols(heads_qkv[0], j), head_cols(heads_qkv[1], j), head_cols(heads_qkv[2], j),
            mask[j], number,
        )
        for j in range(per_dev)
    ]
    attn_heads = jnp.stack([f[1].reshape(length, head_dim) for f in forward], axis=1)

    norm_factor = (n_dp * query.shape[0] * length) ** (-0.5)
    if group:
        me = s_idx % group
        sub = attn_heads.reshape(length, per_dev, group, rows)
        slots = jnp.zeros((length, group, per_dev, rows), attn_heads.dtype)
        slots = lax.dynamic_update_index_in_dim(
            slots, lax.dynamic_index_in_dim(sub, me, 2, False), me, 1
        )
        for shift in range(1, group):
            perm = [
                (base + i, base + (i + shift) % group)
                for base in range(0, n_seq, group)
                for i in range(group)
            ]
            target = (me + shift) % group
            sent = lax.dynamic_index_in_dim(sub, target, 2, False)
            got = lax.ppermute(sent, "seq", perm)
            source = (me - shift) % group
            slots = lax.dynamic_update_index_in_dim(slots, got, source, 1)
        mine = slots.reshape(length, n_dp * rows)
        partial = lax.dot_general(
            mine, grad_doc, (((0,), (0,)), ((), ())), preferred_element_type=jnp.float32
        )

        def weight_grad_of(partial):
            summed = lax.psum_scatter(
                partial.astype(jnp.bfloat16), "dp", scatter_dimension=0, tiled=True
            )
            return summed.astype(jnp.float32)
    else:
        partial = lax.dot_general(
            attn_heads.reshape(length, per_dev * head_dim),
            grad_doc,
            (((0,), (0,)), ((), ())),
            preferred_element_type=jnp.float32,
        )

        def weight_grad_of(partial):
            reduced = lax.psum_scatter(partial, "dp", scatter_dimension=0, tiled=True)
            perm = []
            for d in range(n_dp):
                for s in range(n_seq):
                    perm.append((d * n_seq + s, s * n_dp + d))
            return lax.ppermute(reduced, ("dp", "seq"), perm=perm)
    attention_out = lax.all_to_all(
        attn_heads.reshape(length, per_dev * head_dim), "seq", split_axis=0, concat_axis=1,
        tiled=True,
    )
    partial, grad_heads, attention_out = lax.optimization_barrier(
        (partial * norm_factor, grad_heads, attention_out)
    )
    weight_grad = weight_grad_of(partial)

    results = [
        head_backward(
            head_cols(heads_qkv[0], j), head_cols(heads_qkv[1], j), head_cols(heads_qkv[2], j),
            head_cols(grad_heads, j), forward[j][0], forward[j][1], number,
        )
        for j in range(per_dev)
    ]
    arrived = [
        lax.all_to_all(jnp.stack(r[1:]), "seq", split_axis=1, concat_axis=2, tiled=True)
        for r in results
    ]
    pieces = [a.reshape(3, tokens, n_seq, head_dim) for a in arrived]
    att_pieces = attention_out.reshape(tokens, n_seq, per_dev, head_dim)
    where = {}
    for s, heads in enumerate(plan):
        for j, h in enumerate(heads):
            where[h] = (s, j)
    attention = jnp.concatenate(
        [att_pieces[:, where[h][0], where[h][1]] for h in range(head_count)], axis=1
    )
    joined = jnp.concatenate(
        [pieces[where[h][1]][:, :, where[h][0]] for h in range(head_count)], axis=2
    )
    mixed = jnp.dot(attention, weight, preferred_element_type=jnp.float32).astype(jnp.bfloat16)[
        None
    ]
    back = [joined[i][None] for i in (0, 1, 2)]
    return (mixed, back[0], back[1], back[2], weight_grad)


def grid_cycle(rows, cols):
    cycle = [(r, 0) for r in range(rows)]
    for i, r in enumerate(range(rows - 1, -1, -1)):
        span = range(1, cols) if i % 2 == 0 else range(cols - 1, 0, -1)
        cycle.extend((r, c) for c in span)
    return cycle


def seq_ring(mesh):
    n_seq = mesh.shape["seq"]
    try:
        column = mesh.devices.reshape(-1, n_seq)[0]
        coords = [(d.coords[2], d.coords[0]) for d in column]
        zs = sorted({c[0] for c in coords})
        xs = sorted({c[1] for c in coords})
        where = {c: s for s, c in enumerate(coords)}
        if len(where) == n_seq and len(zs) * len(xs) == n_seq:
            if len(zs) % 2 == 0:
                cells = [(zs[r], xs[c]) for r, c in grid_cycle(len(zs), len(xs))]
            else:
                cells = [(zs[c], xs[r]) for r, c in grid_cycle(len(xs), len(zs))]
            order = [where[c] for c in cells]
            if sorted(order) == list(range(n_seq)):
                return tuple(order)
    except (AttributeError, IndexError, TypeError, KeyError):
        pass
    return tuple(range(n_seq))


def solution(mesh):
    ring = seq_ring(mesh)
    in_specs = (
        P("dp", "seq", None),
        P("dp", "seq", None),
        P("dp", "seq", None),
        P("dp", None),
        P("dp", "seq", None),
        P("dp", None, None, None),
        P("dp", None, None),
    )
    out_specs = (
        P("dp", "seq", None),
        P("dp", "seq", None),
        P("dp", "seq", None),
        P("dp", "seq", None),
        P(("dp", "seq"), None),
    )
    return jax.shard_map(
        functools.partial(per_device, ring), mesh=mesh, in_specs=in_specs, out_specs=out_specs, check_vma=False
    )
```

```python
import functools

import jax
import jax.numpy as jnp
from jax import lax
from jax.sharding import PartitionSpec as P

NEG = -1e30


def block_mask(blocks, live):
    number = blocks.shape[1]
    rows = jnp.arange(number, dtype=jnp.int32)[:, None]
    cols = jnp.arange(number, dtype=jnp.int32)[None, :]
    window = jnp.abs(rows - cols) <= 1
    far_pos = jnp.arange(blocks.shape[2], dtype=jnp.int32)
    far_used = far_pos[None, None, :] < live[:, :, None]
    hits = (blocks[:, :, :, None] == cols[None, None, :, :]) & far_used[:, :, :, None]
    return window[None] | jnp.any(hits, axis=2)


def head_forward(q, k, v, mask, number):
    length, head_dim = q.shape
    rows = length // number
    scale = head_dim ** (-0.5)
    qb = q.reshape(number, rows, head_dim)
    visible = jnp.repeat(mask, rows, axis=1)[:, None, :]
    raw = jnp.einsum("bqd,kd->bqk", qb, k, preferred_element_type=jnp.float32) * scale
    scores = jnp.where(visible, raw, NEG)
    row_max = jnp.max(scores, axis=-1, keepdims=True)
    log_total = row_max + jnp.log(jnp.sum(jnp.exp(scores - row_max), axis=-1, keepdims=True))
    softmax_w = jnp.exp(scores - log_total)
    probs = softmax_w.astype(jnp.bfloat16)
    attention = jnp.einsum("bqk,kd->bqd", probs, v, preferred_element_type=jnp.float32).astype(
        jnp.bfloat16
    )
    return softmax_w, attention


def head_backward(q, k, v, g, softmax_w, attention, number):
    length, head_dim = q.shape
    rows = length // number
    scale = head_dim ** (-0.5)
    qb = q.reshape(number, rows, head_dim)
    gb = g.reshape(number, rows, head_dim)
    probs = softmax_w.astype(jnp.bfloat16)
    row_dots = jnp.sum(
        gb.astype(jnp.float32) * attention.astype(jnp.float32), axis=-1, keepdims=True
    )
    grad_probs = jnp.einsum("bqd,kd->bqk", gb, v, preferred_element_type=jnp.float32)
    dscore = (softmax_w * (grad_probs - row_dots)).astype(jnp.bfloat16)
    grad_q = scale * jnp.einsum("bqk,kd->bqd", dscore, k, preferred_element_type=jnp.float32)
    grad_k = scale * jnp.einsum("bqk,bqd->kd", dscore, qb, preferred_element_type=jnp.float32)
    grad_v = jnp.einsum("bqk,bqd->kd", probs, gb, preferred_element_type=jnp.float32)
    return (
        attention.reshape(length, head_dim),
        grad_q.reshape(length, head_dim).astype(jnp.bfloat16),
        grad_k.astype(jnp.bfloat16),
        grad_v.astype(jnp.bfloat16),
    )


def ring_gather(block, ring, axis):
    n = len(ring)
    position = [0] * n
    for p, member in enumerate(ring):
        position[member] = p
    forward = [(ring[p], ring[(p + 1) % n]) for p in range(n)]
    backward = [(ring[p], ring[(p - 1) % n]) for p in range(n)]
    ring_arr = jnp.array(ring, jnp.int32)
    me = lax.axis_index(axis)
    p = jnp.array(position, jnp.int32)[me]
    out = jnp.zeros((n,) + block.shape, block.dtype)
    out = lax.dynamic_update_index_in_dim(out, block, me, 0)
    ahead, behind = block, block
    n_fwd = n // 2
    n_bwd = n - 1 - n_fwd
    for k in range(1, n_fwd + 1):
        ahead = lax.ppermute(ahead, axis, forward)
        out = lax.dynamic_update_index_in_dim(out, ahead, ring_arr[(p - k) % n], 0)
        if k <= n_bwd:
            behind = lax.ppermute(behind, axis, backward)
            out = lax.dynamic_update_index_in_dim(out, behind, ring_arr[(p + k) % n], 0)
    return out.reshape((n * block.shape[0],) + block.shape[1:])


def head_plan(n_dp, n_seq, head_count, head_dim, features):
    per_dev = head_count // n_seq
    rows = features // (n_dp * n_seq)
    group = head_dim // rows if rows and head_dim % rows == 0 else 0
    if group and n_seq % group == 0 and n_dp == group * per_dev:
        stride = n_seq // group
        plan = [
            [stride * ((s % group) * per_dev + j) + s // group for j in range(per_dev)]
            for s in range(n_seq)
        ]
        return plan, group, rows
    return [[s * per_dev + j for j in range(per_dev)] for s in range(n_seq)], 0, rows


def per_device(ring, query, keys, values, out_weight, grad_out, far_blocks, far_live):
    n_dp = lax.axis_size("dp")
    n_seq = lax.axis_size("seq")
    s_idx = lax.axis_index("seq")
    head_count = far_blocks.shape[1]
    per_dev = head_count // n_seq
    features = query.shape[2]
    head_dim = features // head_count
    number = far_blocks.shape[2]
    plan, group, rows = head_plan(n_dp, n_seq, head_count, head_dim, features)
    order = [h for heads in plan for h in heads]
    plan_arr = jnp.array(plan, jnp.int32)
    my_heads = plan_arr[s_idx]

    stacked = jnp.stack([query[0], keys[0], values[0]])
    tokens = stacked.shape[1]
    by_head = stacked.reshape(3, tokens, head_count, head_dim)
    stacked = jnp.stack([by_head[:, :, h] for h in order], axis=2).reshape(3, tokens, features)
    heads_qkv = lax.all_to_all(stacked, "seq", split_axis=2, concat_axis=1, tiled=True)
    length = heads_qkv.shape[1]

    weight = lax.all_gather(out_weight, "dp", axis=0, tiled=True)
    weight_heads = weight.reshape(head_count, head_dim, weight.shape[1])
    grad_doc = ring_gather(grad_out[0], ring, "seq")
    grad_doc, far_blocks, far_live = lax.optimization_barrier((grad_doc, far_blocks, far_live))
    weight_rows = jnp.concatenate(
        [lax.dynamic_index_in_dim(weight_heads, my_heads[j], 0, False) for j in range(per_dev)]
    )
    grad_heads = lax.dot_general(
        grad_doc, weight_rows, (((1,), (1,)), ((), ())), preferred_element_type=jnp.float32
    ).astype(jnp.bfloat16)

    blocks_dev = jnp.stack(
        [lax.dynamic_index_in_dim(far_blocks[0], my_heads[j], 0, False) for j in range(per_dev)]
    )
    live_dev = jnp.stack(
        [lax.dynamic_index_in_dim(far_live[0], my_heads[j], 0, False) for j in range(per_dev)]
    )
    mask = block_mask(blocks_dev, live_dev)

    def head_cols(array, head):
        return array[:, head * head_dim : (head + 1) * head_dim]

    forward = [
        head_forward(
            head_cols(heads_qkv[0], j), head_cols(heads_qkv[1], j), head_cols(heads_qkv[2], j),
            mask[j], number,
        )
        for j in range(per_dev)
    ]
    attn_heads = jnp.stack([f[1].reshape(length, head_dim) for f in forward], axis=1)

    norm_factor = (n_dp * query.shape[0] * length) ** (-0.5)
    if group:
        me = s_idx % group
        sub = attn_heads.reshape(length, per_dev, group, rows)
        slots = jnp.zeros((length, group, per_dev, rows), attn_heads.dtype)
        slots = lax.dynamic_update_index_in_dim(
            slots, lax.dynamic_index_in_dim(sub, me, 2, False), me, 1
        )
        for shift in range(1, group):
            perm = [
                (base + i, base + (i + shift) % group)
                for base in range(0, n_seq, group)
                for i in range(group)
            ]
            target = (me + shift) % group
            sent = lax.dynamic_index_in_dim(sub, target, 2, False)
            got = lax.ppermute(sent, "seq", perm)
            source = (me - shift) % group
            slots = lax.dynamic_update_index_in_dim(slots, got, source, 1)
        mine = slots.reshape(length, n_dp * rows)
        partial = lax.dot_general(
            mine, grad_doc, (((0,), (0,)), ((), ())), preferred_element_type=jnp.float32
        )

        def weight_grad_of(partial):
            summed = lax.psum_scatter(
                partial.astype(jnp.bfloat16), "dp", scatter_dimension=0, tiled=True
            )
            return summed.astype(jnp.float32)
    else:
        partial = lax.dot_general(
            attn_heads.reshape(length, per_dev * head_dim),
            grad_doc,
            (((0,), (0,)), ((), ())),
            preferred_element_type=jnp.float32,
        )

        def weight_grad_of(partial):
            reduced = lax.psum_scatter(partial, "dp", scatter_dimension=0, tiled=True)
            perm = []
            for d in range(n_dp):
                for s in range(n_seq):
                    perm.append((d * n_seq + s, s * n_dp + d))
            return lax.ppermute(reduced, ("dp", "seq"), perm=perm)
    partial, grad_heads = lax.optimization_barrier((partial * norm_factor, grad_heads))
    weight_grad = weight_grad_of(partial)

    results = [
        head_backward(
            head_cols(heads_qkv[0], j), head_cols(heads_qkv[1], j), head_cols(heads_qkv[2], j),
            head_cols(grad_heads, j), forward[j][0], forward[j][1], number,
        )
        for j in range(per_dev)
    ]
    arrived = [
        lax.all_to_all(jnp.stack(r), "seq", split_axis=1, concat_axis=2, tiled=True)
        for r in results
    ]
    pieces = [a.reshape(4, tokens, n_seq, head_dim) for a in arrived]
    where = {}
    for s, heads in enumerate(plan):
        for j, h in enumerate(heads):
            where[h] = (s, j)
    joined = jnp.concatenate(
        [pieces[where[h][1]][:, :, where[h][0]] for h in range(head_count)], axis=2
    )
    mixed = jnp.dot(joined[0], weight, preferred_element_type=jnp.float32).astype(jnp.bfloat16)[
        None
    ]
    back = [joined[i][None] for i in (1, 2, 3)]
    return (mixed, back[0], back[1], back[2], weight_grad)


def grid_cycle(rows, cols):
    cycle = [(r, 0) for r in range(rows)]
    for i, r in enumerate(range(rows - 1, -1, -1)):
        span = range(1, cols) if i % 2 == 0 else range(cols - 1, 0, -1)
        cycle.extend((r, c) for c in span)
    return cycle


def seq_ring(mesh):
    n_seq = mesh.shape["seq"]
    try:
        column = mesh.devices.reshape(-1, n_seq)[0]
        coords = [(d.coords[2], d.coords[0]) for d in column]
        zs = sorted({c[0] for c in coords})
        xs = sorted({c[1] for c in coords})
        where = {c: s for s, c in enumerate(coords)}
        if len(where) == n_seq and len(zs) * len(xs) == n_seq:
            if len(zs) % 2 == 0:
                cells = [(zs[r], xs[c]) for r, c in grid_cycle(len(zs), len(xs))]
            else:
                cells = [(zs[c], xs[r]) for r, c in grid_cycle(len(xs), len(zs))]
            order = [where[c] for c in cells]
            if sorted(order) == list(range(n_seq)):
                return tuple(order)
    except (AttributeError, IndexError, TypeError, KeyError):
        pass
    return tuple(range(n_seq))


def solution(mesh):
    ring = seq_ring(mesh)
    in_specs = (
        P("dp", "seq", None),
        P("dp", "seq", None),
        P("dp", "seq", None),
        P("dp", None),
        P("dp", "seq", None),
        P("dp", None, None, None),
        P("dp", None, None),
    )
    out_specs = (
        P("dp", "seq", None),
        P("dp", "seq", None),
        P("dp", "seq", None),
        P("dp", "seq", None),
        P(("dp", "seq"), None),
    )
    return jax.shard_map(
        functools.partial(per_device, ring), mesh=mesh, in_specs=in_specs, out_specs=out_specs, check_vma=False
    )
```

```python
import functools

import jax
import jax.numpy as jnp
from jax import lax
from jax.sharding import PartitionSpec as P

NEG = -1e30


def block_mask(blocks, live):
    number = blocks.shape[1]
    rows = jnp.arange(number, dtype=jnp.int32)[:, None]
    cols = jnp.arange(number, dtype=jnp.int32)[None, :]
    window = jnp.abs(rows - cols) <= 1
    far_pos = jnp.arange(blocks.shape[2], dtype=jnp.int32)
    far_used = far_pos[None, None, :] < live[:, :, None]
    hits = (blocks[:, :, :, None] == cols[None, None, :, :]) & far_used[:, :, :, None]
    return window[None] | jnp.any(hits, axis=2)


def head_forward(q, k, v, mask, number):
    length, head_dim = q.shape
    rows = length // number
    scale = head_dim ** (-0.5)
    qb = q.reshape(number, rows, head_dim)
    visible = jnp.repeat(mask, rows, axis=1)[:, None, :]
    raw = jnp.einsum("bqd,kd->bqk", qb, k, preferred_element_type=jnp.float32) * scale
    scores = jnp.where(visible, raw, NEG)
    row_max = jnp.max(scores, axis=-1, keepdims=True)
    log_total = row_max + jnp.log(jnp.sum(jnp.exp(scores - row_max), axis=-1, keepdims=True))
    softmax_w = jnp.exp(scores - log_total)
    probs = softmax_w.astype(jnp.bfloat16)
    attention = jnp.einsum("bqk,kd->bqd", probs, v, preferred_element_type=jnp.float32).astype(
        jnp.bfloat16
    )
    return softmax_w, attention


def head_backward(q, k, v, g, softmax_w, attention, number):
    length, head_dim = q.shape
    rows = length // number
    scale = head_dim ** (-0.5)
    qb = q.reshape(number, rows, head_dim)
    gb = g.reshape(number, rows, head_dim)
    probs = softmax_w.astype(jnp.bfloat16)
    row_dots = jnp.sum(
        gb.astype(jnp.float32) * attention.astype(jnp.float32), axis=-1, keepdims=True
    )
    grad_probs = jnp.einsum("bqd,kd->bqk", gb, v, preferred_element_type=jnp.float32)
    dscore = (softmax_w * (grad_probs - row_dots)).astype(jnp.bfloat16)
    grad_q = scale * jnp.einsum("bqk,kd->bqd", dscore, k, preferred_element_type=jnp.float32)
    grad_k = scale * jnp.einsum("bqk,bqd->kd", dscore, qb, preferred_element_type=jnp.float32)
    grad_v = jnp.einsum("bqk,bqd->kd", probs, gb, preferred_element_type=jnp.float32)
    return (
        attention.reshape(length, head_dim),
        grad_q.reshape(length, head_dim).astype(jnp.bfloat16),
        grad_k.astype(jnp.bfloat16),
        grad_v.astype(jnp.bfloat16),
    )


def ring_gather(block, ring, axis):
    n = len(ring)
    position = [0] * n
    for p, member in enumerate(ring):
        position[member] = p
    forward = [(ring[p], ring[(p + 1) % n]) for p in range(n)]
    backward = [(ring[p], ring[(p - 1) % n]) for p in range(n)]
    ring_arr = jnp.array(ring, jnp.int32)
    me = lax.axis_index(axis)
    p = jnp.array(position, jnp.int32)[me]
    out = jnp.zeros((n,) + block.shape, block.dtype)
    out = lax.dynamic_update_index_in_dim(out, block, me, 0)
    ahead, behind = block, block
    n_fwd = n // 2
    n_bwd = n - 1 - n_fwd
    for k in range(1, n_fwd + 1):
        ahead = lax.ppermute(ahead, axis, forward)
        out = lax.dynamic_update_index_in_dim(out, ahead, ring_arr[(p - k) % n], 0)
        if k <= n_bwd:
            behind = lax.ppermute(behind, axis, backward)
            out = lax.dynamic_update_index_in_dim(out, behind, ring_arr[(p + k) % n], 0)
    return out.reshape((n * block.shape[0],) + block.shape[1:])


def head_plan(n_dp, n_seq, head_count, head_dim, features):
    per_dev = head_count // n_seq
    rows = features // (n_dp * n_seq)
    group = head_dim // rows if rows and head_dim % rows == 0 else 0
    if group and n_seq % group == 0 and n_dp == group * per_dev:
        stride = n_seq // group
        plan = [
            [stride * ((s % group) * per_dev + j) + s // group for j in range(per_dev)]
            for s in range(n_seq)
        ]
        return plan, group, rows
    return [[s * per_dev + j for j in range(per_dev)] for s in range(n_seq)], 0, rows


def per_device(ring, query, keys, values, out_weight, grad_out, far_blocks, far_live):
    n_dp = lax.axis_size("dp")
    n_seq = lax.axis_size("seq")
    s_idx = lax.axis_index("seq")
    head_count = far_blocks.shape[1]
    per_dev = head_count // n_seq
    features = query.shape[2]
    head_dim = features // head_count
    number = far_blocks.shape[2]
    plan, group, rows = head_plan(n_dp, n_seq, head_count, head_dim, features)
    order = [h for heads in plan for h in heads]
    plan_arr = jnp.array(plan, jnp.int32)
    my_heads = plan_arr[s_idx]

    stacked = jnp.stack([query[0], keys[0], values[0]])
    tokens = stacked.shape[1]
    by_head = stacked.reshape(3, tokens, head_count, head_dim)
    stacked = jnp.stack([by_head[:, :, h] for h in order], axis=2).reshape(3, tokens, features)
    heads_qkv = lax.all_to_all(stacked, "seq", split_axis=2, concat_axis=1, tiled=True)
    length = heads_qkv.shape[1]

    weight = lax.all_gather(out_weight, "dp", axis=0, tiled=True)
    weight_heads = weight.reshape(head_count, head_dim, weight.shape[1])
    grad_doc = ring_gather(grad_out[0], ring, "seq")
    weight_rows = jnp.concatenate(
        [lax.dynamic_index_in_dim(weight_heads, my_heads[j], 0, False) for j in range(per_dev)]
    )
    grad_heads = lax.dot_general(
        grad_doc, weight_rows, (((1,), (1,)), ((), ())), preferred_element_type=jnp.float32
    ).astype(jnp.bfloat16)

    blocks_dev = jnp.stack(
        [lax.dynamic_index_in_dim(far_blocks[0], my_heads[j], 0, False) for j in range(per_dev)]
    )
    live_dev = jnp.stack(
        [lax.dynamic_index_in_dim(far_live[0], my_heads[j], 0, False) for j in range(per_dev)]
    )
    mask = block_mask(blocks_dev, live_dev)

    def head_cols(array, head):
        return array[:, head * head_dim : (head + 1) * head_dim]

    forward = [
        head_forward(
            head_cols(heads_qkv[0], j), head_cols(heads_qkv[1], j), head_cols(heads_qkv[2], j),
            mask[j], number,
        )
        for j in range(per_dev)
    ]
    attn_heads = jnp.stack([f[1].reshape(length, head_dim) for f in forward], axis=1)

    norm_factor = (n_dp * query.shape[0] * length) ** (-0.5)
    if group:
        me = s_idx % group
        sub = attn_heads.reshape(length, per_dev, group, rows)
        slots = jnp.zeros((length, group, per_dev, rows), attn_heads.dtype)
        slots = lax.dynamic_update_index_in_dim(
            slots, lax.dynamic_index_in_dim(sub, me, 2, False), me, 1
        )
        for shift in range(1, group):
            perm = [
                (base + i, base + (i + shift) % group)
                for base in range(0, n_seq, group)
                for i in range(group)
            ]
            target = (me + shift) % group
            sent = lax.dynamic_index_in_dim(sub, target, 2, False)
            got = lax.ppermute(sent, "seq", perm)
            source = (me - shift) % group
            slots = lax.dynamic_update_index_in_dim(slots, got, source, 1)
        mine = slots.reshape(length, n_dp * rows)
        partial = lax.dot_general(
            mine, grad_doc, (((0,), (0,)), ((), ())), preferred_element_type=jnp.float32
        )

        def weight_grad_of(partial):
            summed = lax.psum_scatter(
                partial.astype(jnp.bfloat16), "dp", scatter_dimension=0, tiled=True
            )
            return summed.astype(jnp.float32)
    else:
        partial = lax.dot_general(
            attn_heads.reshape(length, per_dev * head_dim),
            grad_doc,
            (((0,), (0,)), ((), ())),
            preferred_element_type=jnp.float32,
        )

        def weight_grad_of(partial):
            reduced = lax.psum_scatter(partial, "dp", scatter_dimension=0, tiled=True)
            perm = []
            for d in range(n_dp):
                for s in range(n_seq):
                    perm.append((d * n_seq + s, s * n_dp + d))
            return lax.ppermute(reduced, ("dp", "seq"), perm=perm)
    partial, grad_heads = lax.optimization_barrier((partial * norm_factor, grad_heads))
    weight_grad = weight_grad_of(partial)

    results = [
        head_backward(
            head_cols(heads_qkv[0], j), head_cols(heads_qkv[1], j), head_cols(heads_qkv[2], j),
            head_cols(grad_heads, j), forward[j][0], forward[j][1], number,
        )
        for j in range(per_dev)
    ]
    arrived = [
        lax.all_to_all(jnp.stack(r), "seq", split_axis=1, concat_axis=2, tiled=True)
        for r in results
    ]
    pieces = [a.reshape(4, tokens, n_seq, head_dim) for a in arrived]
    where = {}
    for s, heads in enumerate(plan):
        for j, h in enumerate(heads):
            where[h] = (s, j)
    joined = jnp.concatenate(
        [pieces[where[h][1]][:, :, where[h][0]] for h in range(head_count)], axis=2
    )
    if group:
        stride = n_seq // group
        weight_5d = weight.reshape(group, per_dev, stride, head_dim, weight.shape[1])
        mixed_sum = None
        for j in range(per_dev):
            part = jnp.einsum(
                "tkid,ikdo->to",
                arrived[j][0].reshape(tokens, stride, group, head_dim),
                weight_5d[:, j],
                preferred_element_type=jnp.float32,
            )
            mixed_sum = part if mixed_sum is None else mixed_sum + part
        mixed = mixed_sum.astype(jnp.bfloat16)[None]
    else:
        mixed = jnp.dot(joined[0], weight, preferred_element_type=jnp.float32).astype(
            jnp.bfloat16
        )[None]
    back = [joined[i][None] for i in (1, 2, 3)]
    return (mixed, back[0], back[1], back[2], weight_grad)


def grid_cycle(rows, cols):
    cycle = [(r, 0) for r in range(rows)]
    for i, r in enumerate(range(rows - 1, -1, -1)):
        span = range(1, cols) if i % 2 == 0 else range(cols - 1, 0, -1)
        cycle.extend((r, c) for c in span)
    return cycle


def seq_ring(mesh):
    n_seq = mesh.shape["seq"]
    try:
        column = mesh.devices.reshape(-1, n_seq)[0]
        coords = [(d.coords[2], d.coords[0]) for d in column]
        zs = sorted({c[0] for c in coords})
        xs = sorted({c[1] for c in coords})
        where = {c: s for s, c in enumerate(coords)}
        if len(where) == n_seq and len(zs) * len(xs) == n_seq:
            if len(zs) % 2 == 0:
                cells = [(zs[r], xs[c]) for r, c in grid_cycle(len(zs), len(xs))]
            else:
                cells = [(zs[c], xs[r]) for r, c in grid_cycle(len(xs), len(zs))]
            order = [where[c] for c in cells]
            if sorted(order) == list(range(n_seq)):
                return tuple(order)
    except (AttributeError, IndexError, TypeError, KeyError):
        pass
    return tuple(range(n_seq))


def solution(mesh):
    ring = seq_ring(mesh)
    in_specs = (
        P("dp", "seq", None),
        P("dp", "seq", None),
        P("dp", "seq", None),
        P("dp", None),
        P("dp", "seq", None),
        P("dp", None, None, None),
        P("dp", None, None),
    )
    out_specs = (
        P("dp", "seq", None),
        P("dp", "seq", None),
        P("dp", "seq", None),
        P("dp", "seq", None),
        P(("dp", "seq"), None),
    )
    return jax.shard_map(
        functools.partial(per_device, ring), mesh=mesh, in_specs=in_specs, out_specs=out_specs, check_vma=False
    )
```

```python
import functools

import jax
import jax.numpy as jnp
from jax import lax
from jax.sharding import PartitionSpec as P

NEG = -1e30


def block_mask(blocks, live):
    number = blocks.shape[1]
    rows = jnp.arange(number, dtype=jnp.int32)[:, None]
    cols = jnp.arange(number, dtype=jnp.int32)[None, :]
    window = jnp.abs(rows - cols) <= 1
    far_pos = jnp.arange(blocks.shape[2], dtype=jnp.int32)
    far_used = far_pos[None, None, :] < live[:, :, None]
    hits = (blocks[:, :, :, None] == cols[None, None, :, :]) & far_used[:, :, :, None]
    return window[None] | jnp.any(hits, axis=2)


def head_forward(q, k, v, mask, number):
    length, head_dim = q.shape
    rows = length // number
    scale = head_dim ** (-0.5)
    qb = q.reshape(number, rows, head_dim)
    visible = jnp.repeat(mask, rows, axis=1)[:, None, :]
    raw = jnp.einsum("bqd,kd->bqk", qb, k, preferred_element_type=jnp.float32) * scale
    scores = jnp.where(visible, raw, NEG)
    row_max = jnp.max(scores, axis=-1, keepdims=True)
    log_total = row_max + jnp.log(jnp.sum(jnp.exp(scores - row_max), axis=-1, keepdims=True))
    softmax_w = jnp.exp(scores - log_total)
    probs = softmax_w.astype(jnp.bfloat16)
    attention = jnp.einsum("bqk,kd->bqd", probs, v, preferred_element_type=jnp.float32).astype(
        jnp.bfloat16
    )
    return softmax_w, attention


def head_backward(q, k, v, g, softmax_w, attention, number):
    length, head_dim = q.shape
    rows = length // number
    scale = head_dim ** (-0.5)
    qb = q.reshape(number, rows, head_dim)
    gb = g.reshape(number, rows, head_dim)
    probs = softmax_w.astype(jnp.bfloat16)
    row_dots = jnp.sum(
        gb.astype(jnp.float32) * attention.astype(jnp.float32), axis=-1, keepdims=True
    )
    grad_probs = jnp.einsum("bqd,kd->bqk", gb, v, preferred_element_type=jnp.float32)
    dscore = (softmax_w * (grad_probs - row_dots)).astype(jnp.bfloat16)
    grad_q = scale * jnp.einsum("bqk,kd->bqd", dscore, k, preferred_element_type=jnp.float32)
    grad_k = scale * jnp.einsum("bqk,bqd->kd", dscore, qb, preferred_element_type=jnp.float32)
    grad_v = jnp.einsum("bqk,bqd->kd", probs, gb, preferred_element_type=jnp.float32)
    return (
        attention.reshape(length, head_dim),
        grad_q.reshape(length, head_dim).astype(jnp.bfloat16),
        grad_k.astype(jnp.bfloat16),
        grad_v.astype(jnp.bfloat16),
    )


def ring_gather(block, ring, axis):
    n = len(ring)
    position = [0] * n
    for p, member in enumerate(ring):
        position[member] = p
    forward = [(ring[p], ring[(p + 1) % n]) for p in range(n)]
    backward = [(ring[p], ring[(p - 1) % n]) for p in range(n)]
    ring_arr = jnp.array(ring, jnp.int32)
    me = lax.axis_index(axis)
    p = jnp.array(position, jnp.int32)[me]
    out = jnp.zeros((n,) + block.shape, block.dtype)
    out = lax.dynamic_update_index_in_dim(out, block, me, 0)
    ahead, behind = block, block
    n_fwd = n // 2
    n_bwd = n - 1 - n_fwd
    for k in range(1, n_fwd + 1):
        ahead = lax.ppermute(ahead, axis, forward)
        out = lax.dynamic_update_index_in_dim(out, ahead, ring_arr[(p - k) % n], 0)
        if k <= n_bwd:
            behind = lax.ppermute(behind, axis, backward)
            out = lax.dynamic_update_index_in_dim(out, behind, ring_arr[(p + k) % n], 0)
    return out.reshape((n * block.shape[0],) + block.shape[1:])


def permute_all_to_all(x, ring, axis, split_axis, concat_axis):
    n = len(ring)
    position = [0] * n
    for p, member in enumerate(ring):
        position[member] = p
    ring_arr = jnp.array(ring, jnp.int32)
    me = lax.axis_index(axis)
    p = jnp.array(position, jnp.int32)[me]
    piece = x.shape[split_axis] // n
    shape = list(x.shape)
    shape[split_axis] = piece
    shape[concat_axis] = shape[concat_axis] * n
    out = jnp.zeros(shape, x.dtype)
    span = x.shape[concat_axis]
    own = lax.dynamic_slice_in_dim(x, me * piece, piece, split_axis)
    out = lax.dynamic_update_slice_in_dim(out, own, me * span, concat_axis)
    for k in range(1, n):
        perm = [(ring[q], ring[(q + k) % n]) for q in range(n)]
        dest = ring_arr[(p + k) % n]
        sent = lax.dynamic_slice_in_dim(x, dest * piece, piece, split_axis)
        got = lax.ppermute(sent, axis, perm)
        src = ring_arr[(p - k) % n]
        out = lax.dynamic_update_slice_in_dim(out, got, src * span, concat_axis)
    return out


def head_plan(n_dp, n_seq, head_count, head_dim, features):
    per_dev = head_count // n_seq
    rows = features // (n_dp * n_seq)
    group = head_dim // rows if rows and head_dim % rows == 0 else 0
    if group and n_seq % group == 0 and n_dp == group * per_dev:
        stride = n_seq // group
        plan = [
            [stride * ((s % group) * per_dev + j) + s // group for j in range(per_dev)]
            for s in range(n_seq)
        ]
        return plan, group, rows
    return [[s * per_dev + j for j in range(per_dev)] for s in range(n_seq)], 0, rows


def per_device(ring, query, keys, values, out_weight, grad_out, far_blocks, far_live):
    n_dp = lax.axis_size("dp")
    n_seq = lax.axis_size("seq")
    s_idx = lax.axis_index("seq")
    head_count = far_blocks.shape[1]
    per_dev = head_count // n_seq
    features = query.shape[2]
    head_dim = features // head_count
    number = far_blocks.shape[2]
    plan, group, rows = head_plan(n_dp, n_seq, head_count, head_dim, features)
    order = [h for heads in plan for h in heads]
    plan_arr = jnp.array(plan, jnp.int32)
    my_heads = plan_arr[s_idx]

    stacked = jnp.stack([query[0], keys[0], values[0]])
    tokens = stacked.shape[1]
    by_head = stacked.reshape(3, tokens, head_count, head_dim)
    stacked = jnp.stack([by_head[:, :, h] for h in order], axis=2).reshape(3, tokens, features)
    heads_qkv = lax.all_to_all(stacked, "seq", split_axis=2, concat_axis=1, tiled=True)
    length = heads_qkv.shape[1]

    weight = lax.all_gather(out_weight, "dp", axis=0, tiled=True)
    weight_heads = weight.reshape(head_count, head_dim, weight.shape[1])
    grad_doc = ring_gather(grad_out[0], ring, "seq")
    weight_rows = jnp.concatenate(
        [lax.dynamic_index_in_dim(weight_heads, my_heads[j], 0, False) for j in range(per_dev)]
    )
    grad_heads = lax.dot_general(
        grad_doc, weight_rows, (((1,), (1,)), ((), ())), preferred_element_type=jnp.float32
    ).astype(jnp.bfloat16)

    blocks_dev = jnp.stack(
        [lax.dynamic_index_in_dim(far_blocks[0], my_heads[j], 0, False) for j in range(per_dev)]
    )
    live_dev = jnp.stack(
        [lax.dynamic_index_in_dim(far_live[0], my_heads[j], 0, False) for j in range(per_dev)]
    )
    mask = block_mask(blocks_dev, live_dev)

    def head_cols(array, head):
        return array[:, head * head_dim : (head + 1) * head_dim]

    forward = [
        head_forward(
            head_cols(heads_qkv[0], j), head_cols(heads_qkv[1], j), head_cols(heads_qkv[2], j),
            mask[j], number,
        )
        for j in range(per_dev)
    ]
    attn_heads = jnp.stack([f[1].reshape(length, head_dim) for f in forward], axis=1)

    norm_factor = (n_dp * query.shape[0] * length) ** (-0.5)
    if group:
        me = s_idx % group
        sub = attn_heads.reshape(length, per_dev, group, rows)
        slots = jnp.zeros((length, group, per_dev, rows), attn_heads.dtype)
        slots = lax.dynamic_update_index_in_dim(
            slots, lax.dynamic_index_in_dim(sub, me, 2, False), me, 1
        )
        for shift in range(1, group):
            perm = [
                (base + i, base + (i + shift) % group)
                for base in range(0, n_seq, group)
                for i in range(group)
            ]
            target = (me + shift) % group
            sent = lax.dynamic_index_in_dim(sub, target, 2, False)
            got = lax.ppermute(sent, "seq", perm)
            source = (me - shift) % group
            slots = lax.dynamic_update_index_in_dim(slots, got, source, 1)
        mine = slots.reshape(length, n_dp * rows)
        partial = lax.dot_general(
            mine, grad_doc, (((0,), (0,)), ((), ())), preferred_element_type=jnp.float32
        )

        def weight_grad_of(partial):
            summed = lax.psum_scatter(
                partial.astype(jnp.bfloat16), "dp", scatter_dimension=0, tiled=True
            )
            return summed.astype(jnp.float32)
    else:
        partial = lax.dot_general(
            attn_heads.reshape(length, per_dev * head_dim),
            grad_doc,
            (((0,), (0,)), ((), ())),
            preferred_element_type=jnp.float32,
        )

        def weight_grad_of(partial):
            reduced = lax.psum_scatter(partial, "dp", scatter_dimension=0, tiled=True)
            perm = []
            for d in range(n_dp):
                for s in range(n_seq):
                    perm.append((d * n_seq + s, s * n_dp + d))
            return lax.ppermute(reduced, ("dp", "seq"), perm=perm)
    partial, grad_heads = lax.optimization_barrier((partial * norm_factor, grad_heads))
    weight_grad = weight_grad_of(partial)

    results = [
        head_backward(
            head_cols(heads_qkv[0], j), head_cols(heads_qkv[1], j), head_cols(heads_qkv[2], j),
            head_cols(grad_heads, j), forward[j][0], forward[j][1], number,
        )
        for j in range(per_dev)
    ]
    arrived = [
        lax.all_to_all(jnp.stack(r), "seq", split_axis=1, concat_axis=2, tiled=True)
        if j == 0
        else permute_all_to_all(jnp.stack(r), ring, "seq", 1, 2)
        for j, r in enumerate(results)
    ]
    pieces = [a.reshape(4, tokens, n_seq, head_dim) for a in arrived]
    where = {}
    for s, heads in enumerate(plan):
        for j, h in enumerate(heads):
            where[h] = (s, j)
    joined = jnp.concatenate(
        [pieces[where[h][1]][:, :, where[h][0]] for h in range(head_count)], axis=2
    )
    mixed = jnp.dot(joined[0], weight, preferred_element_type=jnp.float32).astype(jnp.bfloat16)[
        None
    ]
    back = [joined[i][None] for i in (1, 2, 3)]
    return (mixed, back[0], back[1], back[2], weight_grad)


def grid_cycle(rows, cols):
    cycle = [(r, 0) for r in range(rows)]
    for i, r in enumerate(range(rows - 1, -1, -1)):
        span = range(1, cols) if i % 2 == 0 else range(cols - 1, 0, -1)
        cycle.extend((r, c) for c in span)
    return cycle


def seq_ring(mesh):
    n_seq = mesh.shape["seq"]
    try:
        column = mesh.devices.reshape(-1, n_seq)[0]
        coords = [(d.coords[2], d.coords[0]) for d in column]
        zs = sorted({c[0] for c in coords})
        xs = sorted({c[1] for c in coords})
        where = {c: s for s, c in enumerate(coords)}
        if len(where) == n_seq and len(zs) * len(xs) == n_seq:
            if len(zs) % 2 == 0:
                cells = [(zs[r], xs[c]) for r, c in grid_cycle(len(zs), len(xs))]
            else:
                cells = [(zs[c], xs[r]) for r, c in grid_cycle(len(xs), len(zs))]
            order = [where[c] for c in cells]
            if sorted(order) == list(range(n_seq)):
                return tuple(order)
    except (AttributeError, IndexError, TypeError, KeyError):
        pass
    return tuple(range(n_seq))


def solution(mesh):
    ring = seq_ring(mesh)
    in_specs = (
        P("dp", "seq", None),
        P("dp", "seq", None),
        P("dp", "seq", None),
        P("dp", None),
        P("dp", "seq", None),
        P("dp", None, None, None),
        P("dp", None, None),
    )
    out_specs = (
        P("dp", "seq", None),
        P("dp", "seq", None),
        P("dp", "seq", None),
        P("dp", "seq", None),
        P(("dp", "seq"), None),
    )
    return jax.shard_map(
        functools.partial(per_device, ring), mesh=mesh, in_specs=in_specs, out_specs=out_specs, check_vma=False
    )
```

```python
import functools

import jax
import jax.numpy as jnp
from jax import lax
from jax.sharding import PartitionSpec as P

NEG = -1e30


def block_mask(blocks, live):
    number = blocks.shape[1]
    rows = jnp.arange(number, dtype=jnp.int32)[:, None]
    cols = jnp.arange(number, dtype=jnp.int32)[None, :]
    window = jnp.abs(rows - cols) <= 1
    far_pos = jnp.arange(blocks.shape[2], dtype=jnp.int32)
    far_used = far_pos[None, None, :] < live[:, :, None]
    hits = (blocks[:, :, :, None] == cols[None, None, :, :]) & far_used[:, :, :, None]
    return window[None] | jnp.any(hits, axis=2)


def head_forward(q, k, v, mask, number):
    length, head_dim = q.shape
    rows = length // number
    scale = head_dim ** (-0.5)
    qb = q.reshape(number, rows, head_dim)
    visible = jnp.repeat(mask, rows, axis=1)[:, None, :]
    raw = jnp.einsum("bqd,kd->bqk", qb, k, preferred_element_type=jnp.float32) * scale
    scores = jnp.where(visible, raw, NEG)
    row_max = jnp.max(scores, axis=-1, keepdims=True)
    log_total = row_max + jnp.log(jnp.sum(jnp.exp(scores - row_max), axis=-1, keepdims=True))
    softmax_w = jnp.exp(scores - log_total)
    probs = softmax_w.astype(jnp.bfloat16)
    attention = jnp.einsum("bqk,kd->bqd", probs, v, preferred_element_type=jnp.float32).astype(
        jnp.bfloat16
    )
    return softmax_w, attention


def head_backward(q, k, v, g, softmax_w, attention, number):
    length, head_dim = q.shape
    rows = length // number
    scale = head_dim ** (-0.5)
    qb = q.reshape(number, rows, head_dim)
    gb = g.reshape(number, rows, head_dim)
    probs = softmax_w.astype(jnp.bfloat16)
    row_dots = jnp.sum(
        gb.astype(jnp.float32) * attention.astype(jnp.float32), axis=-1, keepdims=True
    )
    grad_probs = jnp.einsum("bqd,kd->bqk", gb, v, preferred_element_type=jnp.float32)
    dscore = (softmax_w * (grad_probs - row_dots)).astype(jnp.bfloat16)
    grad_q = scale * jnp.einsum("bqk,kd->bqd", dscore, k, preferred_element_type=jnp.float32)
    grad_k = scale * jnp.einsum("bqk,bqd->kd", dscore, qb, preferred_element_type=jnp.float32)
    grad_v = jnp.einsum("bqk,bqd->kd", probs, gb, preferred_element_type=jnp.float32)
    return (
        attention.reshape(length, head_dim),
        grad_q.reshape(length, head_dim).astype(jnp.bfloat16),
        grad_k.astype(jnp.bfloat16),
        grad_v.astype(jnp.bfloat16),
    )


def ring_gather(block, ring, axis):
    n = len(ring)
    position = [0] * n
    for p, member in enumerate(ring):
        position[member] = p
    forward = [(ring[p], ring[(p + 1) % n]) for p in range(n)]
    backward = [(ring[p], ring[(p - 1) % n]) for p in range(n)]
    ring_arr = jnp.array(ring, jnp.int32)
    me = lax.axis_index(axis)
    p = jnp.array(position, jnp.int32)[me]
    out = jnp.zeros((n,) + block.shape, block.dtype)
    out = lax.dynamic_update_index_in_dim(out, block, me, 0)
    ahead, behind = block, block
    n_fwd = n // 2
    n_bwd = n - 1 - n_fwd
    for k in range(1, n_fwd + 1):
        ahead = lax.ppermute(ahead, axis, forward)
        out = lax.dynamic_update_index_in_dim(out, ahead, ring_arr[(p - k) % n], 0)
        if k <= n_bwd:
            behind = lax.ppermute(behind, axis, backward)
            out = lax.dynamic_update_index_in_dim(out, behind, ring_arr[(p + k) % n], 0)
    return out.reshape((n * block.shape[0],) + block.shape[1:])


def head_plan(n_dp, n_seq, head_count, head_dim, features):
    per_dev = head_count // n_seq
    rows = features // (n_dp * n_seq)
    group = head_dim // rows if rows and head_dim % rows == 0 else 0
    if group and n_seq % group == 0 and n_dp == group * per_dev:
        stride = n_seq // group
        plan = [
            [stride * ((s % group) * per_dev + j) + s // group for j in range(per_dev)]
            for s in range(n_seq)
        ]
        return plan, group, rows
    return [[s * per_dev + j for j in range(per_dev)] for s in range(n_seq)], 0, rows


def per_device(ring, query, keys, values, out_weight, grad_out, far_blocks, far_live):
    n_dp = lax.axis_size("dp")
    n_seq = lax.axis_size("seq")
    s_idx = lax.axis_index("seq")
    head_count = far_blocks.shape[1]
    per_dev = head_count // n_seq
    features = query.shape[2]
    head_dim = features // head_count
    number = far_blocks.shape[2]
    plan, group, rows = head_plan(n_dp, n_seq, head_count, head_dim, features)
    order = [h for heads in plan for h in heads]
    plan_arr = jnp.array(plan, jnp.int32)
    my_heads = plan_arr[s_idx]

    stacked = jnp.stack([query[0], keys[0], values[0]])
    tokens = stacked.shape[1]
    by_head = stacked.reshape(3, tokens, head_count, head_dim)
    stacked = jnp.stack([by_head[:, :, h] for h in order], axis=2).reshape(3, tokens, features)
    heads_qkv = lax.all_to_all(stacked, "seq", split_axis=2, concat_axis=1, tiled=True)
    length = heads_qkv.shape[1]

    weight = lax.all_gather(out_weight, "dp", axis=0, tiled=True)
    weight_heads = weight.reshape(head_count, head_dim, weight.shape[1])
    grad_doc = ring_gather(grad_out[0], ring, "seq")
    weight_rows = jnp.concatenate(
        [lax.dynamic_index_in_dim(weight_heads, my_heads[j], 0, False) for j in range(per_dev)]
    )
    grad_heads = lax.dot_general(
        grad_doc, weight_rows, (((1,), (1,)), ((), ())), preferred_element_type=jnp.float32
    ).astype(jnp.bfloat16)

    blocks_dev = jnp.stack(
        [lax.dynamic_index_in_dim(far_blocks[0], my_heads[j], 0, False) for j in range(per_dev)]
    )
    live_dev = jnp.stack(
        [lax.dynamic_index_in_dim(far_live[0], my_heads[j], 0, False) for j in range(per_dev)]
    )
    mask = block_mask(blocks_dev, live_dev)

    def head_cols(array, head):
        return array[:, head * head_dim : (head + 1) * head_dim]

    forward = [
        head_forward(
            head_cols(heads_qkv[0], j), head_cols(heads_qkv[1], j), head_cols(heads_qkv[2], j),
            mask[j], number,
        )
        for j in range(per_dev)
    ]
    attn_heads = jnp.stack([f[1].reshape(length, head_dim) for f in forward], axis=1)

    norm_factor = (n_dp * query.shape[0] * length) ** (-0.5)
    if group:
        me = s_idx % group
        sub = attn_heads.reshape(length, per_dev, group, rows)
        slots = jnp.zeros((length, group, per_dev, rows), attn_heads.dtype)
        slots = lax.dynamic_update_index_in_dim(
            slots, lax.dynamic_index_in_dim(sub, me, 2, False), me, 1
        )
        for shift in range(1, group):
            perm = [
                (base + i, base + (i + shift) % group)
                for base in range(0, n_seq, group)
                for i in range(group)
            ]
            target = (me + shift) % group
            sent = lax.dynamic_index_in_dim(sub, target, 2, False)
            got = lax.ppermute(sent, "seq", perm)
            source = (me - shift) % group
            slots = lax.dynamic_update_index_in_dim(slots, got, source, 1)
        mine = slots.reshape(length, n_dp * rows)
        partial = lax.dot_general(
            mine, grad_doc, (((0,), (0,)), ((), ())), preferred_element_type=jnp.float32
        )

        def weight_grad_of(partial):
            summed = lax.psum_scatter(
                partial.astype(jnp.bfloat16), "dp", scatter_dimension=0, tiled=True
            )
            return summed.astype(jnp.float32)
    else:
        partial = lax.dot_general(
            attn_heads.reshape(length, per_dev * head_dim),
            grad_doc,
            (((0,), (0,)), ((), ())),
            preferred_element_type=jnp.float32,
        )

        def weight_grad_of(partial):
            reduced = lax.psum_scatter(partial, "dp", scatter_dimension=0, tiled=True)
            perm = []
            for d in range(n_dp):
                for s in range(n_seq):
                    perm.append((d * n_seq + s, s * n_dp + d))
            return lax.ppermute(reduced, ("dp", "seq"), perm=perm)
    partial, grad_heads = lax.optimization_barrier((partial * norm_factor, grad_heads))
    weight_grad = weight_grad_of(partial)

    results = [
        head_backward(
            head_cols(heads_qkv[0], j), head_cols(heads_qkv[1], j), head_cols(heads_qkv[2], j),
            head_cols(grad_heads, j), forward[j][0], forward[j][1], number,
        )
        for j in range(per_dev)
    ]
    stacked_out = jnp.stack(
        [jnp.concatenate([r[i] for r in results], axis=1) for i in range(4)]
    )
    arrived = lax.all_to_all(stacked_out, "seq", split_axis=1, concat_axis=2, tiled=True)
    pieces = arrived.reshape(4, tokens, n_seq, per_dev, head_dim)
    where = {}
    for s, heads in enumerate(plan):
        for j, h in enumerate(heads):
            where[h] = (s, j)
    joined = jnp.concatenate(
        [pieces[:, :, where[h][0], where[h][1]] for h in range(head_count)], axis=2
    )
    mixed = jnp.dot(joined[0], weight, preferred_element_type=jnp.float32).astype(jnp.bfloat16)[
        None
    ]
    back = [joined[i][None] for i in (1, 2, 3)]
    return (mixed, back[0], back[1], back[2], weight_grad)


def grid_cycle(rows, cols):
    cycle = [(r, 0) for r in range(rows)]
    for i, r in enumerate(range(rows - 1, -1, -1)):
        span = range(1, cols) if i % 2 == 0 else range(cols - 1, 0, -1)
        cycle.extend((r, c) for c in span)
    return cycle


def seq_ring(mesh):
    n_seq = mesh.shape["seq"]
    try:
        column = mesh.devices.reshape(-1, n_seq)[0]
        coords = [(d.coords[2], d.coords[0]) for d in column]
        zs = sorted({c[0] for c in coords})
        xs = sorted({c[1] for c in coords})
        where = {c: s for s, c in enumerate(coords)}
        if len(where) == n_seq and len(zs) * len(xs) == n_seq:
            if len(zs) % 2 == 0:
                cells = [(zs[r], xs[c]) for r, c in grid_cycle(len(zs), len(xs))]
            else:
                cells = [(zs[c], xs[r]) for r, c in grid_cycle(len(xs), len(zs))]
            order = [where[c] for c in cells]
            if sorted(order) == list(range(n_seq)):
                return tuple(order)
    except (AttributeError, IndexError, TypeError, KeyError):
        pass
    return tuple(range(n_seq))


def solution(mesh):
    ring = seq_ring(mesh)
    in_specs = (
        P("dp", "seq", None),
        P("dp", "seq", None),
        P("dp", "seq", None),
        P("dp", None),
        P("dp", "seq", None),
        P("dp", None, None, None),
        P("dp", None, None),
    )
    out_specs = (
        P("dp", "seq", None),
        P("dp", "seq", None),
        P("dp", "seq", None),
        P("dp", "seq", None),
        P(("dp", "seq"), None),
    )
    return jax.shard_map(
        functools.partial(per_device, ring), mesh=mesh, in_specs=in_specs, out_specs=out_specs, check_vma=False
    )
```

```python
import functools

import jax
import jax.numpy as jnp
from jax import lax
from jax.sharding import PartitionSpec as P

NEG = -1e30


def block_mask(blocks, live):
    number = blocks.shape[1]
    rows = jnp.arange(number, dtype=jnp.int32)[:, None]
    cols = jnp.arange(number, dtype=jnp.int32)[None, :]
    window = jnp.abs(rows - cols) <= 1
    far_pos = jnp.arange(blocks.shape[2], dtype=jnp.int32)
    far_used = far_pos[None, None, :] < live[:, :, None]
    hits = (blocks[:, :, :, None] == cols[None, None, :, :]) & far_used[:, :, :, None]
    return window[None] | jnp.any(hits, axis=2)


def head_forward(q, k, v, mask, number):
    length, head_dim = q.shape
    rows = length // number
    scale = head_dim ** (-0.5)
    qb = q.reshape(number, rows, head_dim)
    visible = jnp.repeat(mask, rows, axis=1)[:, None, :]
    raw = jnp.einsum("bqd,kd->bqk", qb, k, preferred_element_type=jnp.float32) * scale
    scores = jnp.where(visible, raw, NEG)
    row_max = jnp.max(scores, axis=-1, keepdims=True)
    log_total = row_max + jnp.log(jnp.sum(jnp.exp(scores - row_max), axis=-1, keepdims=True))
    softmax_w = jnp.exp(scores - log_total)
    probs = softmax_w.astype(jnp.bfloat16)
    attention = jnp.einsum("bqk,kd->bqd", probs, v, preferred_element_type=jnp.float32).astype(
        jnp.bfloat16
    )
    return softmax_w, attention


def head_backward(q, k, v, g, softmax_w, attention, number):
    length, head_dim = q.shape
    rows = length // number
    scale = head_dim ** (-0.5)
    qb = q.reshape(number, rows, head_dim)
    gb = g.reshape(number, rows, head_dim)
    probs = softmax_w.astype(jnp.bfloat16)
    row_dots = jnp.sum(
        gb.astype(jnp.float32) * attention.astype(jnp.float32), axis=-1, keepdims=True
    )
    grad_probs = jnp.einsum("bqd,kd->bqk", gb, v, preferred_element_type=jnp.float32)
    dscore = (softmax_w * (grad_probs - row_dots)).astype(jnp.bfloat16)
    grad_q = scale * jnp.einsum("bqk,kd->bqd", dscore, k, preferred_element_type=jnp.float32)
    grad_k = scale * jnp.einsum("bqk,bqd->kd", dscore, qb, preferred_element_type=jnp.float32)
    grad_v = jnp.einsum("bqk,bqd->kd", probs, gb, preferred_element_type=jnp.float32)
    return (
        attention.reshape(length, head_dim),
        grad_q.reshape(length, head_dim).astype(jnp.bfloat16),
        grad_k.astype(jnp.bfloat16),
        grad_v.astype(jnp.bfloat16),
    )


def ring_gather(block, ring, axis):
    n = len(ring)
    position = [0] * n
    for p, member in enumerate(ring):
        position[member] = p
    forward = [(ring[p], ring[(p + 1) % n]) for p in range(n)]
    backward = [(ring[p], ring[(p - 1) % n]) for p in range(n)]
    ring_arr = jnp.array(ring, jnp.int32)
    me = lax.axis_index(axis)
    p = jnp.array(position, jnp.int32)[me]
    out = jnp.zeros((n,) + block.shape, block.dtype)
    out = lax.dynamic_update_index_in_dim(out, block, me, 0)
    ahead, behind = block, block
    n_fwd = n // 2
    n_bwd = n - 1 - n_fwd
    for k in range(1, n_fwd + 1):
        ahead = lax.ppermute(ahead, axis, forward)
        out = lax.dynamic_update_index_in_dim(out, ahead, ring_arr[(p - k) % n], 0)
        if k <= n_bwd:
            behind = lax.ppermute(behind, axis, backward)
            out = lax.dynamic_update_index_in_dim(out, behind, ring_arr[(p + k) % n], 0)
    return out.reshape((n * block.shape[0],) + block.shape[1:])


def head_plan(n_dp, n_seq, head_count, head_dim, features):
    per_dev = head_count // n_seq
    rows = features // (n_dp * n_seq)
    group = head_dim // rows if rows and head_dim % rows == 0 else 0
    if group and n_seq % group == 0 and n_dp == group * per_dev:
        stride = n_seq // group
        plan = [
            [stride * ((s % group) * per_dev + j) + s // group for j in range(per_dev)]
            for s in range(n_seq)
        ]
        return plan, group, rows
    return [[s * per_dev + j for j in range(per_dev)] for s in range(n_seq)], 0, rows


def per_device(ring, query, keys, values, out_weight, grad_out, far_blocks, far_live):
    n_dp = lax.axis_size("dp")
    n_seq = lax.axis_size("seq")
    s_idx = lax.axis_index("seq")
    head_count = far_blocks.shape[1]
    per_dev = head_count // n_seq
    features = query.shape[2]
    head_dim = features // head_count
    number = far_blocks.shape[2]
    plan, group, rows = head_plan(n_dp, n_seq, head_count, head_dim, features)
    order = [h for heads in plan for h in heads]
    plan_arr = jnp.array(plan, jnp.int32)
    my_heads = plan_arr[s_idx]

    stacked = jnp.stack([query[0], keys[0], values[0]])
    tokens = stacked.shape[1]
    by_head = stacked.reshape(3, tokens, head_count, head_dim)
    stacked = jnp.stack([by_head[:, :, h] for h in order], axis=2).reshape(3, tokens, features)
    heads_qkv = lax.all_to_all(stacked, "seq", split_axis=2, concat_axis=1, tiled=True)
    length = heads_qkv.shape[1]

    weight = lax.all_gather(out_weight, "dp", axis=0, tiled=True)
    weight_heads = weight.reshape(head_count, head_dim, weight.shape[1])
    grad_doc = ring_gather(grad_out[0], ring, "seq")
    weight_rows = jnp.concatenate(
        [lax.dynamic_index_in_dim(weight_heads, my_heads[j], 0, False) for j in range(per_dev)]
    )
    grad_heads = lax.dot_general(
        grad_doc, weight_rows, (((1,), (1,)), ((), ())), preferred_element_type=jnp.float32
    ).astype(jnp.bfloat16)

    blocks_dev = jnp.stack(
        [lax.dynamic_index_in_dim(far_blocks[0], my_heads[j], 0, False) for j in range(per_dev)]
    )
    live_dev = jnp.stack(
        [lax.dynamic_index_in_dim(far_live[0], my_heads[j], 0, False) for j in range(per_dev)]
    )
    mask = block_mask(blocks_dev, live_dev)

    def head_cols(array, head):
        return array[:, head * head_dim : (head + 1) * head_dim]

    forward = [
        head_forward(
            head_cols(heads_qkv[0], j), head_cols(heads_qkv[1], j), head_cols(heads_qkv[2], j),
            mask[j], number,
        )
        for j in range(per_dev)
    ]
    attn_heads = jnp.stack([f[1].reshape(length, head_dim) for f in forward], axis=1)

    norm_factor = (n_dp * query.shape[0] * length) ** (-0.5)
    if group:
        me = s_idx % group
        sub = attn_heads.reshape(length, per_dev, group, rows)
        slots = jnp.zeros((length, group, per_dev, rows), attn_heads.dtype)
        slots = lax.dynamic_update_index_in_dim(
            slots, lax.dynamic_index_in_dim(sub, me, 2, False), me, 1
        )
        for shift in range(1, group):
            perm = [
                (base + i, base + (i + shift) % group)
                for base in range(0, n_seq, group)
                for i in range(group)
            ]
            target = (me + shift) % group
            sent = lax.dynamic_index_in_dim(sub, target, 2, False)
            got = lax.ppermute(sent, "seq", perm)
            source = (me - shift) % group
            slots = lax.dynamic_update_index_in_dim(slots, got, source, 1)
        mine = slots.reshape(length, n_dp * rows)
        partial = lax.dot_general(
            mine, grad_doc, (((0,), (0,)), ((), ())), preferred_element_type=jnp.float32
        )

        def weight_grad_of(partial):
            summed = lax.psum_scatter(
                partial.astype(jnp.bfloat16), "dp", scatter_dimension=0, tiled=True
            )
            return summed.astype(jnp.float32)
    else:
        partial = lax.dot_general(
            attn_heads.reshape(length, per_dev * head_dim),
            grad_doc,
            (((0,), (0,)), ((), ())),
            preferred_element_type=jnp.float32,
        )

        def weight_grad_of(partial):
            reduced = lax.psum_scatter(partial, "dp", scatter_dimension=0, tiled=True)
            perm = []
            for d in range(n_dp):
                for s in range(n_seq):
                    perm.append((d * n_seq + s, s * n_dp + d))
            return lax.ppermute(reduced, ("dp", "seq"), perm=perm)
    attention_out = lax.all_to_all(
        attn_heads.reshape(length, per_dev * head_dim), "seq", split_axis=0, concat_axis=1,
        tiled=True,
    )
    partial, grad_heads, attention_out = lax.optimization_barrier(
        (partial * norm_factor, grad_heads, attention_out)
    )
    weight_grad = weight_grad_of(partial)

    results = [
        head_backward(
            head_cols(heads_qkv[0], j), head_cols(heads_qkv[1], j), head_cols(heads_qkv[2], j),
            head_cols(grad_heads, j), forward[j][0], forward[j][1], number,
        )
        for j in range(per_dev)
    ]
    stacked_out = jnp.stack(
        [jnp.concatenate([r[i] for r in results], axis=1) for i in (1, 2, 3)]
    )
    arrived = lax.all_to_all(stacked_out, "seq", split_axis=1, concat_axis=2, tiled=True)
    pieces = arrived.reshape(3, tokens, n_seq, per_dev, head_dim)
    att_pieces = attention_out.reshape(tokens, n_seq, per_dev, head_dim)
    where = {}
    for s, heads in enumerate(plan):
        for j, h in enumerate(heads):
            where[h] = (s, j)
    attention = jnp.concatenate(
        [att_pieces[:, where[h][0], where[h][1]] for h in range(head_count)], axis=1
    )
    joined = jnp.concatenate(
        [pieces[:, :, where[h][0], where[h][1]] for h in range(head_count)], axis=2
    )
    mixed = jnp.dot(attention, weight, preferred_element_type=jnp.float32).astype(jnp.bfloat16)[
        None
    ]
    back = [joined[i][None] for i in (0, 1, 2)]
    return (mixed, back[0], back[1], back[2], weight_grad)


def grid_cycle(rows, cols):
    cycle = [(r, 0) for r in range(rows)]
    for i, r in enumerate(range(rows - 1, -1, -1)):
        span = range(1, cols) if i % 2 == 0 else range(cols - 1, 0, -1)
        cycle.extend((r, c) for c in span)
    return cycle


def seq_ring(mesh):
    n_seq = mesh.shape["seq"]
    try:
        column = mesh.devices.reshape(-1, n_seq)[0]
        coords = [(d.coords[2], d.coords[0]) for d in column]
        zs = sorted({c[0] for c in coords})
        xs = sorted({c[1] for c in coords})
        where = {c: s for s, c in enumerate(coords)}
        if len(where) == n_seq and len(zs) * len(xs) == n_seq:
            if len(zs) % 2 == 0:
                cells = [(zs[r], xs[c]) for r, c in grid_cycle(len(zs), len(xs))]
            else:
                cells = [(zs[c], xs[r]) for r, c in grid_cycle(len(xs), len(zs))]
            order = [where[c] for c in cells]
            if sorted(order) == list(range(n_seq)):
                return tuple(order)
    except (AttributeError, IndexError, TypeError, KeyError):
        pass
    return tuple(range(n_seq))


def solution(mesh):
    ring = seq_ring(mesh)
    in_specs = (
        P("dp", "seq", None),
        P("dp", "seq", None),
        P("dp", "seq", None),
        P("dp", None),
        P("dp", "seq", None),
        P("dp", None, None, None),
        P("dp", None, None),
    )
    out_specs = (
        P("dp", "seq", None),
        P("dp", "seq", None),
        P("dp", "seq", None),
        P("dp", "seq", None),
        P(("dp", "seq"), None),
    )
    return jax.shard_map(
        functools.partial(per_device, ring), mesh=mesh, in_specs=in_specs, out_specs=out_specs, check_vma=False
    )
```

```python
import functools

import jax
import jax.numpy as jnp
from jax import lax
from jax.sharding import PartitionSpec as P

NEG = -1e30


def block_mask(blocks, live):
    number = blocks.shape[1]
    rows = jnp.arange(number, dtype=jnp.int32)[:, None]
    cols = jnp.arange(number, dtype=jnp.int32)[None, :]
    window = jnp.abs(rows - cols) <= 1
    far_pos = jnp.arange(blocks.shape[2], dtype=jnp.int32)
    far_used = far_pos[None, None, :] < live[:, :, None]
    hits = (blocks[:, :, :, None] == cols[None, None, :, :]) & far_used[:, :, :, None]
    return window[None] | jnp.any(hits, axis=2)


def head_forward(q, k, v, mask, number):
    length, head_dim = q.shape
    rows = length // number
    scale = head_dim ** (-0.5)
    qb = q.reshape(number, rows, head_dim)
    visible = jnp.repeat(mask, rows, axis=1)[:, None, :]
    raw = jnp.einsum("bqd,kd->bqk", qb, k, preferred_element_type=jnp.float32) * scale
    scores = jnp.where(visible, raw, NEG)
    row_max = jnp.max(scores, axis=-1, keepdims=True)
    log_total = row_max + jnp.log(jnp.sum(jnp.exp(scores - row_max), axis=-1, keepdims=True))
    softmax_w = jnp.exp(scores - log_total)
    probs = softmax_w.astype(jnp.bfloat16)
    attention = jnp.einsum("bqk,kd->bqd", probs, v, preferred_element_type=jnp.float32).astype(
        jnp.bfloat16
    )
    return softmax_w, attention


def head_backward(q, k, v, g, softmax_w, attention, number):
    length, head_dim = q.shape
    rows = length // number
    scale = head_dim ** (-0.5)
    qb = q.reshape(number, rows, head_dim)
    gb = g.reshape(number, rows, head_dim)
    probs = softmax_w.astype(jnp.bfloat16)
    row_dots = jnp.sum(
        gb.astype(jnp.float32) * attention.astype(jnp.float32), axis=-1, keepdims=True
    )
    grad_probs = jnp.einsum("bqd,kd->bqk", gb, v, preferred_element_type=jnp.float32)
    dscore = (softmax_w * (grad_probs - row_dots)).astype(jnp.bfloat16)
    grad_q = scale * jnp.einsum("bqk,kd->bqd", dscore, k, preferred_element_type=jnp.float32)
    grad_k = scale * jnp.einsum("bqk,bqd->kd", dscore, qb, preferred_element_type=jnp.float32)
    grad_v = jnp.einsum("bqk,bqd->kd", probs, gb, preferred_element_type=jnp.float32)
    return (
        attention.reshape(length, head_dim),
        grad_q.reshape(length, head_dim).astype(jnp.bfloat16),
        grad_k.astype(jnp.bfloat16),
        grad_v.astype(jnp.bfloat16),
    )


def ring_gather(block, ring, axis):
    n = len(ring)
    position = [0] * n
    for p, member in enumerate(ring):
        position[member] = p
    forward = [(ring[p], ring[(p + 1) % n]) for p in range(n)]
    backward = [(ring[p], ring[(p - 1) % n]) for p in range(n)]
    ring_arr = jnp.array(ring, jnp.int32)
    me = lax.axis_index(axis)
    p = jnp.array(position, jnp.int32)[me]
    out = jnp.zeros((n,) + block.shape, block.dtype)
    out = lax.dynamic_update_index_in_dim(out, block, me, 0)
    ahead, behind = block, block
    n_fwd = n // 2
    n_bwd = n - 1 - n_fwd
    half = block.shape[-1] // 2
    for k in range(1, n_fwd + 1):
        if k > n_bwd and half and block.shape[-1] % 2 == 0:
            idx = ring_arr[(p - k) % n]
            front = lax.ppermute(ahead[..., :half], axis, forward)
            back = lax.ppermute(behind[..., half:], axis, backward)
            zero = jnp.zeros((), jnp.int32)
            out = lax.dynamic_update_slice(out, front[None], (idx, zero, zero))
            out = lax.dynamic_update_slice(out, back[None], (idx, zero, zero + half))
            break
        ahead = lax.ppermute(ahead, axis, forward)
        out = lax.dynamic_update_index_in_dim(out, ahead, ring_arr[(p - k) % n], 0)
        if k <= n_bwd:
            behind = lax.ppermute(behind, axis, backward)
            out = lax.dynamic_update_index_in_dim(out, behind, ring_arr[(p + k) % n], 0)
    return out.reshape((n * block.shape[0],) + block.shape[1:])


def head_plan(n_dp, n_seq, head_count, head_dim, features):
    per_dev = head_count // n_seq
    rows = features // (n_dp * n_seq)
    group = head_dim // rows if rows and head_dim % rows == 0 else 0
    if group and n_seq % group == 0 and n_dp == group * per_dev:
        stride = n_seq // group
        plan = [
            [stride * ((s % group) * per_dev + j) + s // group for j in range(per_dev)]
            for s in range(n_seq)
        ]
        return plan, group, rows
    return [[s * per_dev + j for j in range(per_dev)] for s in range(n_seq)], 0, rows


def per_device(ring, query, keys, values, out_weight, grad_out, far_blocks, far_live):
    n_dp = lax.axis_size("dp")
    n_seq = lax.axis_size("seq")
    s_idx = lax.axis_index("seq")
    head_count = far_blocks.shape[1]
    per_dev = head_count // n_seq
    features = query.shape[2]
    head_dim = features // head_count
    number = far_blocks.shape[2]
    plan, group, rows = head_plan(n_dp, n_seq, head_count, head_dim, features)
    order = [h for heads in plan for h in heads]
    plan_arr = jnp.array(plan, jnp.int32)
    my_heads = plan_arr[s_idx]

    stacked = jnp.stack([query[0], keys[0], values[0]])
    tokens = stacked.shape[1]
    by_head = stacked.reshape(3, tokens, head_count, head_dim)
    stacked = jnp.stack([by_head[:, :, h] for h in order], axis=2).reshape(3, tokens, features)
    heads_qkv = lax.all_to_all(stacked, "seq", split_axis=2, concat_axis=1, tiled=True)
    length = heads_qkv.shape[1]

    weight = lax.all_gather(out_weight, "dp", axis=0, tiled=True)
    weight_heads = weight.reshape(head_count, head_dim, weight.shape[1])
    grad_doc = ring_gather(grad_out[0], ring, "seq")
    weight_rows = jnp.concatenate(
        [lax.dynamic_index_in_dim(weight_heads, my_heads[j], 0, False) for j in range(per_dev)]
    )
    grad_heads = lax.dot_general(
        grad_doc, weight_rows, (((1,), (1,)), ((), ())), preferred_element_type=jnp.float32
    ).astype(jnp.bfloat16)

    blocks_dev = jnp.stack(
        [lax.dynamic_index_in_dim(far_blocks[0], my_heads[j], 0, False) for j in range(per_dev)]
    )
    live_dev = jnp.stack(
        [lax.dynamic_index_in_dim(far_live[0], my_heads[j], 0, False) for j in range(per_dev)]
    )
    mask = block_mask(blocks_dev, live_dev)

    def head_cols(array, head):
        return array[:, head * head_dim : (head + 1) * head_dim]

    forward = [
        head_forward(
            head_cols(heads_qkv[0], j), head_cols(heads_qkv[1], j), head_cols(heads_qkv[2], j),
            mask[j], number,
        )
        for j in range(per_dev)
    ]
    attn_heads = jnp.stack([f[1].reshape(length, head_dim) for f in forward], axis=1)

    norm_factor = (n_dp * query.shape[0] * length) ** (-0.5)
    if group:
        me = s_idx % group
        sub = attn_heads.reshape(length, per_dev, group, rows)
        slots = jnp.zeros((length, group, per_dev, rows), attn_heads.dtype)
        slots = lax.dynamic_update_index_in_dim(
            slots, lax.dynamic_index_in_dim(sub, me, 2, False), me, 1
        )
        for shift in range(1, group):
            perm = [
                (base + i, base + (i + shift) % group)
                for base in range(0, n_seq, group)
                for i in range(group)
            ]
            target = (me + shift) % group
            sent = lax.dynamic_index_in_dim(sub, target, 2, False)
            got = lax.ppermute(sent, "seq", perm)
            source = (me - shift) % group
            slots = lax.dynamic_update_index_in_dim(slots, got, source, 1)
        mine = slots.reshape(length, n_dp * rows)
        partial = lax.dot_general(
            mine, grad_doc, (((0,), (0,)), ((), ())), preferred_element_type=jnp.float32
        )

        def weight_grad_of(partial):
            summed = lax.psum_scatter(
                partial.astype(jnp.bfloat16), "dp", scatter_dimension=0, tiled=True
            )
            return summed.astype(jnp.float32)
    else:
        partial = lax.dot_general(
            attn_heads.reshape(length, per_dev * head_dim),
            grad_doc,
            (((0,), (0,)), ((), ())),
            preferred_element_type=jnp.float32,
        )

        def weight_grad_of(partial):
            reduced = lax.psum_scatter(partial, "dp", scatter_dimension=0, tiled=True)
            perm = []
            for d in range(n_dp):
                for s in range(n_seq):
                    perm.append((d * n_seq + s, s * n_dp + d))
            return lax.ppermute(reduced, ("dp", "seq"), perm=perm)
    partial, grad_heads = lax.optimization_barrier((partial * norm_factor, grad_heads))
    weight_grad = weight_grad_of(partial)

    results = [
        head_backward(
            head_cols(heads_qkv[0], j), head_cols(heads_qkv[1], j), head_cols(heads_qkv[2], j),
            head_cols(grad_heads, j), forward[j][0], forward[j][1], number,
        )
        for j in range(per_dev)
    ]
    arrived = [
        lax.all_to_all(jnp.stack(r), "seq", split_axis=1, concat_axis=2, tiled=True)
        for r in results
    ]
    pieces = [a.reshape(4, tokens, n_seq, head_dim) for a in arrived]
    where = {}
    for s, heads in enumerate(plan):
        for j, h in enumerate(heads):
            where[h] = (s, j)
    joined = jnp.concatenate(
        [pieces[where[h][1]][:, :, where[h][0]] for h in range(head_count)], axis=2
    )
    mixed = jnp.dot(joined[0], weight, preferred_element_type=jnp.float32).astype(jnp.bfloat16)[
        None
    ]
    back = [joined[i][None] for i in (1, 2, 3)]
    return (mixed, back[0], back[1], back[2], weight_grad)


def grid_cycle(rows, cols):
    cycle = [(r, 0) for r in range(rows)]
    for i, r in enumerate(range(rows - 1, -1, -1)):
        span = range(1, cols) if i % 2 == 0 else range(cols - 1, 0, -1)
        cycle.extend((r, c) for c in span)
    return cycle


def seq_ring(mesh):
    n_seq = mesh.shape["seq"]
    try:
        column = mesh.devices.reshape(-1, n_seq)[0]
        coords = [(d.coords[2], d.coords[0]) for d in column]
        zs = sorted({c[0] for c in coords})
        xs = sorted({c[1] for c in coords})
        where = {c: s for s, c in enumerate(coords)}
        if len(where) == n_seq and len(zs) * len(xs) == n_seq:
            if len(zs) % 2 == 0:
                cells = [(zs[r], xs[c]) for r, c in grid_cycle(len(zs), len(xs))]
            else:
                cells = [(zs[c], xs[r]) for r, c in grid_cycle(len(xs), len(zs))]
            order = [where[c] for c in cells]
            if sorted(order) == list(range(n_seq)):
                return tuple(order)
    except (AttributeError, IndexError, TypeError, KeyError):
        pass
    return tuple(range(n_seq))


def solution(mesh):
    ring = seq_ring(mesh)
    in_specs = (
        P("dp", "seq", None),
        P("dp", "seq", None),
        P("dp", "seq", None),
        P("dp", None),
        P("dp", "seq", None),
        P("dp", None, None, None),
        P("dp", None, None),
    )
    out_specs = (
        P("dp", "seq", None),
        P("dp", "seq", None),
        P("dp", "seq", None),
        P("dp", "seq", None),
        P(("dp", "seq"), None),
    )
    return jax.shard_map(
        functools.partial(per_device, ring), mesh=mesh, in_specs=in_specs, out_specs=out_specs, check_vma=False
    )
```

```python
import functools

import jax
import jax.numpy as jnp
from jax import lax
from jax.sharding import PartitionSpec as P

NEG = -1e30


def block_mask(blocks, live):
    number = blocks.shape[1]
    rows = jnp.arange(number, dtype=jnp.int32)[:, None]
    cols = jnp.arange(number, dtype=jnp.int32)[None, :]
    window = jnp.abs(rows - cols) <= 1
    far_pos = jnp.arange(blocks.shape[2], dtype=jnp.int32)
    far_used = far_pos[None, None, :] < live[:, :, None]
    hits = (blocks[:, :, :, None] == cols[None, None, :, :]) & far_used[:, :, :, None]
    return window[None] | jnp.any(hits, axis=2)


def head_forward(q, k, v, mask, number):
    length, head_dim = q.shape
    rows = length // number
    scale = head_dim ** (-0.5)
    qb = q.reshape(number, rows, head_dim)
    visible = jnp.repeat(mask, rows, axis=1)[:, None, :]
    raw = jnp.einsum("bqd,kd->bqk", qb, k, preferred_element_type=jnp.float32) * scale
    scores = jnp.where(visible, raw, NEG)
    row_max = jnp.max(scores, axis=-1, keepdims=True)
    log_total = row_max + jnp.log(jnp.sum(jnp.exp(scores - row_max), axis=-1, keepdims=True))
    softmax_w = jnp.exp(scores - log_total)
    probs = softmax_w.astype(jnp.bfloat16)
    attention = jnp.einsum("bqk,kd->bqd", probs, v, preferred_element_type=jnp.float32).astype(
        jnp.bfloat16
    )
    return softmax_w, attention


def head_backward(q, k, v, g, softmax_w, attention, number):
    length, head_dim = q.shape
    rows = length // number
    scale = head_dim ** (-0.5)
    qb = q.reshape(number, rows, head_dim)
    gb = g.reshape(number, rows, head_dim)
    probs = softmax_w.astype(jnp.bfloat16)
    row_dots = jnp.sum(
        gb.astype(jnp.float32) * attention.astype(jnp.float32), axis=-1, keepdims=True
    )
    grad_probs = jnp.einsum("bqd,kd->bqk", gb, v, preferred_element_type=jnp.float32)
    dscore = (softmax_w * (grad_probs - row_dots)).astype(jnp.bfloat16)
    grad_q = scale * jnp.einsum("bqk,kd->bqd", dscore, k, preferred_element_type=jnp.float32)
    grad_k = scale * jnp.einsum("bqk,bqd->kd", dscore, qb, preferred_element_type=jnp.float32)
    grad_v = jnp.einsum("bqk,bqd->kd", probs, gb, preferred_element_type=jnp.float32)
    return (
        attention.reshape(length, head_dim),
        grad_q.reshape(length, head_dim).astype(jnp.bfloat16),
        grad_k.astype(jnp.bfloat16),
        grad_v.astype(jnp.bfloat16),
    )


def ring_gather(block, ring, axis):
    n = len(ring)
    position = [0] * n
    for p, member in enumerate(ring):
        position[member] = p
    forward = [(ring[p], ring[(p + 1) % n]) for p in range(n)]
    backward = [(ring[p], ring[(p - 1) % n]) for p in range(n)]
    ring_arr = jnp.array(ring, jnp.int32)
    me = lax.axis_index(axis)
    p = jnp.array(position, jnp.int32)[me]
    out = jnp.zeros((n,) + block.shape, block.dtype)
    out = lax.dynamic_update_index_in_dim(out, block, me, 0)
    ahead, behind = block, block
    n_fwd = n // 2
    n_bwd = n - 1 - n_fwd
    for k in range(1, n_fwd + 1):
        ahead = lax.ppermute(ahead, axis, forward)
        out = lax.dynamic_update_index_in_dim(out, ahead, ring_arr[(p - k) % n], 0)
        if k <= n_bwd:
            behind = lax.ppermute(behind, axis, backward)
            out = lax.dynamic_update_index_in_dim(out, behind, ring_arr[(p + k) % n], 0)
    return out.reshape((n * block.shape[0],) + block.shape[1:])


def head_plan(n_dp, n_seq, head_count, head_dim, features):
    per_dev = head_count // n_seq
    rows = features // (n_dp * n_seq)
    group = head_dim // rows if rows and head_dim % rows == 0 else 0
    if group and n_seq % group == 0 and n_dp == group * per_dev:
        stride = n_seq // group
        plan = [
            [stride * ((s % group) * per_dev + j) + s // group for j in range(per_dev)]
            for s in range(n_seq)
        ]
        return plan, group, rows
    return [[s * per_dev + j for j in range(per_dev)] for s in range(n_seq)], 0, rows


def per_device(ring, query, keys, values, out_weight, grad_out, far_blocks, far_live):
    n_dp = lax.axis_size("dp")
    n_seq = lax.axis_size("seq")
    s_idx = lax.axis_index("seq")
    head_count = far_blocks.shape[1]
    per_dev = head_count // n_seq
    features = query.shape[2]
    head_dim = features // head_count
    number = far_blocks.shape[2]
    plan, group, rows = head_plan(n_dp, n_seq, head_count, head_dim, features)
    order = [h for heads in plan for h in heads]
    plan_arr = jnp.array(plan, jnp.int32)
    my_heads = plan_arr[s_idx]

    stacked = jnp.stack([query[0], keys[0], values[0]])
    tokens = stacked.shape[1]
    by_head = stacked.reshape(3, tokens, head_count, head_dim)
    stacked = jnp.stack([by_head[:, :, h] for h in order], axis=2).reshape(3, tokens, features)
    heads_qkv = lax.all_to_all(stacked, "seq", split_axis=2, concat_axis=1, tiled=True)
    length = heads_qkv.shape[1]

    weight = lax.all_gather(out_weight, "dp", axis=0, tiled=True)
    weight_heads = weight.reshape(head_count, head_dim, weight.shape[1])
    grad_doc = ring_gather(grad_out[0], ring, "seq")
    weight_rows = jnp.concatenate(
        [lax.dynamic_index_in_dim(weight_heads, my_heads[j], 0, False) for j in range(per_dev)]
    )
    grad_heads = lax.dot_general(
        grad_doc, weight_rows, (((1,), (1,)), ((), ())), preferred_element_type=jnp.float32
    ).astype(jnp.bfloat16)

    blocks_dev = jnp.stack(
        [lax.dynamic_index_in_dim(far_blocks[0], my_heads[j], 0, False) for j in range(per_dev)]
    )
    live_dev = jnp.stack(
        [lax.dynamic_index_in_dim(far_live[0], my_heads[j], 0, False) for j in range(per_dev)]
    )
    mask = block_mask(blocks_dev, live_dev)

    def head_cols(array, head):
        return array[:, head * head_dim : (head + 1) * head_dim]

    forward = [
        head_forward(
            head_cols(heads_qkv[0], j), head_cols(heads_qkv[1], j), head_cols(heads_qkv[2], j),
            mask[j], number,
        )
        for j in range(per_dev)
    ]
    attn_heads = jnp.stack([f[1].reshape(length, head_dim) for f in forward], axis=1)

    norm_factor = (n_dp * query.shape[0] * length) ** (-0.5)
    if group:
        me = s_idx % group
        sub = attn_heads.reshape(length, per_dev, group, rows)
        slots = jnp.zeros((length, group, per_dev, rows), attn_heads.dtype)
        slots = lax.dynamic_update_index_in_dim(
            slots, lax.dynamic_index_in_dim(sub, me, 2, False), me, 1
        )
        for shift in range(1, group):
            perm = [
                (base + i, base + (i + shift) % group)
                for base in range(0, n_seq, group)
                for i in range(group)
            ]
            target = (me + shift) % group
            sent = lax.dynamic_index_in_dim(sub, target, 2, False)
            got = lax.ppermute(sent, "seq", perm)
            source = (me - shift) % group
            slots = lax.dynamic_update_index_in_dim(slots, got, source, 1)
        mine = slots.reshape(length, n_dp * rows)
        partial = lax.dot_general(
            mine, grad_doc, (((0,), (0,)), ((), ())), preferred_element_type=jnp.float32
        )

        def weight_grad_of(partial):
            summed = lax.psum_scatter(
                partial.astype(jnp.bfloat16), "dp", scatter_dimension=0, tiled=True
            )
            return summed.astype(jnp.float32)
    else:
        partial = lax.dot_general(
            attn_heads.reshape(length, per_dev * head_dim),
            grad_doc,
            (((0,), (0,)), ((), ())),
            preferred_element_type=jnp.float32,
        )

        def weight_grad_of(partial):
            reduced = lax.psum_scatter(partial, "dp", scatter_dimension=0, tiled=True)
            perm = []
            for d in range(n_dp):
                for s in range(n_seq):
                    perm.append((d * n_seq + s, s * n_dp + d))
            return lax.ppermute(reduced, ("dp", "seq"), perm=perm)
    partial, held_grads = lax.optimization_barrier((partial * norm_factor, grad_heads))
    weight_grad = weight_grad_of(partial)

    results = [
        head_backward(
            head_cols(heads_qkv[0], j), head_cols(heads_qkv[1], j), head_cols(heads_qkv[2], j),
            head_cols(grad_heads if j == 0 else held_grads, j), forward[j][0], forward[j][1],
            number,
        )
        for j in range(per_dev)
    ]
    arrived = [
        lax.all_to_all(jnp.stack(r), "seq", split_axis=1, concat_axis=2, tiled=True)
        for r in results
    ]
    pieces = [a.reshape(4, tokens, n_seq, head_dim) for a in arrived]
    where = {}
    for s, heads in enumerate(plan):
        for j, h in enumerate(heads):
            where[h] = (s, j)
    joined = jnp.concatenate(
        [pieces[where[h][1]][:, :, where[h][0]] for h in range(head_count)], axis=2
    )
    mixed = jnp.dot(joined[0], weight, preferred_element_type=jnp.float32).astype(jnp.bfloat16)[
        None
    ]
    back = [joined[i][None] for i in (1, 2, 3)]
    return (mixed, back[0], back[1], back[2], weight_grad)


def grid_cycle(rows, cols):
    cycle = [(r, 0) for r in range(rows)]
    for i, r in enumerate(range(rows - 1, -1, -1)):
        span = range(1, cols) if i % 2 == 0 else range(cols - 1, 0, -1)
        cycle.extend((r, c) for c in span)
    return cycle


def seq_ring(mesh):
    n_seq = mesh.shape["seq"]
    try:
        column = mesh.devices.reshape(-1, n_seq)[0]
        coords = [(d.coords[2], d.coords[0]) for d in column]
        zs = sorted({c[0] for c in coords})
        xs = sorted({c[1] for c in coords})
        where = {c: s for s, c in enumerate(coords)}
        if len(where) == n_seq and len(zs) * len(xs) == n_seq:
            if len(zs) % 2 == 0:
                cells = [(zs[r], xs[c]) for r, c in grid_cycle(len(zs), len(xs))]
            else:
                cells = [(zs[c], xs[r]) for r, c in grid_cycle(len(xs), len(zs))]
            order = [where[c] for c in cells]
            if sorted(order) == list(range(n_seq)):
                return tuple(order)
    except (AttributeError, IndexError, TypeError, KeyError):
        pass
    return tuple(range(n_seq))


def solution(mesh):
    ring = seq_ring(mesh)
    in_specs = (
        P("dp", "seq", None),
        P("dp", "seq", None),
        P("dp", "seq", None),
        P("dp", None),
        P("dp", "seq", None),
        P("dp", None, None, None),
        P("dp", None, None),
    )
    out_specs = (
        P("dp", "seq", None),
        P("dp", "seq", None),
        P("dp", "seq", None),
        P("dp", "seq", None),
        P(("dp", "seq"), None),
    )
    return jax.shard_map(
        functools.partial(per_device, ring), mesh=mesh, in_specs=in_specs, out_specs=out_specs, check_vma=False
    )
```

```python
import functools

import jax
import jax.numpy as jnp
from jax import lax
from jax.sharding import PartitionSpec as P

NEG = -1e30


def block_mask(blocks, live):
    number = blocks.shape[1]
    rows = jnp.arange(number, dtype=jnp.int32)[:, None]
    cols = jnp.arange(number, dtype=jnp.int32)[None, :]
    window = jnp.abs(rows - cols) <= 1
    far_pos = jnp.arange(blocks.shape[2], dtype=jnp.int32)
    far_used = far_pos[None, None, :] < live[:, :, None]
    hits = (blocks[:, :, :, None] == cols[None, None, :, :]) & far_used[:, :, :, None]
    return window[None] | jnp.any(hits, axis=2)


def head_forward(q, k, v, mask, number):
    length, head_dim = q.shape
    rows = length // number
    scale = head_dim ** (-0.5)
    qb = q.reshape(number, rows, head_dim)
    visible = jnp.repeat(mask, rows, axis=1)[:, None, :]
    raw = jnp.einsum("bqd,kd->bqk", qb, k, preferred_element_type=jnp.float32) * scale
    scores = jnp.where(visible, raw, NEG)
    row_max = jnp.max(scores, axis=-1, keepdims=True)
    log_total = row_max + jnp.log(jnp.sum(jnp.exp(scores - row_max), axis=-1, keepdims=True))
    softmax_w = jnp.exp(scores - log_total)
    probs = softmax_w.astype(jnp.bfloat16)
    attention = jnp.einsum("bqk,kd->bqd", probs, v, preferred_element_type=jnp.float32).astype(
        jnp.bfloat16
    )
    return softmax_w, attention


def head_backward(q, k, v, g, softmax_w, attention, number):
    length, head_dim = q.shape
    rows = length // number
    scale = head_dim ** (-0.5)
    qb = q.reshape(number, rows, head_dim)
    gb = g.reshape(number, rows, head_dim)
    probs = softmax_w.astype(jnp.bfloat16)
    row_dots = jnp.sum(
        gb.astype(jnp.float32) * attention.astype(jnp.float32), axis=-1, keepdims=True
    )
    grad_probs = jnp.einsum("bqd,kd->bqk", gb, v, preferred_element_type=jnp.float32)
    dscore = (softmax_w * (grad_probs - row_dots)).astype(jnp.bfloat16)
    grad_q = scale * jnp.einsum("bqk,kd->bqd", dscore, k, preferred_element_type=jnp.float32)
    grad_k = scale * jnp.einsum("bqk,bqd->kd", dscore, qb, preferred_element_type=jnp.float32)
    grad_v = jnp.einsum("bqk,bqd->kd", probs, gb, preferred_element_type=jnp.float32)
    return (
        attention.reshape(length, head_dim),
        grad_q.reshape(length, head_dim).astype(jnp.bfloat16),
        grad_k.astype(jnp.bfloat16),
        grad_v.astype(jnp.bfloat16),
    )


def ring_gather(block, ring, axis):
    n = len(ring)
    position = [0] * n
    for p, member in enumerate(ring):
        position[member] = p
    forward = [(ring[p], ring[(p + 1) % n]) for p in range(n)]
    backward = [(ring[p], ring[(p - 1) % n]) for p in range(n)]
    ring_arr = jnp.array(ring, jnp.int32)
    me = lax.axis_index(axis)
    p = jnp.array(position, jnp.int32)[me]
    out = jnp.zeros((n,) + block.shape, block.dtype)
    out = lax.dynamic_update_index_in_dim(out, block, me, 0)
    ahead, behind = block, block
    n_bwd = n // 2
    n_fwd = n - 1 - n_bwd
    for k in range(1, max(n_fwd, n_bwd) + 1):
        if k <= n_fwd:
            ahead = lax.ppermute(ahead, axis, forward)
            out = lax.dynamic_update_index_in_dim(out, ahead, ring_arr[(p - k) % n], 0)
        if k <= n_bwd:
            behind = lax.ppermute(behind, axis, backward)
            out = lax.dynamic_update_index_in_dim(out, behind, ring_arr[(p + k) % n], 0)
    return out.reshape((n * block.shape[0],) + block.shape[1:])


def head_plan(n_dp, n_seq, head_count, head_dim, features):
    per_dev = head_count // n_seq
    rows = features // (n_dp * n_seq)
    group = head_dim // rows if rows and head_dim % rows == 0 else 0
    if group and n_seq % group == 0 and n_dp == group * per_dev:
        stride = n_seq // group
        plan = [
            [stride * ((s % group) * per_dev + j) + s // group for j in range(per_dev)]
            for s in range(n_seq)
        ]
        return plan, group, rows
    return [[s * per_dev + j for j in range(per_dev)] for s in range(n_seq)], 0, rows


def per_device(ring, query, keys, values, out_weight, grad_out, far_blocks, far_live):
    n_dp = lax.axis_size("dp")
    n_seq = lax.axis_size("seq")
    s_idx = lax.axis_index("seq")
    head_count = far_blocks.shape[1]
    per_dev = head_count // n_seq
    features = query.shape[2]
    head_dim = features // head_count
    number = far_blocks.shape[2]
    plan, group, rows = head_plan(n_dp, n_seq, head_count, head_dim, features)
    order = [h for heads in plan for h in heads]
    plan_arr = jnp.array(plan, jnp.int32)
    my_heads = plan_arr[s_idx]

    stacked = jnp.stack([query[0], keys[0], values[0]])
    tokens = stacked.shape[1]
    by_head = stacked.reshape(3, tokens, head_count, head_dim)
    stacked = jnp.stack([by_head[:, :, h] for h in order], axis=2).reshape(3, tokens, features)
    heads_qkv = lax.all_to_all(stacked, "seq", split_axis=2, concat_axis=1, tiled=True)
    length = heads_qkv.shape[1]

    weight = lax.all_gather(out_weight, "dp", axis=0, tiled=True)
    weight_heads = weight.reshape(head_count, head_dim, weight.shape[1])
    grad_doc = ring_gather(grad_out[0], ring, "seq")
    weight_rows = jnp.concatenate(
        [lax.dynamic_index_in_dim(weight_heads, my_heads[j], 0, False) for j in range(per_dev)]
    )
    grad_heads = lax.dot_general(
        grad_doc, weight_rows, (((1,), (1,)), ((), ())), preferred_element_type=jnp.float32
    ).astype(jnp.bfloat16)

    blocks_dev = jnp.stack(
        [lax.dynamic_index_in_dim(far_blocks[0], my_heads[j], 0, False) for j in range(per_dev)]
    )
    live_dev = jnp.stack(
        [lax.dynamic_index_in_dim(far_live[0], my_heads[j], 0, False) for j in range(per_dev)]
    )
    mask = block_mask(blocks_dev, live_dev)

    def head_cols(array, head):
        return array[:, head * head_dim : (head + 1) * head_dim]

    forward = [
        head_forward(
            head_cols(heads_qkv[0], j), head_cols(heads_qkv[1], j), head_cols(heads_qkv[2], j),
            mask[j], number,
        )
        for j in range(per_dev)
    ]
    attn_heads = jnp.stack([f[1].reshape(length, head_dim) for f in forward], axis=1)

    norm_factor = (n_dp * query.shape[0] * length) ** (-0.5)
    if group:
        me = s_idx % group
        sub = attn_heads.reshape(length, per_dev, group, rows)
        slots = jnp.zeros((length, group, per_dev, rows), attn_heads.dtype)
        slots = lax.dynamic_update_index_in_dim(
            slots, lax.dynamic_index_in_dim(sub, me, 2, False), me, 1
        )
        for shift in range(1, group):
            perm = [
                (base + i, base + (i + shift) % group)
                for base in range(0, n_seq, group)
                for i in range(group)
            ]
            target = (me + shift) % group
            sent = lax.dynamic_index_in_dim(sub, target, 2, False)
            got = lax.ppermute(sent, "seq", perm)
            source = (me - shift) % group
            slots = lax.dynamic_update_index_in_dim(slots, got, source, 1)
        mine = slots.reshape(length, n_dp * rows)
        partial = lax.dot_general(
            mine, grad_doc, (((0,), (0,)), ((), ())), preferred_element_type=jnp.float32
        )

        def weight_grad_of(partial):
            summed = lax.psum_scatter(
                partial.astype(jnp.bfloat16), "dp", scatter_dimension=0, tiled=True
            )
            return summed.astype(jnp.float32)
    else:
        partial = lax.dot_general(
            attn_heads.reshape(length, per_dev * head_dim),
            grad_doc,
            (((0,), (0,)), ((), ())),
            preferred_element_type=jnp.float32,
        )

        def weight_grad_of(partial):
            reduced = lax.psum_scatter(partial, "dp", scatter_dimension=0, tiled=True)
            perm = []
            for d in range(n_dp):
                for s in range(n_seq):
                    perm.append((d * n_seq + s, s * n_dp + d))
            return lax.ppermute(reduced, ("dp", "seq"), perm=perm)
    partial, grad_heads = lax.optimization_barrier((partial * norm_factor, grad_heads))
    weight_grad = weight_grad_of(partial)

    results = [
        head_backward(
            head_cols(heads_qkv[0], j), head_cols(heads_qkv[1], j), head_cols(heads_qkv[2], j),
            head_cols(grad_heads, j), forward[j][0], forward[j][1], number,
        )
        for j in range(per_dev)
    ]
    arrived = [
        lax.all_to_all(jnp.stack(r), "seq", split_axis=1, concat_axis=2, tiled=True)
        for r in results
    ]
    pieces = [a.reshape(4, tokens, n_seq, head_dim) for a in arrived]
    where = {}
    for s, heads in enumerate(plan):
        for j, h in enumerate(heads):
            where[h] = (s, j)
    joined = jnp.concatenate(
        [pieces[where[h][1]][:, :, where[h][0]] for h in range(head_count)], axis=2
    )
    mixed = jnp.dot(joined[0], weight, preferred_element_type=jnp.float32).astype(jnp.bfloat16)[
        None
    ]
    back = [joined[i][None] for i in (1, 2, 3)]
    return (mixed, back[0], back[1], back[2], weight_grad)


def grid_cycle(rows, cols):
    cycle = [(r, 0) for r in range(rows)]
    for i, r in enumerate(range(rows - 1, -1, -1)):
        span = range(1, cols) if i % 2 == 0 else range(cols - 1, 0, -1)
        cycle.extend((r, c) for c in span)
    return cycle


def seq_ring(mesh):
    n_seq = mesh.shape["seq"]
    try:
        column = mesh.devices.reshape(-1, n_seq)[0]
        coords = [(d.coords[2], d.coords[0]) for d in column]
        zs = sorted({c[0] for c in coords})
        xs = sorted({c[1] for c in coords})
        where = {c: s for s, c in enumerate(coords)}
        if len(where) == n_seq and len(zs) * len(xs) == n_seq:
            if len(zs) % 2 == 0:
                cells = [(zs[r], xs[c]) for r, c in grid_cycle(len(zs), len(xs))]
            else:
                cells = [(zs[c], xs[r]) for r, c in grid_cycle(len(xs), len(zs))]
            order = [where[c] for c in cells]
            if sorted(order) == list(range(n_seq)):
                return tuple(order)
    except (AttributeError, IndexError, TypeError, KeyError):
        pass
    return tuple(range(n_seq))


def solution(mesh):
    ring = seq_ring(mesh)
    in_specs = (
        P("dp", "seq", None),
        P("dp", "seq", None),
        P("dp", "seq", None),
        P("dp", None),
        P("dp", "seq", None),
        P("dp", None, None, None),
        P("dp", None, None),
    )
    out_specs = (
        P("dp", "seq", None),
        P("dp", "seq", None),
        P("dp", "seq", None),
        P("dp", "seq", None),
        P(("dp", "seq"), None),
    )
    return jax.shard_map(
        functools.partial(per_device, ring), mesh=mesh, in_specs=in_specs, out_specs=out_specs, check_vma=False
    )
```
